32 devices in a mesh: real: 4 (over y, x), strike: 8 (over z, core).
Axes of the slice: x: 2, y: 2, z: 4, core: 2. Of those that a mesh axis runs over, the one named last changes fastest.
Arguments:
- grades: bfloat16 [4, 32, 16, 32, 128], P('real', None, 'strike'), may hold values from -6 to 6
- cotangent: bfloat16 [4, 32, 16, 32, 128], P('real', None, 'strike'), may hold values from -6 to 6
- weight: bfloat16 [32, 864], P('real'), may hold values from -0.21875 to 0.21875
- bias: bfloat16 [32], P('real'), may hold values from -3 to 3
Outputs:
- activation: bfloat16 [4, 32, 16, 32, 128], P('real', None, 'strike')
- grad_input: bfloat16 [4, 32, 16, 32, 128], P('real', None, 'strike')
- grad_weight: float32 [32, 864], P('real')
- grad_bias: float32 [32], P('real')
The draws below stay inside these ranges and needn't reach their ends.
All inputs are finite; a program needn't handle non-finite values.
Results may differ from the reference program's by a relative error of at most 0.0095.
Values may be sent and summed in bfloat16 or wider, within the bound.
No kernel may reach another device: no remote copies, remote signals or barrier semaphores. Data moves between devices by JAX's collectives and lax.ppermute only.
A program may use at most 128 MiB of HBM per device.

```python
import jax
import jax.numpy as jnp
from jax import lax

CIN = 32
COUT = 32
TAPS = 27
NY = 32
NZ = 128
NX = 16
GROUPS = 4


def block_levels(own_key, shape, pieces, least, top_value):
    factor_of, own = 1.0, jax.random.fold_in(own_key, 6)
    for dim, shards_of in pieces:
        steps = jnp.exp(jax.random.uniform(jax.random.fold_in(own, dim), (shards_of,), jnp.float32, least / len(pieces), top_value / len(pieces)))
        factor_of = factor_of * jnp.repeat(steps, shape[dim] // shards_of).reshape([-1 if axis == dim else 1 for axis in range(len(shape))])
    return factor_of


def bell_draw(own_key, extent, width, limit, pieces=(), held_as=jnp.bfloat16):
    loudness = block_levels(own_key, extent, pieces, -0.22, 0.18) if pieces else 1.0
    array = jax.random.normal(own_key, extent, jnp.float32) * width * loudness
    return jnp.minimum(jnp.maximum(array, -limit), limit).astype(held_as)


def setup_inputs(seed: int = 0) -> dict:
    key_list = jax.random.split(jax.random.key(seed), 5)
    return {
        "grades": bell_draw(key_list[0], (GROUPS, CIN, NX, NY, NZ), 1.0, 6.0, ((0, 4), (2, 8))),
        "cotangent": bell_draw(key_list[1], (GROUPS, COUT, NX, NY, NZ), 1.0, 6.0, ((0, 4), (2, 8))),
        "weight": bell_draw(key_list[2], (COUT, TAPS * CIN), (TAPS * CIN) ** -0.5, 0.21875, ((0, 4),)),
        "bias": bell_draw(key_list[3], (COUT,), 0.5, 3.0, ((0, 4),)),
    }


def conv_field(field, kernel):
    return lax.conv_general_dilated(field[None], kernel, (1, 1, 1), 'SAME', dimension_numbers=('NCDHW', 'OIDHW', 'NCDHW'), precision=lax.Precision.HIGHEST)[0]

def reference(grades, cotangent, weight, bias):
    kernel = weight.astype(jnp.float32).reshape(COUT, 3, 3, 3, CIN).transpose(0, 4, 1, 2, 3)
    bias_vec = bias.astype(jnp.float32)

    def one_group(pair):
        field, cot = pair
        field32 = field.astype(jnp.float32)
        pre = conv_field(field32, kernel) + bias_vec[:, None, None, None]
        sig = jax.nn.sigmoid(pre)
        activation = (pre * sig).astype(jnp.bfloat16)
        dpre = (cot.astype(jnp.float32) * sig * (1.0 + pre * (1.0 - sig))).astype(jnp.bfloat16)
        _, pull = jax.vjp(conv_field, field32, kernel)
        grad_field, grad_kernel = pull(dpre.astype(jnp.float32))
        grad_b = lax.optimization_barrier(jnp.sum(dpre.astype(jnp.float32), axis=(1, 2, 3)))
        return (activation, grad_field.astype(jnp.bfloat16), grad_kernel, grad_b)
    activation, grad_input, kernels, biases = lax.map(one_group, (grades, cotangent))
    factor = 1.0 / (GROUPS * NX * NY * NZ) ** 0.5
    grad_kernel = lax.optimization_barrier(jnp.sum(kernels, axis=0)).transpose(0, 2, 3, 4, 1).reshape(COUT, TAPS * CIN)
    grad_weight = grad_kernel * factor
    grad_bias = lax.optimization_barrier(jnp.sum(biases, axis=0)) * factor
    return (activation, grad_input, grad_weight, grad_bias)
```

```python
import jax
import jax.numpy as jnp
from jax import lax
from jax.sharding import PartitionSpec as P


def padded(value, sides, width):
    for axis, dim in sides:
        peers, length = (lax.axis_size(axis), value.shape[dim])
        up = [(i, (i + 1) % peers) for i in range(peers - 1)]
        down = [(j, i) for i, j in up]
        last = lax.slice_in_dim(value, length - width, length, axis=dim)
        leading = lax.slice_in_dim(value, 0, width, axis=dim)
        before = lax.ppermute(last, axis, up)
        after = lax.ppermute(leading, axis, down)
        value = jnp.concatenate([before, value, after], axis=dim)
    return value


def swap(value, axis, bit):
    peers = lax.axis_size(axis)
    return lax.ppermute(value, axis, [(i, i ^ bit) for i in range(peers)])


def gather_rows(value, axis):
    peers = lax.axis_size(axis)
    me = lax.axis_index(axis)
    blocks = jnp.zeros((peers,) + value.shape, value.dtype)
    blocks = lax.dynamic_update_index_in_dim(blocks, value, me, 0)
    for k in range(1, peers):
        blocks = lax.dynamic_update_index_in_dim(blocks, swap(value, axis, k), me ^ k, 0)
    return blocks.reshape((peers * value.shape[0],) + value.shape[1:])


def scatter_rows(value, axis):
    peers = lax.axis_size(axis)
    me = lax.axis_index(axis)
    bit = peers // 2
    while bit >= 1:
        half = value.shape[0] // 2
        upper = (me // bit) % 2
        keep = lax.dynamic_slice_in_dim(value, upper * half, half, 0)
        send = lax.dynamic_slice_in_dim(value, (1 - upper) * half, half, 0)
        value = keep + swap(send, axis, bit)
        bit //= 2
    return value


def sum_over(value, axis):
    peers = lax.axis_size(axis)
    bit = 1
    while bit < peers:
        value = value + swap(value, axis, bit)
        bit *= 2
    return value


def tap_list():
    listing = []
    for shift_x in (-1, 0, 1):
        for shift_y in (-1, 0, 1):
            for shift_z in (-1, 0, 1):
                listing.append(
                    (
                        shift_x,
                        shift_y,
                        shift_z,
                        9 * (shift_x + 1) + 3 * (shift_y + 1) + (shift_z + 1),
                    )
                )
    return listing


def transposed_stencil(padded_grad, kernel3, planes, rows, depth):
    total = jnp.zeros((kernel3.shape[2], planes, rows, depth), jnp.float32)
    for shift_x, shift_y, shift_z, column in tap_list():
        window = padded_grad[
            :,
            1 - shift_x : 1 - shift_x + planes,
            1 - shift_y : 1 - shift_y + rows,
            1 - shift_z : 1 - shift_z + depth,
        ]
        total = total + jnp.einsum(
            "oi,oxyz->ixyz", kernel3[:, column, :], window, preferred_element_type=jnp.float32
        )
    return total


def local(grades, cotangent, weight, bias):
    field = grades[0]
    cot = cotangent[0]
    in_chan, planes, rows, depth = field.shape
    taps_in = weight.shape[1]
    packed = jnp.concatenate([weight, bias[:, None]], axis=1)
    whole = gather_rows(packed, "real")
    whole_weight, whole_bias = whole[:, :taps_in], whole[:, taps_in]
    out_chan = whole_weight.shape[0]
    kernel3 = whole_weight.reshape(out_chan, 27, in_chan)
    haloed = padded(field, (("strike", 1),), 1)
    padded_in = jnp.pad(haloed, ((0, 0), (0, 0), (1, 1), (1, 1)))
    total = jnp.zeros((out_chan, planes, rows, depth), jnp.float32)
    for shift_x, shift_y, shift_z, column in tap_list():
        window = padded_in[
            :,
            1 + shift_x : 1 + shift_x + planes,
            1 + shift_y : 1 + shift_y + rows,
            1 + shift_z : 1 + shift_z + depth,
        ]
        total = total + jnp.einsum(
            "oi,ixyz->oxyz", kernel3[:, column, :], window, preferred_element_type=jnp.float32
        )
    pre = total + whole_bias.astype(jnp.float32)[:, None, None, None]
    sig = jax.nn.sigmoid(pre)
    activation = (pre * sig).astype(jnp.bfloat16)
    dpre = (cot.astype(jnp.float32) * sig * (1.0 + pre * (1.0 - sig))).astype(jnp.bfloat16)
    columns = []
    for shift_x, shift_y, shift_z, column in tap_list():
        window = padded_in[
            :,
            1 + shift_x : 1 + shift_x + planes,
            1 + shift_y : 1 + shift_y + rows,
            1 + shift_z : 1 + shift_z + depth,
        ]
        columns.append(
            jnp.einsum("oxyz,ixyz->oi", dpre, window, preferred_element_type=jnp.float32)
        )
    local_weight = jnp.stack(columns, axis=1).reshape(out_chan, 27 * in_chan)
    local_bias = jnp.sum(dpre.astype(jnp.float32), axis=(1, 2, 3))
    local_grads = jnp.concatenate([local_weight, local_bias[:, None]], axis=1)
    owned = sum_over(scatter_rows(local_grads, "real"), "strike")
    grad_haloed = padded(dpre, (("strike", 1),), 1)
    padded_grad = jnp.pad(grad_haloed, ((0, 0), (0, 0), (1, 1), (1, 1)))
    grad_field = transposed_stencil(padded_grad, kernel3, planes, rows, depth)
    grad_input = grad_field.astype(jnp.bfloat16)
    cells = lax.axis_size("real") * lax.axis_size("strike") * planes * rows * depth
    factor = 1.0 / cells**0.5
    owned = owned * factor
    return (activation[None], grad_input[None], owned[:, :taps_in], owned[:, taps_in])


def solution(mesh):
    in_specs = (
        P("real", None, "strike", None, None),
        P("real", None, "strike", None, None),
        P("real", None),
        P("real"),
    )
    out_specs = (
        P("real", None, "strike", None, None),
        P("real", None, "strike", None, None),
        P("real", None),
        P("real"),
    )
    return jax.shard_map(local, mesh=mesh, in_specs=in_specs, out_specs=out_specs, check_vma=False)
```

```python
import jax
import jax.numpy as jnp
from jax import lax
from jax.sharding import PartitionSpec as P


def padded(value, sides, width):
    for axis, dim in sides:
        peers, length = (lax.axis_size(axis), value.shape[dim])
        up = [(i, (i + 1) % peers) for i in range(peers - 1)]
        down = [(j, i) for i, j in up]
        last = lax.slice_in_dim(value, length - width, length, axis=dim)
        leading = lax.slice_in_dim(value, 0, width, axis=dim)
        before = lax.ppermute(last, axis, up)
        after = lax.ppermute(leading, axis, down)
        value = jnp.concatenate([before, value, after], axis=dim)
    return value


def swap(value, axis, bit):
    peers = lax.axis_size(axis)
    return lax.ppermute(value, axis, [(i, i ^ bit) for i in range(peers)])


def gather_rows(value, axis):
    peers = lax.axis_size(axis)
    me = lax.axis_index(axis)
    blocks = jnp.zeros((peers,) + value.shape, value.dtype)
    blocks = lax.dynamic_update_index_in_dim(blocks, value, me, 0)
    for k in range(1, peers):
        blocks = lax.dynamic_update_index_in_dim(blocks, swap(value, axis, k), me ^ k, 0)
    return blocks.reshape((peers * value.shape[0],) + value.shape[1:])


def tap_list():
    listing = []
    for shift_x in (-1, 0, 1):
        for shift_y in (-1, 0, 1):
            for shift_z in (-1, 0, 1):
                listing.append(
                    (
                        shift_x,
                        shift_y,
                        shift_z,
                        9 * (shift_x + 1) + 3 * (shift_y + 1) + (shift_z + 1),
                    )
                )
    return listing


def transposed_taps(total, padded_grad, kernel3, taps, planes, rows, depth):
    for shift_x, shift_y, shift_z, column in taps:
        window = padded_grad[
            :,
            1 - shift_x : 1 - shift_x + planes,
            1 - shift_y : 1 - shift_y + rows,
            1 - shift_z : 1 - shift_z + depth,
        ]
        total = total + jnp.einsum(
            "oi,oxyz->ixyz", kernel3[:, column, :], window, preferred_element_type=jnp.float32
        )
    return total


def reduce_beside(local_grads, padded_grad, kernel3, planes, rows, depth):
    rounds = []
    bit = lax.axis_size("real") // 2
    while bit >= 1:
        rounds.append(("real", bit))
        bit //= 2
    bit = 1
    while bit < lax.axis_size("strike"):
        rounds.append(("strike", bit))
        bit *= 2
    taps = tap_list()
    bounds = [len(taps) * k // len(rounds) for k in range(len(rounds) + 1)]
    total = jnp.zeros((kernel3.shape[2], planes, rows, depth), jnp.float32)
    value = local_grads
    for k, (axis, bit) in enumerate(rounds):
        if axis == "real":
            half = value.shape[0] // 2
            upper = (lax.axis_index(axis) // bit) % 2
            keep = lax.dynamic_slice_in_dim(value, upper * half, half, 0)
            send = lax.dynamic_slice_in_dim(value, (1 - upper) * half, half, 0)
        else:
            keep, send = value, value
        send, total = lax.optimization_barrier((send, total))
        received = swap(send, axis, bit)
        chunk = taps[bounds[k] : bounds[k + 1]]
        total = lax.cond(
            lax.axis_index("strike") < lax.axis_size("strike"),
            lambda t, c=chunk: transposed_taps(t, padded_grad, kernel3, c, planes, rows, depth),
            lambda t: t,
            total,
        )
        received, total = lax.optimization_barrier((received, total))
        value = keep + received
    return value, total


def local(grades, cotangent, weight, bias):
    field = grades[0]
    cot = cotangent[0]
    in_chan, planes, rows, depth = field.shape
    taps_in = weight.shape[1]
    packed = jnp.concatenate([weight, bias[:, None]], axis=1)
    whole = gather_rows(packed, "real")
    whole_weight, whole_bias = whole[:, :taps_in], whole[:, taps_in]
    out_chan = whole_weight.shape[0]
    kernel3 = whole_weight.reshape(out_chan, 27, in_chan)
    haloed = padded(field, (("strike", 1),), 1)
    padded_in = jnp.pad(haloed, ((0, 0), (0, 0), (1, 1), (1, 1)))
    total = jnp.zeros((out_chan, planes, rows, depth), jnp.float32)
    for shift_x, shift_y, shift_z, column in tap_list():
        window = padded_in[
            :,
            1 + shift_x : 1 + shift_x + planes,
            1 + shift_y : 1 + shift_y + rows,
            1 + shift_z : 1 + shift_z + depth,
        ]
        total = total + jnp.einsum(
            "oi,ixyz->oxyz", kernel3[:, column, :], window, preferred_element_type=jnp.float32
        )
    pre = total + whole_bias.astype(jnp.float32)[:, None, None, None]
    sig = jax.nn.sigmoid(pre)
    activation = (pre * sig).astype(jnp.bfloat16)
    dpre = (cot.astype(jnp.float32) * sig * (1.0 + pre * (1.0 - sig))).astype(jnp.bfloat16)
    grad_haloed = padded(dpre, (("strike", 1),), 1)
    def weight_terms(operands):
        values, grads = operands
        columns = []
        for shift_x, shift_y, shift_z, column in tap_list():
            window = values[
                :,
                1 + shift_x : 1 + shift_x + planes,
                1 + shift_y : 1 + shift_y + rows,
                1 + shift_z : 1 + shift_z + depth,
            ]
            columns.append(
                jnp.einsum("oxyz,ixyz->oi", grads, window, preferred_element_type=jnp.float32)
            )
        return jnp.stack(columns, axis=1).reshape(out_chan, 27 * in_chan)

    local_weight = lax.cond(
        lax.axis_index("strike") < lax.axis_size("strike"),
        weight_terms,
        lambda operands: jnp.zeros((out_chan, 27 * in_chan), jnp.float32),
        (padded_in, dpre),
    )
    local_bias = jnp.sum(dpre.astype(jnp.float32), axis=(1, 2, 3))
    local_grads = jnp.concatenate([local_weight, local_bias[:, None]], axis=1)
    grad_haloed, local_grads = lax.optimization_barrier((grad_haloed, local_grads))
    padded_grad = jnp.pad(grad_haloed, ((0, 0), (0, 0), (1, 1), (1, 1)))
    owned, grad_field = reduce_beside(local_grads, padded_grad, kernel3, planes, rows, depth)
    grad_input = grad_field.astype(jnp.bfloat16)
    cells = lax.axis_size("real") * lax.axis_size("strike") * planes * rows * depth
    factor = 1.0 / cells**0.5
    owned = owned * factor
    return (activation[None], grad_input[None], owned[:, :taps_in], owned[:, taps_in])


def solution(mesh):
    in_specs = (
        P("real", None, "strike", None, None),
        P("real", None, "strike", None, None),
        P("real", None),
        P("real"),
    )
    out_specs = (
        P("real", None, "strike", None, None),
        P("real", None, "strike", None, None),
        P("real", None),
        P("real"),
    )
    return jax.shard_map(local, mesh=mesh, in_specs=in_specs, out_specs=out_specs, check_vma=False)
```

```python
import functools

import jax
import jax.numpy as jnp
from jax import lax
from jax.experimental import pallas as pl
from jax.experimental.pallas import tpu as pltpu
from jax.sharding import PartitionSpec as P

OFFSETS = [(b, c) for b in (-1, 0, 1) for c in (-1, 0, 1)]


def plane_masks(rows, depth):
    y = jnp.arange(rows)[:, None]
    z = jnp.arange(depth)[None, :]
    masks = [((y + b >= 0) & (y + b < rows) & (z + c >= 0) & (z + c < depth)) for b, c in OFFSETS]
    return jnp.stack(masks).reshape(len(OFFSETS), 1, rows * depth).astype(jnp.float32)


def _stacked(lo, mid, hi, h, planes):
    def plane(index):
        if index == 0:
            return lo[0]
        if index == planes + 1:
            return hi[0]
        return mid[index - 1]
    return jnp.concatenate([plane(h), plane(h + 1), plane(h + 2)], axis=0)


def _shifted_sum(y, mask, chans, lanes, depth, sign):
    total = None
    for k, (b, c) in enumerate(OFFSETS):
        off = sign * (b * depth + c)
        block = y[k * chans : (k + 1) * chans]
        if off != 0:
            block = pltpu.roll(block, (-off) % lanes, 1)
            block = jnp.where(mask[k if sign > 0 else len(OFFSETS) - 1 - k] > 0.5, block, 0.0)
        total = block if total is None else total + block
    return total


def _forward_kernel(lo, mid, hi, wall, bias, cot, mask, act_out, dpre_out, *, planes, depth):
    chans, lanes = mid.shape[1], mid.shape[2]
    for p in range(planes):
        y = jnp.dot(wall[...], _stacked(lo, mid, hi, p, planes), preferred_element_type=jnp.float32)
        pre = _shifted_sum(y, mask, chans, lanes, depth, 1) + bias[...]
        sig = 1.0 / (1.0 + jnp.exp(-pre))
        act_out[p] = (pre * sig).astype(act_out.dtype)
        dpre_out[p] = (cot[p].astype(jnp.float32) * sig * (1.0 + pre * (1.0 - sig))).astype(dpre_out.dtype)


def _input_kernel(lo, mid, hi, wall, mask, out, *, planes, first, depth):
    chans, lanes = mid.shape[1], mid.shape[2]
    for n in range(out.shape[0]):
        y = jnp.dot(wall[...], _stacked(lo, mid, hi, first + n, planes), preferred_element_type=jnp.float32)
        out[n] = _shifted_sum(y, mask, chans, lanes, depth, -1).astype(out.dtype)


def _weight_kernel(lo, mid, hi, dpre, mask, gw_out, gb_out, *, planes, depth):
    chans, lanes = dpre.shape[1], dpre.shape[2]
    gw = jnp.zeros(gw_out.shape, jnp.float32)
    gb = jnp.zeros(gb_out.shape, jnp.float32)
    for p in range(planes):
        d = dpre[p].astype(jnp.float32)
        gb = gb + jnp.sum(d, axis=1, keepdims=True)
        parts = []
        for k, (b, c) in enumerate(OFFSETS):
            off = b * depth + c
            e = d
            if off != 0:
                e = pltpu.roll(jnp.where(mask[k] > 0.5, d, 0.0), off % lanes, 1)
            parts.append(e.astype(jnp.bfloat16))
        gw = gw + lax.dot_general(
            jnp.concatenate(parts, axis=0), _stacked(lo, mid, hi, p, planes),
            (((1,), (1,)), ((), ())), preferred_element_type=jnp.float32,
        )
    gw_out[...] = gw
    gb_out[...] = gb


def _vmem(n):
    return [pl.BlockSpec(memory_space=pltpu.VMEM)] * n


def forward_call(lo, mid, hi, wall, bias, cot, mask, depth):
    planes, chans, lanes = mid.shape
    shape = jax.ShapeDtypeStruct(mid.shape, jnp.bfloat16)
    flops = 2 * planes * wall.shape[0] * wall.shape[1] * lanes
    return pl.pallas_call(
        functools.partial(_forward_kernel, planes=planes, depth=depth),
        out_shape=(shape, shape),
        in_specs=_vmem(7),
        out_specs=tuple(_vmem(2)),
        cost_estimate=pl.CostEstimate(flops=flops, transcendentals=planes * chans * lanes, bytes_accessed=5 * mid.size * 2),
    )(lo, mid, hi, wall, bias, cot, mask)


def input_call(lo, mid, hi, wall, mask, depth, first, count):
    planes, chans, lanes = mid.shape
    flops = 2 * count * wall.shape[0] * wall.shape[1] * lanes
    return pl.pallas_call(
        functools.partial(_input_kernel, planes=planes, first=first, depth=depth),
        out_shape=jax.ShapeDtypeStruct((count, chans, lanes), jnp.bfloat16),
        in_specs=_vmem(5),
        out_specs=_vmem(1)[0],
        cost_estimate=pl.CostEstimate(flops=flops, transcendentals=0, bytes_accessed=3 * mid.size * 2),
    )(lo, mid, hi, wall, mask)


def weight_call(lo, mid, hi, dpre, mask, depth):
    planes, chans, lanes = mid.shape
    flops = 2 * planes * 9 * chans * 3 * chans * lanes
    return pl.pallas_call(
        functools.partial(_weight_kernel, planes=planes, depth=depth),
        out_shape=(jax.ShapeDtypeStruct((9 * chans, 3 * chans), jnp.float32), jax.ShapeDtypeStruct((chans, 1), jnp.float32)),
        in_specs=_vmem(5),
        out_specs=tuple(_vmem(2)),
        cost_estimate=pl.CostEstimate(flops=flops, transcendentals=0, bytes_accessed=3 * mid.size * 2),
    )(lo, mid, hi, dpre, mask)


def neighbours(first, last, axis):
    peers = lax.axis_size(axis)
    up = [(i, i + 1) for i in range(peers - 1)]
    down = [(j, i) for i, j in up]
    return lax.ppermute(last, axis, up), lax.ppermute(first, axis, down)


def swap(value, axis, bit):
    peers = lax.axis_size(axis)
    return lax.ppermute(value, axis, [(i, i ^ bit) for i in range(peers)])


def gather_rows(value, axis):
    peers = lax.axis_size(axis)
    me = lax.axis_index(axis)
    blocks = jnp.zeros((peers,) + value.shape, value.dtype)
    blocks = lax.dynamic_update_index_in_dim(blocks, value, me, 0)
    for k in range(1, peers):
        blocks = lax.dynamic_update_index_in_dim(blocks, swap(value, axis, k), me ^ k, 0)
    return blocks.reshape((peers * value.shape[0],) + value.shape[1:])


def reduce_beside(local_grads, work):
    rounds = []
    bit = lax.axis_size("real") // 2
    while bit >= 1:
        rounds.append(("real", bit))
        bit //= 2
    bit = 1
    while bit < lax.axis_size("strike"):
        rounds.append(("strike", bit))
        bit *= 2
    results = []
    value = local_grads
    for k, (axis, bit) in enumerate(rounds):
        if axis == "real":
            half = value.shape[0] // 2
            upper = (lax.axis_index(axis) // bit) % 2
            keep = lax.dynamic_slice_in_dim(value, upper * half, half, 0)
            send = lax.dynamic_slice_in_dim(value, (1 - upper) * half, half, 0)
        else:
            keep, send = value, value
        if k < len(work):
            send, inputs = lax.optimization_barrier((send, work[k][1]))
            received = swap(send, axis, bit)
            result = work[k][0](*inputs)
            received, result = lax.optimization_barrier((received, result))
            results.append(result)
        else:
            received = swap(send, axis, bit)
        value = keep + received
    for job, inputs in work[len(rounds) :]:
        results.append(job(*inputs))
    return value, results


def local(grades, cotangent, weight, bias):
    field = grades[0]
    chans, planes, rows, depth = field.shape
    lanes = rows * depth
    taps_in = weight.shape[1]
    packed = jnp.concatenate([weight, bias[:, None]], axis=1)
    whole = gather_rows(packed, "real")
    whole_weight, whole_bias = whole[:, :taps_in], whole[:, taps_in]
    out_chan = whole_weight.shape[0]
    w5 = whole_weight.reshape(out_chan, 3, 3, 3, chans)
    forward_w = w5.transpose(2, 3, 0, 1, 4).reshape(9 * out_chan, 3 * chans)
    backward_w = w5[:, ::-1].transpose(2, 3, 4, 1, 0).reshape(9 * chans, 3 * out_chan)
    mask = plane_masks(rows, depth)

    def flat(value):
        return value.transpose(1, 0, 2, 3).reshape(planes, value.shape[0], lanes)

    def unflat(value):
        return value.reshape(planes, value.shape[1], rows, depth).transpose(1, 0, 2, 3)

    mid = flat(field)
    lo, hi = neighbours(mid[:1], mid[planes - 1 :], "strike")
    act, dpre = forward_call(
        lo, mid, hi, forward_w, whole_bias.astype(jnp.float32)[:, None], flat(cotangent[0]), mask, depth
    )
    dlo, dhi = neighbours(dpre[:1], dpre[planes - 1 :], "strike")
    g, gb = weight_call(lo, mid, hi, dpre, mask, depth)
    local_weight = g.reshape(3, 3, out_chan, 3, chans).transpose(2, 3, 0, 1, 4).reshape(out_chan, 27 * chans)
    local_grads = jnp.concatenate([local_weight, gb], axis=1)
    work = [
        (functools.partial(input_call, depth=depth, first=p, count=1), (dlo, dpre, dhi, backward_w, mask))
        for p in range(planes)
    ]
    owned, pieces = reduce_beside(local_grads, work)
    grad_input = unflat(jnp.concatenate(pieces, axis=0))
    cells = lax.axis_size("real") * lax.axis_size("strike") * planes * rows * depth
    factor = 1.0 / cells**0.5
    owned = owned * factor
    return (unflat(act)[None], grad_input[None], owned[:, :taps_in], owned[:, taps_in])


def solution(mesh):
    in_specs = (
        P("real", None, "strike", None, None),
        P("real", None, "strike", None, None),
        P("real", None),
        P("real"),
    )
    out_specs = (
        P("real", None, "strike", None, None),
        P("real", None, "strike", None, None),
        P("real", None),
        P("real"),
    )
    return jax.shard_map(local, mesh=mesh, in_specs=in_specs, out_specs=out_specs, check_vma=False)
```

```python
import functools

import jax
import jax.numpy as jnp
import numpy as np
from jax import lax
from jax.experimental import pallas as pl
from jax.experimental.pallas import tpu as pltpu
from jax.sharding import PartitionSpec as P

OFFSETS = [(b, c) for b in (-1, 0, 1) for c in (-1, 0, 1)]


def plane_masks(rows, depth):
    y = np.arange(rows)[:, None]
    z = np.arange(depth)[None, :]
    masks = [((y + b >= 0) & (y + b < rows) & (z + c >= 0) & (z + c < depth)) for b, c in OFFSETS]
    return np.stack(masks).reshape(len(OFFSETS), 1, rows * depth).astype(np.float32)


def _stacked(lo, mid, hi, h, planes):
    def plane(index):
        if index == 0:
            return lo[0]
        if index == planes + 1:
            return hi[0]
        return mid[index - 1]
    return jnp.concatenate([plane(h), plane(h + 1), plane(h + 2)], axis=0)


def _shifted_sum(y, mask, chans, lanes, depth, sign):
    total = None
    for k, (b, c) in enumerate(OFFSETS):
        off = sign * (b * depth + c)
        block = y[k * chans : (k + 1) * chans]
        if off != 0:
            block = pltpu.roll(block, (-off) % lanes, 1)
            block = jnp.where(mask[k if sign > 0 else len(OFFSETS) - 1 - k] > 0.5, block, 0.0)
        total = block if total is None else total + block
    return total


def _weight_terms(lo, mid, hi, d, mask, p, planes, depth):
    lanes = d.shape[1]
    parts = []
    for k, (b, c) in enumerate(OFFSETS):
        off = b * depth + c
        e = d
        if off != 0:
            e = pltpu.roll(jnp.where(mask[k] > 0.5, d, 0.0), off % lanes, 1)
        parts.append(e.astype(jnp.bfloat16))
    return lax.dot_general(
        jnp.concatenate(parts, axis=0), _stacked(lo, mid, hi, p, planes),
        (((1,), (1,)), ((), ())), preferred_element_type=jnp.float32,
    )


def _forward_kernel(lo, mid, hi, wall, bias, cot, mask, act_out, dpre_out, gw_out, gb_out, *, planes, depth):
    chans, lanes = mid.shape[1], mid.shape[2]
    gw = jnp.zeros(gw_out.shape, jnp.float32)
    gb = jnp.zeros(gb_out.shape, jnp.float32)
    for p in range(planes):
        y = jnp.dot(wall[...], _stacked(lo, mid, hi, p, planes), preferred_element_type=jnp.float32)
        pre = _shifted_sum(y, mask, chans, lanes, depth, 1) + bias[...]
        sig = 1.0 / (1.0 + jnp.exp(-pre))
        act_out[p] = (pre * sig).astype(act_out.dtype)
        dpre = (cot[p].astype(jnp.float32) * sig * (1.0 + pre * (1.0 - sig))).astype(dpre_out.dtype)
        dpre_out[p] = dpre
        d = dpre.astype(jnp.float32)
        gb = gb + jnp.sum(d, axis=1, keepdims=True)
        gw = gw + _weight_terms(lo, mid, hi, d, mask, p, planes, depth)
    gw_out[...] = gw
    gb_out[...] = gb


def _input_kernel(lo, mid, hi, wall, mask, out, *, planes, first, depth):
    chans, lanes = mid.shape[1], mid.shape[2]
    for n in range(out.shape[0]):
        y = jnp.dot(wall[...], _stacked(lo, mid, hi, first + n, planes), preferred_element_type=jnp.float32)
        out[n] = _shifted_sum(y, mask, chans, lanes, depth, -1).astype(out.dtype)


def _vmem(n):
    return [pl.BlockSpec(memory_space=pltpu.VMEM)] * n


def forward_call(lo, mid, hi, wall, bias, cot, mask, depth):
    planes, chans, lanes = mid.shape
    shape = jax.ShapeDtypeStruct(mid.shape, jnp.bfloat16)
    flops = 4 * planes * wall.shape[0] * wall.shape[1] * lanes
    return pl.pallas_call(
        functools.partial(_forward_kernel, planes=planes, depth=depth),
        out_shape=(
            shape,
            shape,
            jax.ShapeDtypeStruct(wall.shape, jnp.float32),
            jax.ShapeDtypeStruct((chans, 1), jnp.float32),
        ),
        in_specs=_vmem(7),
        out_specs=tuple(_vmem(4)),
        cost_estimate=pl.CostEstimate(flops=flops, transcendentals=planes * chans * lanes, bytes_accessed=5 * mid.size * 2),
    )(lo, mid, hi, wall, bias, cot, mask)


def input_call(lo, mid, hi, wall, mask, depth, first, count):
    planes, chans, lanes = mid.shape
    flops = 2 * count * wall.shape[0] * wall.shape[1] * lanes
    return pl.pallas_call(
        functools.partial(_input_kernel, planes=planes, first=first, depth=depth),
        out_shape=jax.ShapeDtypeStruct((count, chans, lanes), jnp.bfloat16),
        in_specs=_vmem(5),
        out_specs=_vmem(1)[0],
        cost_estimate=pl.CostEstimate(flops=flops, transcendentals=0, bytes_accessed=3 * mid.size * 2),
    )(lo, mid, hi, wall, mask)


def neighbours(first, last, axis):
    peers = lax.axis_size(axis)
    up = [(i, i + 1) for i in range(peers - 1)]
    down = [(j, i) for i, j in up]
    return lax.ppermute(last, axis, up), lax.ppermute(first, axis, down)


def swap(value, axis, bit):
    peers = lax.axis_size(axis)
    return lax.ppermute(value, axis, [(i, i ^ bit) for i in range(peers)])


def gather_rows(value, axis):
    peers = lax.axis_size(axis)
    me = lax.axis_index(axis)
    blocks = jnp.zeros((peers,) + value.shape, value.dtype)
    blocks = lax.dynamic_update_index_in_dim(blocks, value, me, 0)
    for k in range(1, peers):
        blocks = lax.dynamic_update_index_in_dim(blocks, swap(value, axis, k), me ^ k, 0)
    return blocks.reshape((peers * value.shape[0],) + value.shape[1:])


def reduce_beside(local_grads, work):
    rounds = []
    bit = lax.axis_size("real") // 2
    while bit >= 1:
        rounds.append(("real", bit))
        bit //= 2
    bit = 1
    while bit < lax.axis_size("strike"):
        rounds.append(("strike", bit))
        bit *= 2
    results = []
    value = local_grads
    for k, (axis, bit) in enumerate(rounds):
        if axis == "real":
            half = value.shape[0] // 2
            upper = (lax.axis_index(axis) // bit) % 2
            keep = lax.dynamic_slice_in_dim(value, upper * half, half, 0)
            send = lax.dynamic_slice_in_dim(value, (1 - upper) * half, half, 0)
        else:
            keep, send = value, value
        if k < len(work):
            send, inputs = lax.optimization_barrier((send, work[k][1]))
            received = swap(send, axis, bit)
            result = work[k][0](*inputs)
            received, result = lax.optimization_barrier((received, result))
            results.append(result)
        else:
            received = swap(send, axis, bit)
        value = keep + received
    for job, inputs in work[len(rounds) :]:
        results.append(job(*inputs))
    return value, results


def local(grades, cotangent, weight, bias):
    field = grades[0]
    chans, planes, rows, depth = field.shape
    lanes = rows * depth
    taps_in = weight.shape[1]
    packed = jnp.concatenate([weight, bias[:, None]], axis=1)
    whole = gather_rows(packed, "real")
    whole_weight, whole_bias = whole[:, :taps_in], whole[:, taps_in]
    out_chan = whole_weight.shape[0]
    w5 = whole_weight.reshape(out_chan, 3, 3, 3, chans)
    forward_w = w5.transpose(2, 3, 0, 1, 4).reshape(9 * out_chan, 3 * chans)
    backward_w = w5[:, ::-1].transpose(2, 3, 4, 1, 0).reshape(9 * chans, 3 * out_chan)
    mask = jnp.asarray(plane_masks(rows, depth))

    def flat(value):
        return value.transpose(1, 0, 2, 3).reshape(planes, value.shape[0], lanes)

    def unflat(value):
        return value.reshape(planes, value.shape[1], rows, depth).transpose(1, 0, 2, 3)

    mid = flat(field)
    lo, hi = neighbours(mid[:1], mid[planes - 1 :], "strike")
    act, dpre, g, gb = forward_call(
        lo, mid, hi, forward_w, whole_bias.astype(jnp.float32)[:, None], flat(cotangent[0]), mask, depth
    )
    dlo, dhi = neighbours(dpre[:1], dpre[planes - 1 :], "strike")
    local_weight = g.reshape(3, 3, out_chan, 3, chans).transpose(2, 3, 0, 1, 4).reshape(out_chan, 27 * chans)
    local_grads = jnp.concatenate([local_weight, gb], axis=1)
    work = [(unflat, (act,))] + [
        (functools.partial(input_call, depth=depth, first=p, count=1), (dlo, dpre, dhi, backward_w, mask))
        for p in range(planes)
    ]
    owned, pieces = reduce_beside(local_grads, work)
    activation = pieces[0]
    grad_input = unflat(jnp.concatenate(pieces[1:], axis=0))
    cells = lax.axis_size("real") * lax.axis_size("strike") * planes * rows * depth
    factor = 1.0 / cells**0.5
    owned = owned * factor
    return (activation[None], grad_input[None], owned[:, :taps_in], owned[:, taps_in])


def solution(mesh):
    in_specs = (
        P("real", None, "strike", None, None),
        P("real", None, "strike", None, None),
        P("real", None),
        P("real"),
    )
    out_specs = (
        P("real", None, "strike", None, None),
        P("real", None, "strike", None, None),
        P("real", None),
        P("real"),
    )
    return jax.shard_map(local, mesh=mesh, in_specs=in_specs, out_specs=out_specs, check_vma=False)
```

```python
import functools

import jax
import jax.numpy as jnp
import numpy as np
from jax import lax
from jax.experimental import pallas as pl
from jax.experimental.pallas import tpu as pltpu
from jax.sharding import PartitionSpec as P

OFFSETS = [(b, c) for b in (-1, 0, 1) for c in (-1, 0, 1)]


def plane_masks(rows, depth):
    y = np.arange(rows)[:, None]
    z = np.arange(depth)[None, :]
    masks = [((y + b >= 0) & (y + b < rows) & (z + c >= 0) & (z + c < depth)) for b, c in OFFSETS]
    return np.stack(masks).reshape(len(OFFSETS), 1, rows * depth).astype(np.float32)


def _stacked(lo, mid, hi, h, planes):
    def plane(index):
        if index == 0:
            return lo[0]
        if index == planes + 1:
            return hi[0]
        return mid[index - 1]
    return jnp.concatenate([plane(h), plane(h + 1), plane(h + 2)], axis=0)


def _shifted_sum(y, mask, chans, lanes, depth, sign):
    total = None
    for k, (b, c) in enumerate(OFFSETS):
        off = sign * (b * depth + c)
        block = y[k * chans : (k + 1) * chans]
        if off != 0:
            block = pltpu.roll(block, (-off) % lanes, 1)
            block = jnp.where(mask[k if sign > 0 else len(OFFSETS) - 1 - k] > 0.5, block, 0.0)
        total = block if total is None else total + block
    return total


def _weight_terms(lo, mid, hi, d, mask, p, planes, depth):
    lanes = d.shape[1]
    parts = []
    for k, (b, c) in enumerate(OFFSETS):
        off = b * depth + c
        e = d
        if off != 0:
            e = pltpu.roll(jnp.where(mask[k] > 0.5, d, 0.0), off % lanes, 1)
        parts.append(e.astype(jnp.bfloat16))
    return lax.dot_general(
        jnp.concatenate(parts, axis=0), _stacked(lo, mid, hi, p, planes),
        (((1,), (1,)), ((), ())), preferred_element_type=jnp.float32,
    )


def _forward_kernel(lo, mid, hi, wall, bias, cot, mask, act_out, dpre_out, gw_out, gb_out, *, planes, depth):
    chans, lanes = mid.shape[1], mid.shape[2]
    gw = jnp.zeros(gw_out.shape, jnp.float32)
    gb = jnp.zeros(gb_out.shape, jnp.float32)
    for p in range(planes):
        y = jnp.dot(wall[...], _stacked(lo, mid, hi, p, planes), preferred_element_type=jnp.float32)
        pre = _shifted_sum(y, mask, chans, lanes, depth, 1) + bias[...]
        sig = 1.0 / (1.0 + jnp.exp(-pre))
        act_out[p] = (pre * sig).astype(act_out.dtype)
        dpre = (cot[p].astype(jnp.float32) * sig * (1.0 + pre * (1.0 - sig))).astype(dpre_out.dtype)
        dpre_out[p] = dpre
        d = dpre.astype(jnp.float32)
        gb = gb + jnp.sum(d, axis=1, keepdims=True)
        gw = gw + _weight_terms(lo, mid, hi, d, mask, p, planes, depth)
    gw_out[...] = gw
    gb_out[...] = gb


def _input_kernel(lo, mid, hi, wall, mask, out, *, planes, first, depth):
    chans, lanes = mid.shape[1], mid.shape[2]
    for n in range(out.shape[0]):
        y = jnp.dot(wall[...], _stacked(lo, mid, hi, first + n, planes), preferred_element_type=jnp.float32)
        out[n] = _shifted_sum(y, mask, chans, lanes, depth, -1).astype(out.dtype)


def _vmem(n):
    return [pl.BlockSpec(memory_space=pltpu.VMEM)] * n


def forward_call(lo, mid, hi, wall, bias, cot, mask, depth):
    planes, chans, lanes = mid.shape
    shape = jax.ShapeDtypeStruct(mid.shape, jnp.bfloat16)
    flops = 4 * planes * wall.shape[0] * wall.shape[1] * lanes
    return pl.pallas_call(
        functools.partial(_forward_kernel, planes=planes, depth=depth),
        out_shape=(
            shape,
            shape,
            jax.ShapeDtypeStruct(wall.shape, jnp.float32),
            jax.ShapeDtypeStruct((chans, 1), jnp.float32),
        ),
        in_specs=_vmem(7),
        out_specs=tuple(_vmem(4)),
        cost_estimate=pl.CostEstimate(flops=flops, transcendentals=planes * chans * lanes, bytes_accessed=5 * mid.size * 2),
    )(lo, mid, hi, wall, bias, cot, mask)


def input_call(lo, mid, hi, wall, mask, depth, first, count):
    planes, chans, lanes = mid.shape
    flops = 2 * count * wall.shape[0] * wall.shape[1] * lanes
    return pl.pallas_call(
        functools.partial(_input_kernel, planes=planes, first=first, depth=depth),
        out_shape=jax.ShapeDtypeStruct((count, chans, lanes), jnp.bfloat16),
        in_specs=_vmem(5),
        out_specs=_vmem(1)[0],
        cost_estimate=pl.CostEstimate(flops=flops, transcendentals=0, bytes_accessed=3 * mid.size * 2),
    )(lo, mid, hi, wall, mask)


def neighbours(first, last, axis):
    peers = lax.axis_size(axis)
    up = [(i, i + 1) for i in range(peers - 1)]
    down = [(j, i) for i, j in up]
    return lax.ppermute(last, axis, up), lax.ppermute(first, axis, down)


def swap(value, axis, bit):
    peers = lax.axis_size(axis)
    return lax.ppermute(value, axis, [(i, i ^ bit) for i in range(peers)])


def gather_rows(value, axis):
    peers = lax.axis_size(axis)
    me = lax.axis_index(axis)
    blocks = jnp.zeros((peers,) + value.shape, value.dtype)
    blocks = lax.dynamic_update_index_in_dim(blocks, value, me, 0)
    for k in range(1, peers):
        blocks = lax.dynamic_update_index_in_dim(blocks, swap(value, axis, k), me ^ k, 0)
    return blocks.reshape((peers * value.shape[0],) + value.shape[1:])


def reduction_rounds():
    rounds = []
    bit = lax.axis_size("real") // 2
    while bit >= 1:
        rounds.append(("real", bit))
        bit //= 2
    bit = 1
    while bit < lax.axis_size("strike"):
        rounds.append(("strike", bit))
        bit *= 2
    return rounds


def reduce_beside(value, carry, jobs):
    for k, (axis, bit) in enumerate(reduction_rounds()):
        if axis == "real":
            half = value.shape[0] // 2
            upper = (lax.axis_index(axis) // bit) % 2
            keep = lax.dynamic_slice_in_dim(value, upper * half, half, 0)
            send = lax.dynamic_slice_in_dim(value, (1 - upper) * half, half, 0)
        else:
            keep, send = value, value
        if k < len(jobs):
            send, carry = lax.optimization_barrier((send, carry))
            received = swap(send, axis, bit)
            carry = jobs[k](carry)
            received, carry = lax.optimization_barrier((received, carry))
        else:
            received = swap(send, axis, bit)
        value = keep + received
    for job in jobs[len(reduction_rounds()) :]:
        carry = job(carry)
    return value, carry


def local(grades, cotangent, weight, bias):
    field = grades[0]
    chans, planes, rows, depth = field.shape
    lanes = rows * depth
    taps_in = weight.shape[1]
    packed = jnp.concatenate([weight, bias[:, None]], axis=1)
    whole = gather_rows(packed, "real")
    whole_weight, whole_bias = whole[:, :taps_in], whole[:, taps_in]
    out_chan = whole_weight.shape[0]
    w5 = whole_weight.reshape(out_chan, 3, 3, 3, chans)
    forward_w = w5.transpose(2, 3, 0, 1, 4).reshape(9 * out_chan, 3 * chans)
    mask = jnp.asarray(plane_masks(rows, depth))

    def flat(value):
        return value.transpose(1, 0, 2, 3).reshape(planes, value.shape[0], lanes)

    def unflat(value):
        return value.reshape(planes, value.shape[1], rows, depth).transpose(1, 0, 2, 3)

    mid = flat(field)
    lo, hi = neighbours(mid[:1], mid[planes - 1 :], "strike")
    act, dpre, g, gb = forward_call(
        lo, mid, hi, forward_w, whole_bias.astype(jnp.float32)[:, None], flat(cotangent[0]), mask, depth
    )
    dlo, dhi = neighbours(dpre[:1], dpre[planes - 1 :], "strike")
    local_weight = g.reshape(3, 3, out_chan, 3, chans).transpose(2, 3, 0, 1, 4).reshape(out_chan, 27 * chans)
    local_grads = jnp.concatenate([local_weight, gb], axis=1)
    dlo, dhi, local_grads, activation = lax.optimization_barrier((dlo, dhi, local_grads, unflat(act)))

    def backward_weights(carry):
        weights = carry[3].reshape(out_chan, 3, 3, 3, chans)
        return carry[:3] + (weights[:, ::-1].transpose(2, 3, 4, 1, 0).reshape(9 * chans, 3 * out_chan),) + carry[4:]

    def plane_job(p):
        def job(carry):
            lo_d, mid_d, hi_d, weights = carry[:4]
            piece = input_call(lo_d, mid_d, hi_d, weights, mask, depth=depth, first=p, count=1)
            return carry + (piece,)
        return job

    def finish(carry):
        return (unflat(jnp.concatenate(carry[4:], axis=0)),)

    jobs = [lambda carry: plane_job(0)(backward_weights(carry))] + [plane_job(p) for p in range(1, planes)] + [finish]
    owned, (grad_input,) = reduce_beside(local_grads, (dlo, dpre, dhi, whole_weight), jobs)
    cells = lax.axis_size("real") * lax.axis_size("strike") * planes * rows * depth
    factor = 1.0 / cells**0.5
    owned = owned * factor
    return (activation[None], grad_input[None], owned[:, :taps_in], owned[:, taps_in])


def solution(mesh):
    in_specs = (
        P("real", None, "strike", None, None),
        P("real", None, "strike", None, None),
        P("real", None),
        P("real"),
    )
    out_specs = (
        P("real", None, "strike", None, None),
        P("real", None, "strike", None, None),
        P("real", None),
        P("real"),
    )
    return jax.shard_map(local, mesh=mesh, in_specs=in_specs, out_specs=out_specs, check_vma=False)
```

```python
import functools

import jax
import jax.numpy as jnp
import numpy as np
from jax import lax
from jax.experimental import pallas as pl
from jax.experimental.pallas import tpu as pltpu
from jax.sharding import PartitionSpec as P

OFFSETS = [(b, c) for b in (-1, 0, 1) for c in (-1, 0, 1)]


def plane_masks(rows, depth):
    y = np.arange(rows)[:, None]
    z = np.arange(depth)[None, :]
    masks = [((y + b >= 0) & (y + b < rows) & (z + c >= 0) & (z + c < depth)) for b, c in OFFSETS]
    return np.stack(masks).reshape(len(OFFSETS), 1, rows * depth).astype(np.float32)


def _stacked(haloed, h):
    return jnp.concatenate([haloed[h], haloed[h + 1], haloed[h + 2]], axis=0)


def _stacked_parts(lo, mid, hi, h, planes):
    def plane(index):
        if index == 0:
            return lo[0]
        if index == planes + 1:
            return hi[0]
        return mid[index - 1]
    return jnp.concatenate([plane(h), plane(h + 1), plane(h + 2)], axis=0)


def _shifted_sum(y, mask, chans, lanes, depth, sign):
    total = None
    for k, (b, c) in enumerate(OFFSETS):
        off = sign * (b * depth + c)
        block = y[k * chans : (k + 1) * chans]
        if off != 0:
            block = pltpu.roll(block, (-off) % lanes, 1)
            block = jnp.where(mask[k if sign > 0 else len(OFFSETS) - 1 - k] > 0.5, block, 0.0)
        total = block if total is None else total + block
    return total


def _forward_kernel(haloed, wall, bias, cot, mask, act_out, dpre_out, first_out, last_out, *, planes, depth):
    chans, lanes = haloed.shape[1], haloed.shape[2]
    for p in range(planes):
        y = jnp.dot(wall[...], _stacked(haloed, p), preferred_element_type=jnp.float32)
        pre = _shifted_sum(y, mask, chans, lanes, depth, 1) + bias[...]
        sig = 1.0 / (1.0 + jnp.exp(-pre))
        act_out[p] = (pre * sig).astype(act_out.dtype)
        dpre = (cot[p].astype(jnp.float32) * sig * (1.0 + pre * (1.0 - sig))).astype(dpre_out.dtype)
        dpre_out[p] = dpre
        if p == 0:
            first_out[0] = dpre
        if p == planes - 1:
            last_out[0] = dpre


def _input_kernel(lo, mid, hi, wall, mask, out, *, planes, first, depth):
    chans, lanes = mid.shape[1], mid.shape[2]
    for n in range(out.shape[0]):
        y = jnp.dot(wall[...], _stacked_parts(lo, mid, hi, first + n, planes), preferred_element_type=jnp.float32)
        out[n] = _shifted_sum(y, mask, chans, lanes, depth, -1).astype(out.dtype)


def _weight_kernel(haloed, dpre, mask, gw_out, gb_out, *, planes, depth):
    chans, lanes = dpre.shape[1], dpre.shape[2]
    gw = jnp.zeros(gw_out.shape, jnp.float32)
    gb = jnp.zeros(gb_out.shape, jnp.float32)
    for p in range(planes):
        d = dpre[p].astype(jnp.float32)
        gb = gb + jnp.sum(d, axis=1, keepdims=True)
        parts = []
        for k, (b, c) in enumerate(OFFSETS):
            off = b * depth + c
            e = d
            if off != 0:
                e = pltpu.roll(jnp.where(mask[k] > 0.5, d, 0.0), off % lanes, 1)
            parts.append(e.astype(jnp.bfloat16))
        gw = gw + lax.dot_general(
            jnp.concatenate(parts, axis=0), _stacked(haloed, p),
            (((1,), (1,)), ((), ())), preferred_element_type=jnp.float32,
        )
    gw_out[...] = gw
    gb_out[...] = gb


def _vmem(n):
    return [pl.BlockSpec(memory_space=pltpu.VMEM)] * n


def forward_call(haloed, wall, bias, cot, mask, depth):
    planes, chans, lanes = cot.shape
    shape = jax.ShapeDtypeStruct(cot.shape, jnp.bfloat16)
    edge = jax.ShapeDtypeStruct((1, chans, lanes), jnp.bfloat16)
    flops = 2 * planes * wall.shape[0] * wall.shape[1] * lanes
    return pl.pallas_call(
        functools.partial(_forward_kernel, planes=planes, depth=depth),
        out_shape=(shape, shape, edge, edge),
        in_specs=_vmem(5),
        out_specs=tuple(_vmem(4)),
        cost_estimate=pl.CostEstimate(flops=flops, transcendentals=planes * chans * lanes, bytes_accessed=5 * cot.size * 2),
    )(haloed, wall, bias, cot, mask)


def input_call(lo, mid, hi, wall, mask, depth, first, count):
    planes, chans, lanes = mid.shape
    flops = 2 * count * wall.shape[0] * wall.shape[1] * lanes
    return pl.pallas_call(
        functools.partial(_input_kernel, planes=planes, first=first, depth=depth),
        out_shape=jax.ShapeDtypeStruct((count, chans, lanes), jnp.bfloat16),
        in_specs=_vmem(5),
        out_specs=_vmem(1)[0],
        cost_estimate=pl.CostEstimate(flops=flops, transcendentals=0, bytes_accessed=3 * mid.size * 2),
    )(lo, mid, hi, wall, mask)


def weight_call(haloed, dpre, mask, depth):
    planes, chans, lanes = dpre.shape
    flops = 2 * planes * 9 * chans * 3 * chans * lanes
    return pl.pallas_call(
        functools.partial(_weight_kernel, planes=planes, depth=depth),
        out_shape=(jax.ShapeDtypeStruct((9 * chans, 3 * chans), jnp.float32), jax.ShapeDtypeStruct((chans, 1), jnp.float32)),
        in_specs=_vmem(3),
        out_specs=tuple(_vmem(2)),
        cost_estimate=pl.CostEstimate(flops=flops, transcendentals=0, bytes_accessed=3 * dpre.size * 2),
    )(haloed, dpre, mask)


def neighbours(first, last, axis):
    peers = lax.axis_size(axis)
    up = [(i, i + 1) for i in range(peers - 1)]
    down = [(j, i) for i, j in up]
    return lax.ppermute(last, axis, up), lax.ppermute(first, axis, down)


def swap(value, axis, bit):
    peers = lax.axis_size(axis)
    return lax.ppermute(value, axis, [(i, i ^ bit) for i in range(peers)])


def gather_rows(value, axis):
    peers = lax.axis_size(axis)
    me = lax.axis_index(axis)
    blocks = jnp.zeros((peers,) + value.shape, value.dtype)
    blocks = lax.dynamic_update_index_in_dim(blocks, value, me, 0)
    for k in range(1, peers):
        blocks = lax.dynamic_update_index_in_dim(blocks, swap(value, axis, k), me ^ k, 0)
    return blocks.reshape((peers * value.shape[0],) + value.shape[1:])


def reduce_beside(local_grads, work):
    rounds = []
    bit = lax.axis_size("real") // 2
    while bit >= 1:
        rounds.append(("real", bit))
        bit //= 2
    bit = 1
    while bit < lax.axis_size("strike"):
        rounds.append(("strike", bit))
        bit *= 2
    results = []
    value = local_grads
    for k, (axis, bit) in enumerate(rounds):
        if axis == "real":
            half = value.shape[0] // 2
            upper = (lax.axis_index(axis) // bit) % 2
            keep = lax.dynamic_slice_in_dim(value, upper * half, half, 0)
            send = lax.dynamic_slice_in_dim(value, (1 - upper) * half, half, 0)
        else:
            keep, send = value, value
        if k < len(work):
            send, inputs = lax.optimization_barrier((send, work[k][1]))
            received = swap(send, axis, bit)
            result = work[k][0](*inputs)
            received, result = lax.optimization_barrier((received, result))
            results.append(result)
        else:
            received = swap(send, axis, bit)
        value = keep + received
    for job, inputs in work[len(rounds) :]:
        results.append(job(*inputs))
    return value, results


def local(grades, cotangent, weight, bias):
    field = grades[0]
    chans, planes, rows, depth = field.shape
    lanes = rows * depth
    taps_in = weight.shape[1]
    packed = jnp.concatenate([weight, bias[:, None]], axis=1)
    whole = gather_rows(packed, "real")
    whole_weight, whole_bias = whole[:, :taps_in], whole[:, taps_in]
    out_chan = whole_weight.shape[0]
    w5 = whole_weight.reshape(out_chan, 3, 3, 3, chans)
    forward_w = w5.transpose(2, 3, 0, 1, 4).reshape(9 * out_chan, 3 * chans)
    backward_w = w5[:, ::-1].transpose(2, 3, 4, 1, 0).reshape(9 * chans, 3 * out_chan)
    mask = jnp.asarray(plane_masks(rows, depth))

    def flat(value):
        return value.transpose(1, 0, 2, 3).reshape(planes, value.shape[0], lanes)

    def unflat(value):
        return value.reshape(planes, value.shape[1], rows, depth).transpose(1, 0, 2, 3)

    below, above = neighbours(field[:, :1], field[:, planes - 1 :], "strike")
    haloed = jnp.concatenate([below, field, above], axis=1)
    haloed = haloed.transpose(1, 0, 2, 3).reshape(planes + 2, chans, lanes)
    act, dpre, first, last = forward_call(
        haloed, forward_w, whole_bias.astype(jnp.float32)[:, None], flat(cotangent[0]), mask, depth
    )
    dlo, dhi = neighbours(first, last, "strike")
    g, gb = weight_call(haloed, dpre, mask, depth)
    local_weight = g.reshape(3, 3, out_chan, 3, chans).transpose(2, 3, 0, 1, 4).reshape(out_chan, 27 * chans)
    local_grads = jnp.concatenate([local_weight, gb], axis=1)
    work = [
        (functools.partial(input_call, depth=depth, first=p, count=1), (dlo, dpre, dhi, backward_w, mask))
        for p in range(planes)
    ]
    owned, pieces = reduce_beside(local_grads, work)
    grad_input = unflat(jnp.concatenate(pieces, axis=0))
    cells = lax.axis_size("real") * lax.axis_size("strike") * planes * rows * depth
    factor = 1.0 / cells**0.5
    owned = owned * factor
    return (unflat(act)[None], grad_input[None], owned[:, :taps_in], owned[:, taps_in])


def solution(mesh):
    in_specs = (
        P("real", None, "strike", None, None),
        P("real", None, "strike", None, None),
        P("real", None),
        P("real"),
    )
    out_specs = (
        P("real", None, "strike", None, None),
        P("real", None, "strike", None, None),
        P("real", None),
        P("real"),
    )
    return jax.shard_map(local, mesh=mesh, in_specs=in_specs, out_specs=out_specs, check_vma=False)
```

```python
import functools

import jax
import jax.numpy as jnp
import numpy as np
from jax import lax
from jax.experimental import pallas as pl
from jax.experimental.pallas import tpu as pltpu
from jax.sharding import PartitionSpec as P

OFFSETS = [(b, c) for b in (-1, 0, 1) for c in (-1, 0, 1)]


def plane_masks(rows, depth):
    y = np.arange(rows)[:, None]
    z = np.arange(depth)[None, :]
    masks = [((y + b >= 0) & (y + b < rows) & (z + c >= 0) & (z + c < depth)) for b, c in OFFSETS]
    return np.stack(masks).reshape(len(OFFSETS), 1, rows * depth).astype(np.float32)


def _stacked(haloed, h):
    return jnp.concatenate([haloed[h], haloed[h + 1], haloed[h + 2]], axis=0)


def _stacked_parts(lo, mid, hi, h, planes):
    def plane(index):
        if index == 0:
            return lo[0]
        if index == planes + 1:
            return hi[0]
        return mid[index - 1]
    return jnp.concatenate([plane(h), plane(h + 1), plane(h + 2)], axis=0)


def _shifted_sum(y, mask, chans, lanes, depth, sign):
    total = None
    for k, (b, c) in enumerate(OFFSETS):
        off = sign * (b * depth + c)
        block = y[k * chans : (k + 1) * chans]
        if off != 0:
            block = pltpu.roll(block, (-off) % lanes, 1)
            block = jnp.where(mask[k if sign > 0 else len(OFFSETS) - 1 - k] > 0.5, block, 0.0)
        total = block if total is None else total + block
    return total


def _forward_kernel(haloed, wall, bias, cot, mask, act_out, dpre_out, first_out, last_out, *, planes, depth):
    chans, lanes = haloed.shape[1], haloed.shape[2]
    for p in range(planes):
        y = jnp.dot(wall[...], _stacked(haloed, p), preferred_element_type=jnp.float32)
        pre = _shifted_sum(y, mask, chans, lanes, depth, 1) + bias[...]
        sig = 1.0 / (1.0 + jnp.exp(-pre))
        act_out[p] = (pre * sig).astype(act_out.dtype)
        dpre = (cot[p].astype(jnp.float32) * sig * (1.0 + pre * (1.0 - sig))).astype(dpre_out.dtype)
        dpre_out[p] = dpre
        if p == 0:
            first_out[0] = dpre
        if p == planes - 1:
            last_out[0] = dpre


def _input_kernel(lo, mid, hi, wall, mask, out, *, planes, first, depth):
    chans, lanes = mid.shape[1], mid.shape[2]
    for n in range(out.shape[0]):
        y = jnp.dot(wall[...], _stacked_parts(lo, mid, hi, first + n, planes), preferred_element_type=jnp.float32)
        out[n] = _shifted_sum(y, mask, chans, lanes, depth, -1).astype(out.dtype)


def _weight_kernel(haloed, dpre, mask, gw_out, *, planes, depth):
    chans, lanes = dpre.shape[1], dpre.shape[2]
    gw = jnp.zeros((9 * chans, 3 * chans), jnp.float32)
    gb = jnp.zeros((chans, 1), jnp.float32)
    for p in range(planes):
        d = dpre[p].astype(jnp.float32)
        gb = gb + jnp.sum(d, axis=1, keepdims=True)
        parts = []
        for k, (b, c) in enumerate(OFFSETS):
            off = b * depth + c
            e = d
            if off != 0:
                e = pltpu.roll(jnp.where(mask[k] > 0.5, d, 0.0), off % lanes, 1)
            parts.append(e.astype(jnp.bfloat16))
        gw = gw + lax.dot_general(
            jnp.concatenate(parts, axis=0), _stacked(haloed, p),
            (((1,), (1,)), ((), ())), preferred_element_type=jnp.float32,
        )
    chans_in = gw.shape[1] // 3
    for k in range(len(OFFSETS)):
        for a in range(3):
            t = 9 * a + k
            gw_out[:, t * chans_in : (t + 1) * chans_in] = gw[k * chans : (k + 1) * chans, a * chans_in : (a + 1) * chans_in]
    gw_out[:, 27 * chans_in :] = gb


def _vmem(n):
    return [pl.BlockSpec(memory_space=pltpu.VMEM)] * n


def forward_call(haloed, wall, bias, cot, mask, depth):
    planes, chans, lanes = cot.shape
    shape = jax.ShapeDtypeStruct(cot.shape, jnp.bfloat16)
    edge = jax.ShapeDtypeStruct((1, chans, lanes), jnp.bfloat16)
    flops = 2 * planes * wall.shape[0] * wall.shape[1] * lanes
    return pl.pallas_call(
        functools.partial(_forward_kernel, planes=planes, depth=depth),
        out_shape=(shape, shape, edge, edge),
        in_specs=_vmem(5),
        out_specs=tuple(_vmem(4)),
        cost_estimate=pl.CostEstimate(flops=flops, transcendentals=planes * chans * lanes, bytes_accessed=5 * cot.size * 2),
    )(haloed, wall, bias, cot, mask)


def input_call(lo, mid, hi, wall, mask, depth, first, count):
    planes, chans, lanes = mid.shape
    flops = 2 * count * wall.shape[0] * wall.shape[1] * lanes
    return pl.pallas_call(
        functools.partial(_input_kernel, planes=planes, first=first, depth=depth),
        out_shape=jax.ShapeDtypeStruct((count, chans, lanes), jnp.bfloat16),
        in_specs=_vmem(5),
        out_specs=_vmem(1)[0],
        cost_estimate=pl.CostEstimate(flops=flops, transcendentals=0, bytes_accessed=3 * mid.size * 2),
    )(lo, mid, hi, wall, mask)


def weight_call(haloed, dpre, mask, depth):
    planes, chans, lanes = dpre.shape
    flops = 2 * planes * 9 * chans * 3 * chans * lanes
    return pl.pallas_call(
        functools.partial(_weight_kernel, planes=planes, depth=depth),
        out_shape=jax.ShapeDtypeStruct((chans, 27 * chans + 1), jnp.float32),
        in_specs=_vmem(3),
        out_specs=_vmem(1)[0],
        cost_estimate=pl.CostEstimate(flops=flops, transcendentals=0, bytes_accessed=3 * dpre.size * 2),
    )(haloed, dpre, mask)


def neighbours(first, last, axis):
    peers = lax.axis_size(axis)
    up = [(i, i + 1) for i in range(peers - 1)]
    down = [(j, i) for i, j in up]
    return lax.ppermute(last, axis, up), lax.ppermute(first, axis, down)


def swap(value, axis, bit):
    peers = lax.axis_size(axis)
    return lax.ppermute(value, axis, [(i, i ^ bit) for i in range(peers)])


def gather_rows(value, axis):
    peers = lax.axis_size(axis)
    me = lax.axis_index(axis)
    blocks = jnp.zeros((peers,) + value.shape, value.dtype)
    blocks = lax.dynamic_update_index_in_dim(blocks, value, me, 0)
    for k in range(1, peers):
        blocks = lax.dynamic_update_index_in_dim(blocks, swap(value, axis, k), me ^ k, 0)
    return blocks.reshape((peers * value.shape[0],) + value.shape[1:])


def reduce_beside(local_grads, work):
    rounds = []
    bit = lax.axis_size("real") // 2
    while bit >= 1:
        rounds.append(("real", bit))
        bit //= 2
    bit = 1
    while bit < lax.axis_size("strike"):
        rounds.append(("strike", bit))
        bit *= 2
    results = []
    value = local_grads
    for k, (axis, bit) in enumerate(rounds):
        if axis == "real":
            half = value.shape[0] // 2
            upper = (lax.axis_index(axis) // bit) % 2
            keep = lax.dynamic_slice_in_dim(value, upper * half, half, 0)
            send = lax.dynamic_slice_in_dim(value, (1 - upper) * half, half, 0)
        else:
            keep, send = value, value
        if k < len(work):
            send, inputs = lax.optimization_barrier((send, work[k][1]))
            received = swap(send, axis, bit)
            result = work[k][0](*inputs)
            received, result = lax.optimization_barrier((received, result))
            results.append(result)
        else:
            received = swap(send, axis, bit)
        value = keep + received
    for job, inputs in work[len(rounds) :]:
        results.append(job(*inputs))
    return value, results


def local(grades, cotangent, weight, bias):
    field = grades[0]
    chans, planes, rows, depth = field.shape
    lanes = rows * depth
    taps_in = weight.shape[1]
    packed = jnp.concatenate([weight, bias[:, None]], axis=1)
    whole = gather_rows(packed, "real")
    whole_weight, whole_bias = whole[:, :taps_in], whole[:, taps_in]
    out_chan = whole_weight.shape[0]
    w5 = whole_weight.reshape(out_chan, 3, 3, 3, chans)
    forward_w = w5.transpose(2, 3, 0, 1, 4).reshape(9 * out_chan, 3 * chans)
    backward_w = w5[:, ::-1].transpose(2, 3, 4, 1, 0).reshape(9 * chans, 3 * out_chan)
    mask = jnp.asarray(plane_masks(rows, depth))

    def flat(value):
        return value.transpose(1, 0, 2, 3).reshape(planes, value.shape[0], lanes)

    def unflat(value):
        return value.reshape(planes, value.shape[1], rows, depth).transpose(1, 0, 2, 3)

    below, above = neighbours(field[:, :1], field[:, planes - 1 :], "strike")
    haloed = jnp.concatenate([below, field, above], axis=1)
    haloed = haloed.transpose(1, 0, 2, 3).reshape(planes + 2, chans, lanes)
    act, dpre, first, last = forward_call(
        haloed, forward_w, whole_bias.astype(jnp.float32)[:, None], flat(cotangent[0]), mask, depth
    )
    dlo, dhi = neighbours(first, last, "strike")
    local_grads = weight_call(haloed, dpre, mask, depth)
    work = [
        (functools.partial(input_call, depth=depth, first=p, count=1), (dlo, dpre, dhi, backward_w, mask))
        for p in range(planes)
    ]
    owned, pieces = reduce_beside(local_grads, work)
    grad_input = unflat(jnp.concatenate(pieces, axis=0))
    cells = lax.axis_size("real") * lax.axis_size("strike") * planes * rows * depth
    factor = 1.0 / cells**0.5
    owned = owned * factor
    return (unflat(act)[None], grad_input[None], owned[:, :taps_in], owned[:, taps_in])


def solution(mesh):
    in_specs = (
        P("real", None, "strike", None, None),
        P("real", None, "strike", None, None),
        P("real", None),
        P("real"),
    )
    out_specs = (
        P("real", None, "strike", None, None),
        P("real", None, "strike", None, None),
        P("real", None),
        P("real"),
    )
    return jax.shard_map(local, mesh=mesh, in_specs=in_specs, out_specs=out_specs, check_vma=False)
```

```python
import functools

import jax
import jax.numpy as jnp
import numpy as np
from jax import lax
from jax.experimental import pallas as pl
from jax.experimental.pallas import tpu as pltpu
from jax.sharding import PartitionSpec as P

OFFSETS = [(b, c) for b in (-1, 0, 1) for c in (-1, 0, 1)]


def plane_masks(rows, depth):
    y = np.arange(rows)[:, None]
    z = np.arange(depth)[None, :]
    masks = [((y + b >= 0) & (y + b < rows) & (z + c >= 0) & (z + c < depth)) for b, c in OFFSETS]
    return np.stack(masks).reshape(len(OFFSETS), 1, rows * depth).astype(np.float32)


def _stacked(haloed, h):
    return jnp.concatenate([haloed[h], haloed[h + 1], haloed[h + 2]], axis=0)


def _stacked_parts(lo, mid, hi, h, planes):
    def plane(index):
        if index == 0:
            return lo[0]
        if index == planes + 1:
            return hi[0]
        return mid[index - 1]
    return jnp.concatenate([plane(h), plane(h + 1), plane(h + 2)], axis=0)


def _shifted_sum(y, mask, chans, lanes, depth, sign):
    total = None
    for k, (b, c) in enumerate(OFFSETS):
        off = sign * (b * depth + c)
        block = y[k * chans : (k + 1) * chans]
        if off != 0:
            block = pltpu.roll(block, (-off) % lanes, 1)
            block = jnp.where(mask[k if sign > 0 else len(OFFSETS) - 1 - k] > 0.5, block, 0.0)
        total = block if total is None else total + block
    return total


def _forward_kernel(haloed, wall, bias, cot, mask, act_out, dpre_out, first_out, last_out, *, planes, depth):
    chans, lanes = haloed.shape[1], haloed.shape[2]
    for p in range(planes):
        y = jnp.dot(wall[...], _stacked(haloed, p), preferred_element_type=jnp.float32)
        pre = _shifted_sum(y, mask, chans, lanes, depth, 1) + bias[...]
        sig = 1.0 / (1.0 + jnp.exp(-pre))
        act_out[p] = (pre * sig).astype(act_out.dtype)
        dpre = (cot[p].astype(jnp.float32) * sig * (1.0 + pre * (1.0 - sig))).astype(dpre_out.dtype)
        dpre_out[p] = dpre
        if p == 0:
            first_out[0] = dpre
        if p == planes - 1:
            last_out[0] = dpre


def _input_kernel(lo, mid, hi, wall, mask, out, *, planes, first, depth):
    chans, lanes = mid.shape[1], mid.shape[2]
    for n in range(out.shape[0]):
        y = jnp.dot(wall[...], _stacked_parts(lo, mid, hi, first + n, planes), preferred_element_type=jnp.float32)
        out[n] = _shifted_sum(y, mask, chans, lanes, depth, -1).astype(out.dtype)


def _weight_kernel(haloed, dpre, mask, gw_out, *, planes, depth):
    chans, lanes = dpre.shape[1], dpre.shape[2]
    gw = jnp.zeros((9 * chans, 3 * chans), jnp.float32)
    gb = jnp.zeros((chans, 1), jnp.float32)
    for p in range(planes):
        d = dpre[p].astype(jnp.float32)
        gb = gb + jnp.sum(d, axis=1, keepdims=True)
        parts = []
        for k, (b, c) in enumerate(OFFSETS):
            off = b * depth + c
            e = d
            if off != 0:
                e = pltpu.roll(jnp.where(mask[k] > 0.5, d, 0.0), off % lanes, 1)
            parts.append(e.astype(jnp.bfloat16))
        gw = gw + lax.dot_general(
            jnp.concatenate(parts, axis=0), _stacked(haloed, p),
            (((1,), (1,)), ((), ())), preferred_element_type=jnp.float32,
        )
    chans_in = gw.shape[1] // 3
    for k in range(len(OFFSETS)):
        for a in range(3):
            t = 9 * a + k
            gw_out[:, t * chans_in : (t + 1) * chans_in] = gw[k * chans : (k + 1) * chans, a * chans_in : (a + 1) * chans_in]
    gw_out[:, 27 * chans_in :] = gb


def _vmem(n):
    return [pl.BlockSpec(memory_space=pltpu.VMEM)] * n


def forward_call(haloed, wall, bias, cot, mask, depth):
    planes, chans, lanes = cot.shape
    shape = jax.ShapeDtypeStruct(cot.shape, jnp.bfloat16)
    edge = jax.ShapeDtypeStruct((1, chans, lanes), jnp.bfloat16)
    flops = 2 * planes * wall.shape[0] * wall.shape[1] * lanes
    return pl.pallas_call(
        functools.partial(_forward_kernel, planes=planes, depth=depth),
        out_shape=(shape, shape, edge, edge),
        in_specs=_vmem(5),
        out_specs=tuple(_vmem(4)),
        cost_estimate=pl.CostEstimate(flops=flops, transcendentals=planes * chans * lanes, bytes_accessed=5 * cot.size * 2),
    )(haloed, wall, bias, cot, mask)


def input_call(lo, mid, hi, wall, mask, depth, first, count):
    planes, chans, lanes = mid.shape
    flops = 2 * count * wall.shape[0] * wall.shape[1] * lanes
    return pl.pallas_call(
        functools.partial(_input_kernel, planes=planes, first=first, depth=depth),
        out_shape=jax.ShapeDtypeStruct((count, chans, lanes), jnp.bfloat16),
        in_specs=_vmem(5),
        out_specs=_vmem(1)[0],
        cost_estimate=pl.CostEstimate(flops=flops, transcendentals=0, bytes_accessed=3 * mid.size * 2),
    )(lo, mid, hi, wall, mask)


def weight_call(haloed, dpre, mask, depth):
    planes, chans, lanes = dpre.shape
    flops = 2 * planes * 9 * chans * 3 * chans * lanes
    return pl.pallas_call(
        functools.partial(_weight_kernel, planes=planes, depth=depth),
        out_shape=jax.ShapeDtypeStruct((chans, 27 * chans + 1), jnp.float32),
        in_specs=_vmem(3),
        out_specs=_vmem(1)[0],
        cost_estimate=pl.CostEstimate(flops=flops, transcendentals=0, bytes_accessed=3 * dpre.size * 2),
    )(haloed, dpre, mask)


def neighbours(first, last, axis, ordered=False):
    peers = lax.axis_size(axis)
    odd = lax.axis_index(axis) % 2 == 1
    pairs = [(i, i + 1) for i in range(1, peers - 1, 2)]
    within_send = jnp.where(odd, first, last)
    across = lax.ppermute(jnp.where(odd, last, first), axis, pairs + [(j, i) for i, j in pairs])
    if ordered:
        within_send, across = lax.optimization_barrier((within_send, across))
    within = swap(within_send, axis, 1)
    return jnp.where(odd, within, across), jnp.where(odd, across, within)


def swap(value, axis, bit):
    peers = lax.axis_size(axis)
    return lax.ppermute(value, axis, [(i, i ^ bit) for i in range(peers)])


def gather_rows(value, axis):
    peers = lax.axis_size(axis)
    me = lax.axis_index(axis)
    blocks = jnp.zeros((peers,) + value.shape, value.dtype)
    blocks = lax.dynamic_update_index_in_dim(blocks, value, me, 0)
    for k in range(1, peers):
        blocks = lax.dynamic_update_index_in_dim(blocks, swap(value, axis, k), me ^ k, 0)
    return blocks.reshape((peers * value.shape[0],) + value.shape[1:])


def reduce_beside(local_grads, work):
    rounds = []
    bit = lax.axis_size("real") // 2
    while bit >= 1:
        rounds.append(("real", bit))
        bit //= 2
    bit = 1
    while bit < lax.axis_size("strike"):
        rounds.append(("strike", bit))
        bit *= 2
    results = []
    value = local_grads
    for k, (axis, bit) in enumerate(rounds):
        if axis == "real":
            half = value.shape[0] // 2
            upper = (lax.axis_index(axis) // bit) % 2
            keep = lax.dynamic_slice_in_dim(value, upper * half, half, 0)
            send = lax.dynamic_slice_in_dim(value, (1 - upper) * half, half, 0)
        else:
            keep, send = value, value
        if k < len(work):
            send, inputs = lax.optimization_barrier((send, work[k][1]))
            received = swap(send, axis, bit)
            result = work[k][0](*inputs)
            received, result = lax.optimization_barrier((received, result))
            results.append(result)
        else:
            received = swap(send, axis, bit)
        value = keep + received
    for job, inputs in work[len(rounds) :]:
        results.append(job(*inputs))
    return value, results


def local(grades, cotangent, weight, bias):
    field = grades[0]
    chans, planes, rows, depth = field.shape
    lanes = rows * depth
    taps_in = weight.shape[1]
    packed = jnp.concatenate([weight, bias[:, None]], axis=1)
    whole = gather_rows(packed, "real")
    whole_weight, whole_bias = whole[:, :taps_in], whole[:, taps_in]
    out_chan = whole_weight.shape[0]
    w5 = whole_weight.reshape(out_chan, 3, 3, 3, chans)
    forward_w = w5.transpose(2, 3, 0, 1, 4).reshape(9 * out_chan, 3 * chans)
    backward_w = w5[:, ::-1].transpose(2, 3, 4, 1, 0).reshape(9 * chans, 3 * out_chan)
    mask = jnp.asarray(plane_masks(rows, depth))

    def flat(value):
        return value.transpose(1, 0, 2, 3).reshape(planes, value.shape[0], lanes)

    def unflat(value):
        return value.reshape(planes, value.shape[1], rows, depth).transpose(1, 0, 2, 3)

    below, above = neighbours(field[:, :1], field[:, planes - 1 :], "strike", ordered=True)
    haloed = jnp.concatenate([below, field, above], axis=1)
    haloed = haloed.transpose(1, 0, 2, 3).reshape(planes + 2, chans, lanes)
    act, dpre, first, last = forward_call(
        haloed, forward_w, whole_bias.astype(jnp.float32)[:, None], flat(cotangent[0]), mask, depth
    )
    dlo, dhi = neighbours(first, last, "strike")
    local_grads = weight_call(haloed, dpre, mask, depth)
    work = [
        (functools.partial(input_call, depth=depth, first=p, count=1), (dlo, dpre, dhi, backward_w, mask))
        for p in range(planes)
    ]
    owned, pieces = reduce_beside(local_grads, work)
    grad_input = unflat(jnp.concatenate(pieces, axis=0))
    cells = lax.axis_size("real") * lax.axis_size("strike") * planes * rows * depth
    factor = 1.0 / cells**0.5
    owned = owned * factor
    return (unflat(act)[None], grad_input[None], owned[:, :taps_in], owned[:, taps_in])


def solution(mesh):
    in_specs = (
        P("real", None, "strike", None, None),
        P("real", None, "strike", None, None),
        P("real", None),
        P("real"),
    )
    out_specs = (
        P("real", None, "strike", None, None),
        P("real", None, "strike", None, None),
        P("real", None),
        P("real"),
    )
    return jax.shard_map(local, mesh=mesh, in_specs=in_specs, out_specs=out_specs, check_vma=False)
```

```python
import functools

import jax
import jax.numpy as jnp
import numpy as np
from jax import lax
from jax.experimental import pallas as pl
from jax.experimental.pallas import tpu as pltpu
from jax.sharding import PartitionSpec as P

OFFSETS = [(b, c) for b in (-1, 0, 1) for c in (-1, 0, 1)]


def plane_masks(rows, depth):
    y = np.arange(rows)[:, None]
    z = np.arange(depth)[None, :]
    masks = [((y + b >= 0) & (y + b < rows) & (z + c >= 0) & (z + c < depth)) for b, c in OFFSETS]
    return np.stack(masks).reshape(len(OFFSETS), 1, rows * depth).astype(np.float32)


def _stacked(haloed, h):
    return jnp.concatenate([haloed[h], haloed[h + 1], haloed[h + 2]], axis=0)


def _stacked_parts(lo, mid, hi, h, planes):
    def plane(index):
        if index == 0:
            return lo[0]
        if index == planes + 1:
            return hi[0]
        return mid[index - 1]
    return jnp.concatenate([plane(h), plane(h + 1), plane(h + 2)], axis=0)


def _shifted_sum(y, mask, chans, lanes, depth, sign):
    total = None
    for k, (b, c) in enumerate(OFFSETS):
        off = sign * (b * depth + c)
        block = y[k * chans : (k + 1) * chans]
        if off != 0:
            block = pltpu.roll(block, (-off) % lanes, 1)
            block = jnp.where(mask[k if sign > 0 else len(OFFSETS) - 1 - k] > 0.5, block, 0.0)
        total = block if total is None else total + block
    return total


def _forward_kernel(haloed, wall, packed, cot, mask, act_out, dpre_out, first_out, last_out, *, planes, depth):
    chans, lanes = haloed.shape[1], haloed.shape[2]
    bias = packed[:, packed.shape[1] - 1 :].astype(jnp.float32)
    for p in range(planes):
        y = jnp.dot(wall[...], _stacked(haloed, p), preferred_element_type=jnp.float32)
        pre = _shifted_sum(y, mask, chans, lanes, depth, 1) + bias
        sig = 1.0 / (1.0 + jnp.exp(-pre))
        act_out[p] = (pre * sig).astype(act_out.dtype)
        dpre = (cot[p].astype(jnp.float32) * sig * (1.0 + pre * (1.0 - sig))).astype(dpre_out.dtype)
        dpre_out[p] = dpre
        if p == 0:
            first_out[0] = dpre
        if p == planes - 1:
            last_out[0] = dpre


def _input_kernel(lo, mid, hi, wall, mask, out, *, planes, first, depth):
    chans, lanes = mid.shape[1], mid.shape[2]
    for n in range(out.shape[0]):
        y = jnp.dot(wall[...], _stacked_parts(lo, mid, hi, first + n, planes), preferred_element_type=jnp.float32)
        out[n] = _shifted_sum(y, mask, chans, lanes, depth, -1).astype(out.dtype)


def _weight_kernel(haloed, dpre, mask, gw_out, *, planes, depth):
    chans, lanes = dpre.shape[1], dpre.shape[2]
    gw = jnp.zeros((9 * chans, 3 * chans), jnp.float32)
    gb = jnp.zeros((chans, 1), jnp.float32)
    for p in range(planes):
        d = dpre[p].astype(jnp.float32)
        gb = gb + jnp.sum(d, axis=1, keepdims=True)
        parts = []
        for k, (b, c) in enumerate(OFFSETS):
            off = b * depth + c
            e = d
            if off != 0:
                e = pltpu.roll(jnp.where(mask[k] > 0.5, d, 0.0), off % lanes, 1)
            parts.append(e.astype(jnp.bfloat16))
        gw = gw + lax.dot_general(
            jnp.concatenate(parts, axis=0), _stacked(haloed, p),
            (((1,), (1,)), ((), ())), preferred_element_type=jnp.float32,
        )
    chans_in = gw.shape[1] // 3
    for k in range(len(OFFSETS)):
        for a in range(3):
            t = 9 * a + k
            gw_out[:, t * chans_in : (t + 1) * chans_in] = gw[k * chans : (k + 1) * chans, a * chans_in : (a + 1) * chans_in]
    gw_out[:, 27 * chans_in :] = gb


def _vmem(n):
    return [pl.BlockSpec(memory_space=pltpu.VMEM)] * n


def forward_call(haloed, wall, packed, cot, mask, depth):
    planes, chans, lanes = cot.shape
    shape = jax.ShapeDtypeStruct(cot.shape, jnp.bfloat16)
    edge = jax.ShapeDtypeStruct((1, chans, lanes), jnp.bfloat16)
    flops = 2 * planes * wall.shape[0] * wall.shape[1] * lanes
    return pl.pallas_call(
        functools.partial(_forward_kernel, planes=planes, depth=depth),
        out_shape=(shape, shape, edge, edge),
        in_specs=_vmem(5),
        out_specs=tuple(_vmem(4)),
        cost_estimate=pl.CostEstimate(flops=flops, transcendentals=planes * chans * lanes, bytes_accessed=5 * cot.size * 2),
    )(haloed, wall, packed, cot, mask)


def input_call(lo, mid, hi, wall, mask, depth, first, count):
    planes, chans, lanes = mid.shape
    flops = 2 * count * wall.shape[0] * wall.shape[1] * lanes
    return pl.pallas_call(
        functools.partial(_input_kernel, planes=planes, first=first, depth=depth),
        out_shape=jax.ShapeDtypeStruct((count, chans, lanes), jnp.bfloat16),
        in_specs=_vmem(5),
        out_specs=_vmem(1)[0],
        cost_estimate=pl.CostEstimate(flops=flops, transcendentals=0, bytes_accessed=3 * mid.size * 2),
    )(lo, mid, hi, wall, mask)


def weight_call(haloed, dpre, mask, depth):
    planes, chans, lanes = dpre.shape
    flops = 2 * planes * 9 * chans * 3 * chans * lanes
    return pl.pallas_call(
        functools.partial(_weight_kernel, planes=planes, depth=depth),
        out_shape=jax.ShapeDtypeStruct((chans, 27 * chans + 1), jnp.float32),
        in_specs=_vmem(3),
        out_specs=_vmem(1)[0],
        cost_estimate=pl.CostEstimate(flops=flops, transcendentals=0, bytes_accessed=3 * dpre.size * 2),
    )(haloed, dpre, mask)


def neighbours(first, last, axis):
    peers = lax.axis_size(axis)
    up = [(i, i + 1) for i in range(peers - 1)]
    down = [(j, i) for i, j in up]
    return lax.ppermute(last, axis, up), lax.ppermute(first, axis, down)


def swap(value, axis, bit):
    peers = lax.axis_size(axis)
    return lax.ppermute(value, axis, [(i, i ^ bit) for i in range(peers)])


def gather_rows(value, axis):
    peers = lax.axis_size(axis)
    me = lax.axis_index(axis)
    blocks = jnp.zeros((peers,) + value.shape, value.dtype)
    blocks = lax.dynamic_update_index_in_dim(blocks, value, me, 0)
    for k in range(1, peers):
        blocks = lax.dynamic_update_index_in_dim(blocks, swap(value, axis, k), me ^ k, 0)
    return blocks.reshape((peers * value.shape[0],) + value.shape[1:])


def reduce_beside(value, carry, jobs):
    rounds = []
    bit = lax.axis_size("real") // 2
    while bit >= 1:
        rounds.append(("real", bit))
        bit //= 2
    bit = 1
    while bit < lax.axis_size("strike"):
        rounds.append(("strike", bit))
        bit *= 2
    for k, (axis, bit) in enumerate(rounds):
        if axis == "real":
            half = value.shape[0] // 2
            upper = (lax.axis_index(axis) // bit) % 2
            keep = lax.dynamic_slice_in_dim(value, upper * half, half, 0)
            send = lax.dynamic_slice_in_dim(value, (1 - upper) * half, half, 0)
        else:
            keep, send = value, value
        if k < len(jobs):
            send, carry = lax.optimization_barrier((send, carry))
            received = swap(send, axis, bit)
            carry = jobs[k](carry)
            received, carry = lax.optimization_barrier((received, carry))
        else:
            received = swap(send, axis, bit)
        value = keep + received
    for job in jobs[len(rounds) :]:
        carry = job(carry)
    return value, carry


def local(grades, cotangent, weight, bias):
    field = grades[0]
    chans, planes, rows, depth = field.shape
    lanes = rows * depth
    taps_in = weight.shape[1]
    packed = jnp.concatenate([weight, bias[:, None]], axis=1)
    whole = gather_rows(packed, "real")
    whole_weight = whole[:, :taps_in]
    out_chan = whole_weight.shape[0]
    w5 = whole_weight.reshape(out_chan, 3, 3, 3, chans)
    forward_w = w5.transpose(2, 3, 0, 1, 4).reshape(9 * out_chan, 3 * chans)
    mask = jnp.asarray(plane_masks(rows, depth))

    def flat(value):
        return value.transpose(1, 0, 2, 3).reshape(planes, value.shape[0], lanes)

    def unflat(value):
        return value.reshape(planes, value.shape[1], rows, depth).transpose(1, 0, 2, 3)

    below, above = neighbours(field[:, :1], field[:, planes - 1 :], "strike")
    haloed = jnp.concatenate([below, field, above], axis=1)
    haloed = haloed.transpose(1, 0, 2, 3).reshape(planes + 2, chans, lanes)
    act, dpre, first, last = forward_call(
        haloed, forward_w, whole, flat(cotangent[0]), mask, depth
    )
    dlo, dhi = neighbours(first, last, "strike")
    local_grads = weight_call(haloed, dpre, mask, depth)

    def plane_job(p, first_job):
        def job(carry):
            lo_d, mid_d, hi_d, weights = carry[:4]
            if first_job:
                weights = weights.reshape(out_chan, 3, 3, 3, chans)[:, ::-1]
                weights = weights.transpose(2, 3, 4, 1, 0).reshape(9 * chans, 3 * out_chan)
            piece = input_call(lo_d, mid_d, hi_d, weights, mask, depth=depth, first=p, count=1)
            return (lo_d, mid_d, hi_d, weights) + carry[4:] + (piece,)
        return job

    jobs = [plane_job(p, p == 0) for p in range(planes)]
    owned, carry = reduce_beside(local_grads, (dlo, dpre, dhi, whole_weight), jobs)
    grad_input = unflat(jnp.concatenate(carry[4:], axis=0))
    cells = lax.axis_size("real") * lax.axis_size("strike") * planes * rows * depth
    factor = 1.0 / cells**0.5
    owned = owned * factor
    return (unflat(act)[None], grad_input[None], owned[:, :taps_in], owned[:, taps_in])


def solution(mesh):
    in_specs = (
        P("real", None, "strike", None, None),
        P("real", None, "strike", None, None),
        P("real", None),
        P("real"),
    )
    out_specs = (
        P("real", None, "strike", None, None),
        P("real", None, "strike", None, None),
        P("real", None),
        P("real"),
    )
    return jax.shard_map(local, mesh=mesh, in_specs=in_specs, out_specs=out_specs, check_vma=False)
```

```python
import functools

import jax
import jax.numpy as jnp
import numpy as np
from jax import lax
from jax.experimental import pallas as pl
from jax.experimental.pallas import tpu as pltpu
from jax.sharding import PartitionSpec as P

OFFSETS = [(b, c) for b in (-1, 0, 1) for c in (-1, 0, 1)]


def plane_masks(rows, depth):
    y = np.arange(rows)[:, None]
    z = np.arange(depth)[None, :]
    masks = [((y + b >= 0) & (y + b < rows) & (z + c >= 0) & (z + c < depth)) for b, c in OFFSETS]
    return np.stack(masks).reshape(len(OFFSETS), 1, rows * depth).astype(np.float32)


def _stacked(haloed, h):
    return jnp.concatenate([haloed[h], haloed[h + 1], haloed[h + 2]], axis=0)


def _stacked_parts(lo, mid, hi, h, planes):
    def plane(index):
        if index == 0:
            return lo[0]
        if index == planes + 1:
            return hi[0]
        return mid[index - 1]
    return jnp.concatenate([plane(h), plane(h + 1), plane(h + 2)], axis=0)


def _shifted_sum(y, mask, chans, lanes, depth, sign):
    total = None
    for k, (b, c) in enumerate(OFFSETS):
        off = sign * (b * depth + c)
        block = y[k * chans : (k + 1) * chans]
        if off != 0:
            block = pltpu.roll(block, (-off) % lanes, 1)
            block = jnp.where(mask[k if sign > 0 else len(OFFSETS) - 1 - k] > 0.5, block, 0.0)
        total = block if total is None else total + block
    return total


def _forward_kernel(haloed, wall, bias, cot, mask, act_out, dpre_out, first_out, last_out, *, planes, depth):
    chans, lanes = haloed.shape[1], haloed.shape[2]
    for p in range(planes):
        y = jnp.dot(wall[...], _stacked(haloed, p), preferred_element_type=jnp.float32)
        pre = _shifted_sum(y, mask, chans, lanes, depth, 1) + bias[...]
        sig = 1.0 / (1.0 + jnp.exp(-pre))
        act_out[p] = (pre * sig).astype(act_out.dtype)
        dpre = (cot[p].astype(jnp.float32) * sig * (1.0 + pre * (1.0 - sig))).astype(dpre_out.dtype)
        dpre_out[p] = dpre
        if p == 0:
            first_out[0] = dpre
        if p == planes - 1:
            last_out[0] = dpre


def _input_kernel(lo, mid, hi, wall, mask, out, *, planes, first, depth):
    chans, lanes = mid.shape[1], mid.shape[2]
    for n in range(out.shape[0]):
        y = jnp.dot(wall[...], _stacked_parts(lo, mid, hi, first + n, planes), preferred_element_type=jnp.float32)
        out[n] = _shifted_sum(y, mask, chans, lanes, depth, -1).astype(out.dtype)


def _weight_kernel(upper, haloed, dpre, mask, keep_out, send_out, full, *, planes, depth):
    chans, lanes = dpre.shape[1], dpre.shape[2]
    gw = jnp.zeros((9 * chans, 3 * chans), jnp.float32)
    gb = jnp.zeros((chans, 1), jnp.float32)
    for p in range(planes):
        d = dpre[p].astype(jnp.float32)
        gb = gb + jnp.sum(d, axis=1, keepdims=True)
        parts = []
        for k, (b, c) in enumerate(OFFSETS):
            off = b * depth + c
            e = d
            if off != 0:
                e = pltpu.roll(jnp.where(mask[k] > 0.5, d, 0.0), off % lanes, 1)
            parts.append(e.astype(jnp.bfloat16))
        gw = gw + lax.dot_general(
            jnp.concatenate(parts, axis=0), _stacked(haloed, p),
            (((1,), (1,)), ((), ())), preferred_element_type=jnp.float32,
        )
    chans_in = gw.shape[1] // 3
    for k in range(len(OFFSETS)):
        for a in range(3):
            t = 9 * a + k
            full[:, t * chans_in : (t + 1) * chans_in] = gw[k * chans : (k + 1) * chans, a * chans_in : (a + 1) * chans_in]
    full[:, 27 * chans_in :] = gb
    half = keep_out.shape[0]
    kept = upper[0]
    keep_out[...] = full[pl.ds(pl.multiple_of(kept * half, 8), half), :]
    send_out[...] = full[pl.ds(pl.multiple_of((1 - kept) * half, 8), half), :]


def _vmem(n):
    return [pl.BlockSpec(memory_space=pltpu.VMEM)] * n


def forward_call(haloed, wall, bias, cot, mask, depth):
    planes, chans, lanes = cot.shape
    shape = jax.ShapeDtypeStruct(cot.shape, jnp.bfloat16)
    edge = jax.ShapeDtypeStruct((1, chans, lanes), jnp.bfloat16)
    flops = 2 * planes * wall.shape[0] * wall.shape[1] * lanes
    return pl.pallas_call(
        functools.partial(_forward_kernel, planes=planes, depth=depth),
        out_shape=(shape, shape, edge, edge),
        in_specs=_vmem(5),
        out_specs=tuple(_vmem(4)),
        cost_estimate=pl.CostEstimate(flops=flops, transcendentals=planes * chans * lanes, bytes_accessed=5 * cot.size * 2),
    )(haloed, wall, bias, cot, mask)


def input_call(lo, mid, hi, wall, mask, depth, first, count):
    planes, chans, lanes = mid.shape
    flops = 2 * count * wall.shape[0] * wall.shape[1] * lanes
    return pl.pallas_call(
        functools.partial(_input_kernel, planes=planes, first=first, depth=depth),
        out_shape=jax.ShapeDtypeStruct((count, chans, lanes), jnp.bfloat16),
        in_specs=_vmem(5),
        out_specs=_vmem(1)[0],
        cost_estimate=pl.CostEstimate(flops=flops, transcendentals=0, bytes_accessed=3 * mid.size * 2),
    )(lo, mid, hi, wall, mask)


def weight_call(upper, haloed, dpre, mask, depth):
    planes, chans, lanes = dpre.shape
    flops = 2 * planes * 9 * chans * 3 * chans * lanes
    half = jax.ShapeDtypeStruct((chans // 2, 27 * chans + 1), jnp.float32)
    return pl.pallas_call(
        functools.partial(_weight_kernel, planes=planes, depth=depth),
        out_shape=(half, half),
        in_specs=[pl.BlockSpec(memory_space=pltpu.SMEM)] + _vmem(3),
        out_specs=tuple(_vmem(2)),
        scratch_shapes=[pltpu.VMEM((chans, 27 * chans + 1), jnp.float32)],
        cost_estimate=pl.CostEstimate(flops=flops, transcendentals=0, bytes_accessed=3 * dpre.size * 2),
    )(upper, haloed, dpre, mask)


def neighbours(first, last, axis):
    peers = lax.axis_size(axis)
    up = [(i, i + 1) for i in range(peers - 1)]
    down = [(j, i) for i, j in up]
    return lax.ppermute(last, axis, up), lax.ppermute(first, axis, down)


def swap(value, axis, bit):
    peers = lax.axis_size(axis)
    return lax.ppermute(value, axis, [(i, i ^ bit) for i in range(peers)])


def gather_rows(value, axis):
    peers = lax.axis_size(axis)
    me = lax.axis_index(axis)
    blocks = jnp.zeros((peers,) + value.shape, value.dtype)
    blocks = lax.dynamic_update_index_in_dim(blocks, value, me, 0)
    for k in range(1, peers):
        blocks = lax.dynamic_update_index_in_dim(blocks, swap(value, axis, k), me ^ k, 0)
    return blocks.reshape((peers * value.shape[0],) + value.shape[1:])


def first_upper():
    return (lax.axis_index("real") // (lax.axis_size("real") // 2)) % 2


def reduce_beside(local_grads, work):
    rounds = []
    bit = lax.axis_size("real") // 2
    while bit >= 1:
        rounds.append(("real", bit))
        bit //= 2
    bit = 1
    while bit < lax.axis_size("strike"):
        rounds.append(("strike", bit))
        bit *= 2
    results = []
    value = None
    for k, (axis, bit) in enumerate(rounds):
        if k == 0:
            keep, send = local_grads
        elif axis == "real":
            half = value.shape[0] // 2
            upper = (lax.axis_index(axis) // bit) % 2
            keep = lax.dynamic_slice_in_dim(value, upper * half, half, 0)
            send = lax.dynamic_slice_in_dim(value, (1 - upper) * half, half, 0)
        else:
            keep, send = value, value
        if k < len(work):
            send, inputs = lax.optimization_barrier((send, work[k][1]))
            received = swap(send, axis, bit)
            result = work[k][0](*inputs)
            received, result = lax.optimization_barrier((received, result))
            results.append(result)
        else:
            received = swap(send, axis, bit)
        value = keep + received
    for job, inputs in work[len(rounds) :]:
        results.append(job(*inputs))
    return value, results


def local(grades, cotangent, weight, bias):
    field = grades[0]
    chans, planes, rows, depth = field.shape
    lanes = rows * depth
    taps_in = weight.shape[1]
    packed = jnp.concatenate([weight, bias[:, None]], axis=1)
    whole = gather_rows(packed, "real")
    whole_weight, whole_bias = whole[:, :taps_in], whole[:, taps_in]
    out_chan = whole_weight.shape[0]
    w5 = whole_weight.reshape(out_chan, 3, 3, 3, chans)
    forward_w = w5.transpose(2, 3, 0, 1, 4).reshape(9 * out_chan, 3 * chans)
    backward_w = w5[:, ::-1].transpose(2, 3, 4, 1, 0).reshape(9 * chans, 3 * out_chan)
    mask = jnp.asarray(plane_masks(rows, depth))

    def flat(value):
        return value.transpose(1, 0, 2, 3).reshape(planes, value.shape[0], lanes)

    def unflat(value):
        return value.reshape(planes, value.shape[1], rows, depth).transpose(1, 0, 2, 3)

    below, above = neighbours(field[:, :1], field[:, planes - 1 :], "strike")
    haloed = jnp.concatenate([below, field, above], axis=1)
    haloed = haloed.transpose(1, 0, 2, 3).reshape(planes + 2, chans, lanes)
    act, dpre, first, last = forward_call(
        haloed, forward_w, whole_bias.astype(jnp.float32)[:, None], flat(cotangent[0]), mask, depth
    )
    dlo, dhi = neighbours(first, last, "strike")
    local_grads = weight_call(first_upper().astype(jnp.int32)[None], haloed, dpre, mask, depth)
    work = [
        (functools.partial(input_call, depth=depth, first=p, count=1), (dlo, dpre, dhi, backward_w, mask))
        for p in range(planes)
    ]
    owned, pieces = reduce_beside(local_grads, work)
    grad_input = unflat(jnp.concatenate(pieces, axis=0))
    cells = lax.axis_size("real") * lax.axis_size("strike") * planes * rows * depth
    factor = 1.0 / cells**0.5
    owned = owned * factor
    return (unflat(act)[None], grad_input[None], owned[:, :taps_in], owned[:, taps_in])


def solution(mesh):
    in_specs = (
        P("real", None, "strike", None, None),
        P("real", None, "strike", None, None),
        P("real", None),
        P("real"),
    )
    out_specs = (
        P("real", None, "strike", None, None),
        P("real", None, "strike", None, None),
        P("real", None),
        P("real"),
    )
    return jax.shard_map(local, mesh=mesh, in_specs=in_specs, out_specs=out_specs, check_vma=False)
```

```python
import functools

import jax
import jax.numpy as jnp
import numpy as np
from jax import lax
from jax.experimental import pallas as pl
from jax.experimental.pallas import tpu as pltpu
from jax.sharding import PartitionSpec as P

OFFSETS = [(b, c) for b in (-1, 0, 1) for c in (-1, 0, 1)]


def plane_masks(rows, depth):
    y = np.arange(rows)[:, None]
    z = np.arange(depth)[None, :]
    masks = [((y + b >= 0) & (y + b < rows) & (z + c >= 0) & (z + c < depth)) for b, c in OFFSETS]
    return np.stack(masks).reshape(len(OFFSETS), 1, rows * depth).astype(np.float32)


def _stacked(haloed, h):
    return jnp.concatenate([haloed[h], haloed[h + 1], haloed[h + 2]], axis=0)


def _stacked_parts(lo, mid, hi, h, planes):
    def plane(index):
        if index == 0:
            return lo[0]
        if index == planes + 1:
            return hi[0]
        return mid[index - 1]
    return jnp.concatenate([plane(h), plane(h + 1), plane(h + 2)], axis=0)


def _shifted_sum(y, mask, chans, lanes, depth, sign):
    total = None
    for k, (b, c) in enumerate(OFFSETS):
        off = sign * (b * depth + c)
        block = y[k * chans : (k + 1) * chans]
        if off != 0:
            block = pltpu.roll(block, (-off) % lanes, 1)
            block = jnp.where(mask[k if sign > 0 else len(OFFSETS) - 1 - k] > 0.5, block, 0.0)
        total = block if total is None else total + block
    return total


def _forward_kernel(haloed, wall, bias, cot, mask, act_out, dpre_out, first_out, last_out, *, planes, depth):
    chans, lanes = haloed.shape[1], haloed.shape[2]
    for p in range(planes):
        y = jnp.dot(wall[...], _stacked(haloed, p), preferred_element_type=jnp.float32)
        pre = _shifted_sum(y, mask, chans, lanes, depth, 1) + bias[...]
        sig = 1.0 / (1.0 + jnp.exp(-pre))
        act_out[p] = (pre * sig).astype(act_out.dtype)
        dpre = (cot[p].astype(jnp.float32) * sig * (1.0 + pre * (1.0 - sig))).astype(dpre_out.dtype)
        dpre_out[p] = dpre
        if p == 0:
            first_out[0] = dpre
        if p == planes - 1:
            last_out[0] = dpre


def _input_kernel(lo, mid, hi, wall, mask, out, *, planes, first, depth):
    chans, lanes = mid.shape[1], mid.shape[2]
    for n in range(out.shape[0]):
        y = jnp.dot(wall[...], _stacked_parts(lo, mid, hi, first + n, planes), preferred_element_type=jnp.float32)
        out[n] = _shifted_sum(y, mask, chans, lanes, depth, -1).astype(out.dtype)


def _weight_kernel(upper, haloed, dpre, mask, keep_out, send_out, full, *, planes, depth):
    chans, lanes = dpre.shape[1], dpre.shape[2]
    gw = jnp.zeros((9 * chans, 3 * chans), jnp.float32)
    gb = jnp.zeros((chans, 1), jnp.float32)
    for p in range(planes):
        d = dpre[p].astype(jnp.float32)
        gb = gb + jnp.sum(d, axis=1, keepdims=True)
        parts = []
        for k, (b, c) in enumerate(OFFSETS):
            off = b * depth + c
            e = d
            if off != 0:
                e = pltpu.roll(jnp.where(mask[k] > 0.5, d, 0.0), off % lanes, 1)
            parts.append(e.astype(jnp.bfloat16))
        gw = gw + lax.dot_general(
            jnp.concatenate(parts, axis=0), _stacked(haloed, p),
            (((1,), (1,)), ((), ())), preferred_element_type=jnp.float32,
        )
    chans_in = gw.shape[1] // 3
    for k in range(len(OFFSETS)):
        for a in range(3):
            t = 9 * a + k
            full[:, t * chans_in : (t + 1) * chans_in] = gw[k * chans : (k + 1) * chans, a * chans_in : (a + 1) * chans_in]
    full[:, 27 * chans_in :] = gb
    half = keep_out.shape[0]
    kept = upper[0]
    keep_out[...] = full[pl.ds(pl.multiple_of(kept * half, 8), half), :]
    send_out[...] = full[pl.ds(pl.multiple_of((1 - kept) * half, 8), half), :]


def _vmem(n):
    return [pl.BlockSpec(memory_space=pltpu.VMEM)] * n


def forward_call(haloed, wall, bias, cot, mask, depth):
    planes, chans, lanes = cot.shape
    shape = jax.ShapeDtypeStruct(cot.shape, jnp.bfloat16)
    edge = jax.ShapeDtypeStruct((1, chans, lanes), jnp.bfloat16)
    flops = 2 * planes * wall.shape[0] * wall.shape[1] * lanes
    return pl.pallas_call(
        functools.partial(_forward_kernel, planes=planes, depth=depth),
        out_shape=(shape, shape, edge, edge),
        in_specs=_vmem(5),
        out_specs=tuple(_vmem(4)),
        cost_estimate=pl.CostEstimate(flops=flops, transcendentals=planes * chans * lanes, bytes_accessed=5 * cot.size * 2),
    )(haloed, wall, bias, cot, mask)


def input_call(lo, mid, hi, wall, mask, depth, first, count):
    planes, chans, lanes = mid.shape
    flops = 2 * count * wall.shape[0] * wall.shape[1] * lanes
    return pl.pallas_call(
        functools.partial(_input_kernel, planes=planes, first=first, depth=depth),
        out_shape=jax.ShapeDtypeStruct((count, chans, lanes), jnp.bfloat16),
        in_specs=_vmem(5),
        out_specs=_vmem(1)[0],
        cost_estimate=pl.CostEstimate(flops=flops, transcendentals=0, bytes_accessed=3 * mid.size * 2),
    )(lo, mid, hi, wall, mask)


def weight_call(upper, haloed, dpre, mask, depth):
    planes, chans, lanes = dpre.shape
    flops = 2 * planes * 9 * chans * 3 * chans * lanes
    half = jax.ShapeDtypeStruct((chans // 2, 27 * chans + 1), jnp.float32)
    return pl.pallas_call(
        functools.partial(_weight_kernel, planes=planes, depth=depth),
        out_shape=(half, half),
        in_specs=[pl.BlockSpec(memory_space=pltpu.SMEM)] + _vmem(3),
        out_specs=tuple(_vmem(2)),
        scratch_shapes=[pltpu.VMEM((chans, 27 * chans + 1), jnp.float32)],
        cost_estimate=pl.CostEstimate(flops=flops, transcendentals=0, bytes_accessed=3 * dpre.size * 2),
    )(upper, haloed, dpre, mask)


def neighbours(first, last, axis):
    peers = lax.axis_size(axis)
    up = [(i, i + 1) for i in range(peers - 1)]
    down = [(j, i) for i, j in up]
    return lax.ppermute(last, axis, up), lax.ppermute(first, axis, down)


def swap(value, axis, bit):
    peers = lax.axis_size(axis)
    return lax.ppermute(value, axis, [(i, i ^ bit) for i in range(peers)])


def gather_rows(value, axis):
    peers = lax.axis_size(axis)
    me = lax.axis_index(axis)
    blocks = jnp.zeros((peers,) + value.shape, value.dtype)
    blocks = lax.dynamic_update_index_in_dim(blocks, value, me, 0)
    for k in range(1, peers):
        blocks = lax.dynamic_update_index_in_dim(blocks, swap(value, axis, k), me ^ k, 0)
    return blocks.reshape((peers * value.shape[0],) + value.shape[1:])


def first_upper():
    return (lax.axis_index("real") // (lax.axis_size("real") // 2)) % 2


def reduce_beside(local_grads, work):
    rounds = []
    bit = lax.axis_size("real") // 2
    while bit >= 1:
        rounds.append(("real", bit))
        bit //= 2
    bit = 1
    while bit < lax.axis_size("strike"):
        rounds.append(("strike", bit))
        bit *= 2
    results = []
    value = None
    for k, (axis, bit) in enumerate(rounds):
        if k == 0:
            keep, send = local_grads
        elif axis == "real":
            half = value.shape[0] // 2
            upper = (lax.axis_index(axis) // bit) % 2
            keep = lax.dynamic_slice_in_dim(value, upper * half, half, 0)
            send = lax.dynamic_slice_in_dim(value, (1 - upper) * half, half, 0)
        else:
            keep, send = value, value
        if k < len(work):
            send, inputs = lax.optimization_barrier((send, work[k][1]))
            received = swap(send, axis, bit)
            result = work[k][0](*inputs)
            received, result = lax.optimization_barrier((received, result))
            results.append(result)
        else:
            received = swap(send, axis, bit)
        value = keep + received
    for job, inputs in work[len(rounds) :]:
        results.append(job(*inputs))
    return value, results


def local(grades, cotangent, weight, bias):
    field = grades[0]
    chans, planes, rows, depth = field.shape
    lanes = rows * depth
    taps_in = weight.shape[1]
    packed = jnp.concatenate([weight, bias[:, None]], axis=1)
    whole = gather_rows(packed, "real")
    whole_weight, whole_bias = whole[:, :taps_in], whole[:, taps_in]
    out_chan = whole_weight.shape[0]
    w5 = whole_weight.reshape(out_chan, 3, 3, 3, chans)
    forward_w = w5.transpose(2, 3, 0, 1, 4).reshape(9 * out_chan, 3 * chans)
    backward_w = w5[:, ::-1].transpose(2, 3, 4, 1, 0).reshape(9 * chans, 3 * out_chan)
    mask = jnp.asarray(plane_masks(rows, depth))

    def flat(value):
        return value.transpose(1, 0, 2, 3).reshape(planes, value.shape[0], lanes)

    def unflat(value):
        return value.reshape(planes, value.shape[1], rows, depth).transpose(1, 0, 2, 3)

    below, above = neighbours(field[:, :1], field[:, planes - 1 :], "strike")
    haloed = jnp.concatenate([below, field, above], axis=1)
    haloed = haloed.transpose(1, 0, 2, 3).reshape(planes + 2, chans, lanes)
    haloed, backward_w = lax.optimization_barrier((haloed, backward_w))
    act, dpre, first, last = forward_call(
        haloed, forward_w, whole_bias.astype(jnp.float32)[:, None], flat(cotangent[0]), mask, depth
    )
    dlo, dhi = neighbours(first, last, "strike")
    local_grads = weight_call(first_upper().astype(jnp.int32)[None], haloed, dpre, mask, depth)
    work = [
        (functools.partial(input_call, depth=depth, first=p, count=1), (dlo, dpre, dhi, backward_w, mask))
        for p in range(planes)
    ]
    owned, pieces = reduce_beside(local_grads, work)
    grad_input = unflat(jnp.concatenate(pieces, axis=0))
    cells = lax.axis_size("real") * lax.axis_size("strike") * planes * rows * depth
    factor = 1.0 / cells**0.5
    owned = owned * factor
    return (unflat(act)[None], grad_input[None], owned[:, :taps_in], owned[:, taps_in])


def solution(mesh):
    in_specs = (
        P("real", None, "strike", None, None),
        P("real", None, "strike", None, None),
        P("real", None),
        P("real"),
    )
    out_specs = (
        P("real", None, "strike", None, None),
        P("real", None, "strike", None, None),
        P("real", None),
        P("real"),
    )
    return jax.shard_map(local, mesh=mesh, in_specs=in_specs, out_specs=out_specs, check_vma=False)
```

```python
import functools

import jax
import jax.numpy as jnp
import numpy as np
from jax import lax
from jax.experimental import pallas as pl
from jax.experimental.pallas import tpu as pltpu
from jax.sharding import PartitionSpec as P

OFFSETS = [(b, c) for b in (-1, 0, 1) for c in (-1, 0, 1)]


def plane_masks(rows, depth):
    y = np.arange(rows)[:, None]
    z = np.arange(depth)[None, :]
    masks = [((y + b >= 0) & (y + b < rows) & (z + c >= 0) & (z + c < depth)) for b, c in OFFSETS]
    return np.stack(masks).reshape(len(OFFSETS), 1, rows * depth).astype(np.float32)


def _stacked(haloed, h):
    return jnp.concatenate([haloed[h], haloed[h + 1], haloed[h + 2]], axis=0)


def _stacked_parts(lo, mid, hi, h, planes):
    def plane(index):
        if index == 0:
            return lo[0]
        if index == planes + 1:
            return hi[0]
        return mid[index - 1]
    return jnp.concatenate([plane(h), plane(h + 1), plane(h + 2)], axis=0)


def _shifted_sum(y, mask, chans, lanes, depth, sign):
    total = None
    for k, (b, c) in enumerate(OFFSETS):
        off = sign * (b * depth + c)
        block = y[k * chans : (k + 1) * chans]
        if off != 0:
            block = pltpu.roll(block, (-off) % lanes, 1)
            block = jnp.where(mask[k if sign > 0 else len(OFFSETS) - 1 - k] > 0.5, block, 0.0)
        total = block if total is None else total + block
    return total


def _forward_kernel(haloed, wall, bias, cot, mask, act_out, dpre_out, first_out, last_out, *, planes, depth):
    chans, lanes = haloed.shape[1], haloed.shape[2]
    for p in range(planes):
        y = jnp.dot(wall[...], _stacked(haloed, p), preferred_element_type=jnp.float32)
        pre = _shifted_sum(y, mask, chans, lanes, depth, 1) + bias[...]
        sig = 1.0 / (1.0 + jnp.exp(-pre))
        act_out[p] = (pre * sig).astype(act_out.dtype)
        dpre = (cot[p].astype(jnp.float32) * sig * (1.0 + pre * (1.0 - sig))).astype(dpre_out.dtype)
        dpre_out[p] = dpre
        if p == 0:
            first_out[0] = dpre
        if p == planes - 1:
            last_out[0] = dpre


def _input_kernel(lo, mid, hi, wall, mask, out, *, planes, first, depth):
    chans, lanes = mid.shape[1], mid.shape[2]
    for n in range(out.shape[0]):
        y = jnp.dot(wall[...], _stacked_parts(lo, mid, hi, first + n, planes), preferred_element_type=jnp.float32)
        out[n] = _shifted_sum(y, mask, chans, lanes, depth, -1).astype(out.dtype)


def _weight_kernel(upper, haloed, dpre, mask, keep_out, send_out, full, *, planes, depth):
    chans, lanes = dpre.shape[1], dpre.shape[2]
    gw = jnp.zeros((9 * chans, 3 * chans), jnp.float32)
    gb = jnp.zeros((chans, 1), jnp.float32)
    for p in range(planes):
        d = dpre[p].astype(jnp.float32)
        gb = gb + jnp.sum(d, axis=1, keepdims=True)
        parts = []
        for k, (b, c) in enumerate(OFFSETS):
            off = b * depth + c
            e = d
            if off != 0:
                e = pltpu.roll(jnp.where(mask[k] > 0.5, d, 0.0), off % lanes, 1)
            parts.append(e.astype(jnp.bfloat16))
        gw = gw + lax.dot_general(
            jnp.concatenate(parts, axis=0), _stacked(haloed, p),
            (((1,), (1,)), ((), ())), preferred_element_type=jnp.float32,
        )
    chans_in = gw.shape[1] // 3
    for k in range(len(OFFSETS)):
        for a in range(3):
            t = 9 * a + k
            full[:, t * chans_in : (t + 1) * chans_in] = gw[k * chans : (k + 1) * chans, a * chans_in : (a + 1) * chans_in]
    full[:, 27 * chans_in :] = gb
    half = keep_out.shape[0]
    kept = upper[0]
    keep_out[...] = full[pl.ds(pl.multiple_of(kept * half, 8), half), :]
    send_out[...] = full[pl.ds(pl.multiple_of((1 - kept) * half, 8), half), :]


def _vmem(n):
    return [pl.BlockSpec(memory_space=pltpu.VMEM)] * n


def forward_call(haloed, wall, bias, cot, mask, depth):
    planes, chans, lanes = cot.shape
    shape = jax.ShapeDtypeStruct(cot.shape, jnp.bfloat16)
    edge = jax.ShapeDtypeStruct((1, chans, lanes), jnp.bfloat16)
    flops = 2 * planes * wall.shape[0] * wall.shape[1] * lanes
    return pl.pallas_call(
        functools.partial(_forward_kernel, planes=planes, depth=depth),
        out_shape=(shape, shape, edge, edge),
        in_specs=_vmem(5),
        out_specs=tuple(_vmem(4)),
        cost_estimate=pl.CostEstimate(flops=flops, transcendentals=planes * chans * lanes, bytes_accessed=5 * cot.size * 2),
    )(haloed, wall, bias, cot, mask)


def input_call(lo, mid, hi, wall, mask, depth, first, count):
    planes, chans, lanes = mid.shape
    flops = 2 * count * wall.shape[0] * wall.shape[1] * lanes
    return pl.pallas_call(
        functools.partial(_input_kernel, planes=planes, first=first, depth=depth),
        out_shape=jax.ShapeDtypeStruct((count, chans, lanes), jnp.bfloat16),
        in_specs=_vmem(5),
        out_specs=_vmem(1)[0],
        cost_estimate=pl.CostEstimate(flops=flops, transcendentals=0, bytes_accessed=3 * mid.size * 2),
    )(lo, mid, hi, wall, mask)


def weight_call(upper, haloed, dpre, mask, depth):
    planes, chans, lanes = dpre.shape
    flops = 2 * planes * 9 * chans * 3 * chans * lanes
    half = jax.ShapeDtypeStruct((chans // 2, 27 * chans + 1), jnp.float32)
    return pl.pallas_call(
        functools.partial(_weight_kernel, planes=planes, depth=depth),
        out_shape=(half, half),
        in_specs=[pl.BlockSpec(memory_space=pltpu.SMEM)] + _vmem(3),
        out_specs=tuple(_vmem(2)),
        scratch_shapes=[pltpu.VMEM((chans, 27 * chans + 1), jnp.float32)],
        cost_estimate=pl.CostEstimate(flops=flops, transcendentals=0, bytes_accessed=3 * dpre.size * 2),
    )(upper, haloed, dpre, mask)


def neighbours(first, last, axis):
    peers = lax.axis_size(axis)
    up = [(i, i + 1) for i in range(peers - 1)]
    down = [(j, i) for i, j in up]
    return lax.ppermute(last, axis, up), lax.ppermute(first, axis, down)


def swap(value, axis, bit):
    peers = lax.axis_size(axis)
    return lax.ppermute(value, axis, [(i, i ^ bit) for i in range(peers)])


def gather_rows(value, axis):
    peers = lax.axis_size(axis)
    me = lax.axis_index(axis)
    blocks = jnp.zeros((peers,) + value.shape, value.dtype)
    blocks = lax.dynamic_update_index_in_dim(blocks, value, me, 0)
    for k in range(1, peers):
        blocks = lax.dynamic_update_index_in_dim(blocks, swap(value, axis, k), me ^ k, 0)
    return blocks.reshape((peers * value.shape[0],) + value.shape[1:])


def first_upper():
    return (lax.axis_index("real") // (lax.axis_size("real") // 2)) % 2


def reduce_beside(local_grads, work):
    rounds = []
    bit = lax.axis_size("real") // 2
    while bit >= 1:
        rounds.append(("real", bit))
        bit //= 2
    bit = 1
    while bit < lax.axis_size("strike"):
        rounds.append(("strike", bit))
        bit *= 2
    results = []
    value = None
    for k, (axis, bit) in enumerate(rounds):
        if k == 0:
            keep, send = local_grads
        elif axis == "real":
            half = value.shape[0] // 2
            upper = (lax.axis_index(axis) // bit) % 2
            keep = lax.dynamic_slice_in_dim(value, upper * half, half, 0)
            send = lax.dynamic_slice_in_dim(value, (1 - upper) * half, half, 0)
        else:
            keep, send = value, value
        if k < len(work):
            send, inputs = lax.optimization_barrier((send, work[k][1]))
            received = swap(send, axis, bit)
            result = work[k][0](*inputs)
            received, result = lax.optimization_barrier((received, result))
            results.append(result)
        else:
            received = swap(send, axis, bit)
        value = keep + received
    for job, inputs in work[len(rounds) :]:
        results.append(job(*inputs))
    return value, results


def local(grades, cotangent, weight, bias):
    field = grades[0]
    chans, planes, rows, depth = field.shape
    lanes = rows * depth
    taps_in = weight.shape[1]
    packed = jnp.concatenate([weight, bias[:, None]], axis=1)
    edges = (field[:, :1], field[:, planes - 1 :])
    below, above = neighbours(*edges, "strike")
    packed, below = lax.optimization_barrier((packed, below))
    whole = gather_rows(packed, "real")
    whole_weight, whole_bias = whole[:, :taps_in], whole[:, taps_in]
    out_chan = whole_weight.shape[0]
    w5 = whole_weight.reshape(out_chan, 3, 3, 3, chans)
    forward_w = w5.transpose(2, 3, 0, 1, 4).reshape(9 * out_chan, 3 * chans)
    backward_w = w5[:, ::-1].transpose(2, 3, 4, 1, 0).reshape(9 * chans, 3 * out_chan)
    mask = jnp.asarray(plane_masks(rows, depth))

    def flat(value):
        return value.transpose(1, 0, 2, 3).reshape(planes, value.shape[0], lanes)

    def unflat(value):
        return value.reshape(planes, value.shape[1], rows, depth).transpose(1, 0, 2, 3)

    haloed = jnp.concatenate([below, field, above], axis=1)
    haloed = haloed.transpose(1, 0, 2, 3).reshape(planes + 2, chans, lanes)
    haloed, backward_w = lax.optimization_barrier((haloed, backward_w))
    act, dpre, first, last = forward_call(
        haloed, forward_w, whole_bias.astype(jnp.float32)[:, None], flat(cotangent[0]), mask, depth
    )
    dlo, dhi = neighbours(first, last, "strike")
    local_grads = weight_call(first_upper().astype(jnp.int32)[None], haloed, dpre, mask, depth)
    work = [
        (functools.partial(input_call, depth=depth, first=p, count=1), (dlo, dpre, dhi, backward_w, mask))
        for p in range(planes)
    ]
    owned, pieces = reduce_beside(local_grads, work)
    grad_input = unflat(jnp.concatenate(pieces, axis=0))
    cells = lax.axis_size("real") * lax.axis_size("strike") * planes * rows * depth
    factor = 1.0 / cells**0.5
    owned = owned * factor
    return (unflat(act)[None], grad_input[None], owned[:, :taps_in], owned[:, taps_in])


def solution(mesh):
    in_specs = (
        P("real", None, "strike", None, None),
        P("real", None, "strike", None, None),
        P("real", None),
        P("real"),
    )
    out_specs = (
        P("real", None, "strike", None, None),
        P("real", None, "strike", None, None),
        P("real", None),
        P("real"),
    )
    return jax.shard_map(local, mesh=mesh, in_specs=in_specs, out_specs=out_specs, check_vma=False)
```

```python
import functools

import jax
import jax.numpy as jnp
import numpy as np
from jax import lax
from jax.experimental import pallas as pl
from jax.experimental.pallas import tpu as pltpu
from jax.sharding import PartitionSpec as P

OFFSETS = [(b, c) for b in (-1, 0, 1) for c in (-1, 0, 1)]


def plane_masks(rows, depth):
    y = np.arange(rows)[:, None]
    z = np.arange(depth)[None, :]
    masks = [((y + b >= 0) & (y + b < rows) & (z + c >= 0) & (z + c < depth)) for b, c in OFFSETS]
    return np.stack(masks).reshape(len(OFFSETS), 1, rows * depth).astype(np.float32)


def _stacked(haloed, h):
    return jnp.concatenate([haloed[h], haloed[h + 1], haloed[h + 2]], axis=0)


def _stacked_parts(lo, mid, hi, h, planes):
    def plane(index):
        if index == 0:
            return lo[0]
        if index == planes + 1:
            return hi[0]
        return mid[index - 1]
    return jnp.concatenate([plane(h), plane(h + 1), plane(h + 2)], axis=0)


def _shifted_sum(y, mask, chans, lanes, depth, sign):
    total = None
    for k, (b, c) in enumerate(OFFSETS):
        off = sign * (b * depth + c)
        block = y[k * chans : (k + 1) * chans]
        if off != 0:
            block = pltpu.roll(block, (-off) % lanes, 1)
            block = jnp.where(mask[k if sign > 0 else len(OFFSETS) - 1 - k] > 0.5, block, 0.0)
        total = block if total is None else total + block
    return total


def _forward_kernel(haloed, wall, bias, cot, mask, act_out, dpre_out, first_out, last_out, *, planes, depth):
    chans, lanes = haloed.shape[1], haloed.shape[2]
    for p in range(planes):
        y = jnp.dot(wall[...], _stacked(haloed, p), preferred_element_type=jnp.float32)
        pre = _shifted_sum(y, mask, chans, lanes, depth, 1) + bias[...]
        sig = 1.0 / (1.0 + jnp.exp(-pre))
        act_out[p] = (pre * sig).astype(act_out.dtype)
        dpre = (cot[p].astype(jnp.float32) * sig * (1.0 + pre * (1.0 - sig))).astype(dpre_out.dtype)
        dpre_out[p] = dpre
        if p == 0:
            first_out[0] = dpre
        if p == planes - 1:
            last_out[0] = dpre


def _input_kernel(lo, mid, hi, wall, mask, out, *, planes, first, depth):
    chans, lanes = mid.shape[1], mid.shape[2]
    for n in range(out.shape[0]):
        y = jnp.dot(wall[...], _stacked_parts(lo, mid, hi, first + n, planes), preferred_element_type=jnp.float32)
        out[n] = _shifted_sum(y, mask, chans, lanes, depth, -1).astype(out.dtype)


def _weight_kernel(upper, haloed, dpre, mask, keep_out, send_out, full, *, planes, depth):
    chans, lanes = dpre.shape[1], dpre.shape[2]
    gw = jnp.zeros((9 * chans, 3 * chans), jnp.float32)
    gb = jnp.zeros((chans, 1), jnp.float32)
    for p in range(planes):
        d = dpre[p].astype(jnp.float32)
        gb = gb + jnp.sum(d, axis=1, keepdims=True)
        parts = []
        for k, (b, c) in enumerate(OFFSETS):
            off = b * depth + c
            e = d
            if off != 0:
                e = pltpu.roll(jnp.where(mask[k] > 0.5, d, 0.0), off % lanes, 1)
            parts.append(e.astype(jnp.bfloat16))
        gw = gw + lax.dot_general(
            jnp.concatenate(parts, axis=0), _stacked(haloed, p),
            (((1,), (1,)), ((), ())), preferred_element_type=jnp.float32,
        )
    chans_in = gw.shape[1] // 3
    for k in range(len(OFFSETS)):
        for a in range(3):
            t = 9 * a + k
            full[:, t * chans_in : (t + 1) * chans_in] = gw[k * chans : (k + 1) * chans, a * chans_in : (a + 1) * chans_in]
    full[:, 27 * chans_in :] = gb
    half = keep_out.shape[0]
    kept = upper[0]
    keep_out[...] = full[pl.ds(pl.multiple_of(kept * half, 8), half), :]
    send_out[...] = full[pl.ds(pl.multiple_of((1 - kept) * half, 8), half), :]


def _vmem(n):
    return [pl.BlockSpec(memory_space=pltpu.VMEM)] * n


def forward_call(haloed, wall, bias, cot, mask, depth):
    planes, chans, lanes = cot.shape
    shape = jax.ShapeDtypeStruct(cot.shape, jnp.bfloat16)
    edge = jax.ShapeDtypeStruct((1, chans, lanes), jnp.bfloat16)
    flops = 2 * planes * wall.shape[0] * wall.shape[1] * lanes
    return pl.pallas_call(
        functools.partial(_forward_kernel, planes=planes, depth=depth),
        out_shape=(shape, shape, edge, edge),
        in_specs=_vmem(5),
        out_specs=tuple(_vmem(4)),
        cost_estimate=pl.CostEstimate(flops=flops, transcendentals=planes * chans * lanes, bytes_accessed=5 * cot.size * 2),
    )(haloed, wall, bias, cot, mask)


def input_call(lo, mid, hi, wall, mask, depth, first, count):
    planes, chans, lanes = mid.shape
    flops = 2 * count * wall.shape[0] * wall.shape[1] * lanes
    return pl.pallas_call(
        functools.partial(_input_kernel, planes=planes, first=first, depth=depth),
        out_shape=jax.ShapeDtypeStruct((count, chans, lanes), jnp.bfloat16),
        in_specs=_vmem(5),
        out_specs=_vmem(1)[0],
        cost_estimate=pl.CostEstimate(flops=flops, transcendentals=0, bytes_accessed=3 * mid.size * 2),
    )(lo, mid, hi, wall, mask)


def weight_call(upper, haloed, dpre, mask, depth):
    planes, chans, lanes = dpre.shape
    flops = 2 * planes * 9 * chans * 3 * chans * lanes
    half = jax.ShapeDtypeStruct((chans // 2, 27 * chans + 1), jnp.float32)
    return pl.pallas_call(
        functools.partial(_weight_kernel, planes=planes, depth=depth),
        out_shape=(half, half),
        in_specs=[pl.BlockSpec(memory_space=pltpu.SMEM)] + _vmem(3),
        out_specs=tuple(_vmem(2)),
        scratch_shapes=[pltpu.VMEM((chans, 27 * chans + 1), jnp.float32)],
        cost_estimate=pl.CostEstimate(flops=flops, transcendentals=0, bytes_accessed=3 * dpre.size * 2),
    )(upper, haloed, dpre, mask)


def neighbours(first, last, axis):
    peers = lax.axis_size(axis)
    up = [(i, i + 1) for i in range(peers - 1)]
    down = [(j, i) for i, j in up]
    return lax.ppermute(last, axis, up), lax.ppermute(first, axis, down)


def swap(value, axis, bit):
    peers = lax.axis_size(axis)
    return lax.ppermute(value, axis, [(i, i ^ bit) for i in range(peers)])


def gather_rows(value, axis, beside):
    peers = lax.axis_size(axis)
    me = lax.axis_index(axis)
    held = value
    bit = 1
    while bit < peers:
        got = swap(held, axis, bit)
        if bit == 1:
            got, beside = lax.optimization_barrier((got, beside))
        held = jnp.where((me // bit) % 2 == 0, jnp.concatenate([held, got]), jnp.concatenate([got, held]))
        bit *= 2
    return held, beside


def first_upper():
    return (lax.axis_index("real") // (lax.axis_size("real") // 2)) % 2


def reduce_beside(local_grads, work):
    rounds = []
    bit = lax.axis_size("real") // 2
    while bit >= 1:
        rounds.append(("real", bit))
        bit //= 2
    bit = 1
    while bit < lax.axis_size("strike"):
        rounds.append(("strike", bit))
        bit *= 2
    results = []
    value = None
    for k, (axis, bit) in enumerate(rounds):
        if k == 0:
            keep, send = local_grads
        elif axis == "real":
            half = value.shape[0] // 2
            upper = (lax.axis_index(axis) // bit) % 2
            keep = lax.dynamic_slice_in_dim(value, upper * half, half, 0)
            send = lax.dynamic_slice_in_dim(value, (1 - upper) * half, half, 0)
        else:
            keep, send = value, value
        if k < len(work):
            send, inputs = lax.optimization_barrier((send, work[k][1]))
            received = swap(send, axis, bit)
            result = work[k][0](*inputs)
            received, result = lax.optimization_barrier((received, result))
            results.append(result)
        else:
            received = swap(send, axis, bit)
        value = keep + received
    for job, inputs in work[len(rounds) :]:
        results.append(job(*inputs))
    return value, results


def local(grades, cotangent, weight, bias):
    field = grades[0]
    chans, planes, rows, depth = field.shape
    lanes = rows * depth
    taps_in = weight.shape[1]
    packed = jnp.concatenate([weight, bias[:, None]], axis=1)
    whole, edges = gather_rows(packed, "real", (field[:, :1], field[:, planes - 1 :]))
    whole_weight, whole_bias = whole[:, :taps_in], whole[:, taps_in]
    out_chan = whole_weight.shape[0]
    w5 = whole_weight.reshape(out_chan, 3, 3, 3, chans)
    forward_w = w5.transpose(2, 3, 0, 1, 4).reshape(9 * out_chan, 3 * chans)
    backward_w = w5[:, ::-1].transpose(2, 3, 4, 1, 0).reshape(9 * chans, 3 * out_chan)
    mask = jnp.asarray(plane_masks(rows, depth))

    def flat(value):
        return value.transpose(1, 0, 2, 3).reshape(planes, value.shape[0], lanes)

    def unflat(value):
        return value.reshape(planes, value.shape[1], rows, depth).transpose(1, 0, 2, 3)

    below, above = neighbours(*edges, "strike")
    haloed = jnp.concatenate([below, field, above], axis=1)
    haloed = haloed.transpose(1, 0, 2, 3).reshape(planes + 2, chans, lanes)
    act, dpre, first, last = forward_call(
        haloed, forward_w, whole_bias.astype(jnp.float32)[:, None], flat(cotangent[0]), mask, depth
    )
    dlo, dhi = neighbours(first, last, "strike")
    local_grads = weight_call(first_upper().astype(jnp.int32)[None], haloed, dpre, mask, depth)
    work = [
        (functools.partial(input_call, depth=depth, first=p, count=1), (dlo, dpre, dhi, backward_w, mask))
        for p in range(planes)
    ]
    owned, pieces = reduce_beside(local_grads, work)
    grad_input = unflat(jnp.concatenate(pieces, axis=0))
    cells = lax.axis_size("real") * lax.axis_size("strike") * planes * rows * depth
    factor = 1.0 / cells**0.5
    owned = owned * factor
    return (unflat(act)[None], grad_input[None], owned[:, :taps_in], owned[:, taps_in])


def solution(mesh):
    in_specs = (
        P("real", None, "strike", None, None),
        P("real", None, "strike", None, None),
        P("real", None),
        P("real"),
    )
    out_specs = (
        P("real", None, "strike", None, None),
        P("real", None, "strike", None, None),
        P("real", None),
        P("real"),
    )
    return jax.shard_map(local, mesh=mesh, in_specs=in_specs, out_specs=out_specs, check_vma=False)
```

```python
import functools

import jax
import jax.numpy as jnp
import numpy as np
from jax import lax
from jax.experimental import pallas as pl
from jax.experimental.pallas import tpu as pltpu
from jax.sharding import PartitionSpec as P

OFFSETS = [(b, c) for b in (-1, 0, 1) for c in (-1, 0, 1)]


def plane_masks(rows, depth):
    y = np.arange(rows)[:, None]
    z = np.arange(depth)[None, :]
    masks = [((y + b >= 0) & (y + b < rows) & (z + c >= 0) & (z + c < depth)) for b, c in OFFSETS]
    return np.stack(masks).reshape(len(OFFSETS), 1, rows * depth).astype(np.float32)


def _stacked_parts(lo, mid, hi, h, planes):
    def plane(index):
        if index == 0:
            return lo[0]
        if index == planes + 1:
            return hi[0]
        return mid[index - 1]
    return jnp.concatenate([plane(h), plane(h + 1), plane(h + 2)], axis=0)


def _shifted_sum(y, mask, chans, lanes, depth, sign):
    total = None
    for k, (b, c) in enumerate(OFFSETS):
        off = sign * (b * depth + c)
        block = y[k * chans : (k + 1) * chans]
        if off != 0:
            block = pltpu.roll(block, (-off) % lanes, 1)
            block = jnp.where(mask[k if sign > 0 else len(OFFSETS) - 1 - k] > 0.5, block, 0.0)
        total = block if total is None else total + block
    return total


def _forward_kernel(lo, mid, hi, wall, bias, cot, mask, act_out, dpre_out, first_out, last_out, *, planes, depth):
    chans, lanes = mid.shape[1], mid.shape[2]
    for p in range(planes):
        y = jnp.dot(wall[...], _stacked_parts(lo, mid, hi, p, planes), preferred_element_type=jnp.float32)
        pre = _shifted_sum(y, mask, chans, lanes, depth, 1) + bias[...]
        sig = 1.0 / (1.0 + jnp.exp(-pre))
        act_out[p] = (pre * sig).astype(act_out.dtype)
        dpre = (cot[p].astype(jnp.float32) * sig * (1.0 + pre * (1.0 - sig))).astype(dpre_out.dtype)
        dpre_out[p] = dpre
        if p == 0:
            first_out[0] = dpre
        if p == planes - 1:
            last_out[0] = dpre


def _input_kernel(lo, mid, hi, wall, mask, out, *, planes, first, depth):
    chans, lanes = mid.shape[1], mid.shape[2]
    for n in range(out.shape[0]):
        y = jnp.dot(wall[...], _stacked_parts(lo, mid, hi, first + n, planes), preferred_element_type=jnp.float32)
        out[n] = _shifted_sum(y, mask, chans, lanes, depth, -1).astype(out.dtype)


def _weight_kernel(upper, lo, mid, hi, dpre, mask, keep_out, send_out, full, *, planes, depth):
    chans, lanes = dpre.shape[1], dpre.shape[2]
    gw = jnp.zeros((9 * chans, 3 * chans), jnp.float32)
    gb = jnp.zeros((chans, 1), jnp.float32)
    for p in range(planes):
        d = dpre[p].astype(jnp.float32)
        gb = gb + jnp.sum(d, axis=1, keepdims=True)
        parts = []
        for k, (b, c) in enumerate(OFFSETS):
            off = b * depth + c
            e = d
            if off != 0:
                e = pltpu.roll(jnp.where(mask[k] > 0.5, d, 0.0), off % lanes, 1)
            parts.append(e.astype(jnp.bfloat16))
        gw = gw + lax.dot_general(
            jnp.concatenate(parts, axis=0), _stacked_parts(lo, mid, hi, p, planes),
            (((1,), (1,)), ((), ())), preferred_element_type=jnp.float32,
        )
    chans_in = gw.shape[1] // 3
    for k in range(len(OFFSETS)):
        for a in range(3):
            t = 9 * a + k
            full[:, t * chans_in : (t + 1) * chans_in] = gw[k * chans : (k + 1) * chans, a * chans_in : (a + 1) * chans_in]
    full[:, 27 * chans_in :] = gb
    half = keep_out.shape[0]
    kept = upper[0]
    keep_out[...] = full[pl.ds(pl.multiple_of(kept * half, 8), half), :]
    send_out[...] = full[pl.ds(pl.multiple_of((1 - kept) * half, 8), half), :]


def _vmem(n):
    return [pl.BlockSpec(memory_space=pltpu.VMEM)] * n


def forward_call(lo, mid, hi, wall, bias, cot, mask, depth):
    planes, chans, lanes = cot.shape
    shape = jax.ShapeDtypeStruct(cot.shape, jnp.bfloat16)
    edge = jax.ShapeDtypeStruct((1, chans, lanes), jnp.bfloat16)
    flops = 2 * planes * wall.shape[0] * wall.shape[1] * lanes
    return pl.pallas_call(
        functools.partial(_forward_kernel, planes=planes, depth=depth),
        out_shape=(shape, shape, edge, edge),
        in_specs=_vmem(7),
        out_specs=tuple(_vmem(4)),
        cost_estimate=pl.CostEstimate(flops=flops, transcendentals=planes * chans * lanes, bytes_accessed=5 * cot.size * 2),
    )(lo, mid, hi, wall, bias, cot, mask)


def input_call(lo, mid, hi, wall, mask, depth, first, count):
    planes, chans, lanes = mid.shape
    flops = 2 * count * wall.shape[0] * wall.shape[1] * lanes
    return pl.pallas_call(
        functools.partial(_input_kernel, planes=planes, first=first, depth=depth),
        out_shape=jax.ShapeDtypeStruct((count, chans, lanes), jnp.bfloat16),
        in_specs=_vmem(5),
        out_specs=_vmem(1)[0],
        cost_estimate=pl.CostEstimate(flops=flops, transcendentals=0, bytes_accessed=3 * mid.size * 2),
    )(lo, mid, hi, wall, mask)


def weight_call(upper, lo, mid, hi, dpre, mask, depth):
    planes, chans, lanes = dpre.shape
    flops = 2 * planes * 9 * chans * 3 * chans * lanes
    half = jax.ShapeDtypeStruct((chans // 2, 27 * chans + 1), jnp.float32)
    return pl.pallas_call(
        functools.partial(_weight_kernel, planes=planes, depth=depth),
        out_shape=(half, half),
        in_specs=[pl.BlockSpec(memory_space=pltpu.SMEM)] + _vmem(5),
        out_specs=tuple(_vmem(2)),
        scratch_shapes=[pltpu.VMEM((chans, 27 * chans + 1), jnp.float32)],
        cost_estimate=pl.CostEstimate(flops=flops, transcendentals=0, bytes_accessed=3 * dpre.size * 2),
    )(upper, lo, mid, hi, dpre, mask)


def neighbours(first, last, axis):
    peers = lax.axis_size(axis)
    up = [(i, i + 1) for i in range(peers - 1)]
    down = [(j, i) for i, j in up]
    return lax.ppermute(last, axis, up), lax.ppermute(first, axis, down)


def swap(value, axis, bit):
    peers = lax.axis_size(axis)
    return lax.ppermute(value, axis, [(i, i ^ bit) for i in range(peers)])


def gather_rows(value, axis):
    peers = lax.axis_size(axis)
    me = lax.axis_index(axis)
    blocks = jnp.zeros((peers,) + value.shape, value.dtype)
    blocks = lax.dynamic_update_index_in_dim(blocks, value, me, 0)
    for k in range(1, peers):
        blocks = lax.dynamic_update_index_in_dim(blocks, swap(value, axis, k), me ^ k, 0)
    return blocks.reshape((peers * value.shape[0],) + value.shape[1:])


def first_upper():
    return (lax.axis_index("real") // (lax.axis_size("real") // 2)) % 2


def reduce_beside(local_grads, work):
    rounds = []
    bit = lax.axis_size("real") // 2
    while bit >= 1:
        rounds.append(("real", bit))
        bit //= 2
    bit = 1
    while bit < lax.axis_size("strike"):
        rounds.append(("strike", bit))
        bit *= 2
    results = []
    value = None
    for k, (axis, bit) in enumerate(rounds):
        if k == 0:
            keep, send = local_grads
        elif axis == "real":
            half = value.shape[0] // 2
            upper = (lax.axis_index(axis) // bit) % 2
            keep = lax.dynamic_slice_in_dim(value, upper * half, half, 0)
            send = lax.dynamic_slice_in_dim(value, (1 - upper) * half, half, 0)
        else:
            keep, send = value, value
        if k < len(work):
            send, inputs = lax.optimization_barrier((send, work[k][1]))
            received = swap(send, axis, bit)
            result = work[k][0](*inputs)
            received, result = lax.optimization_barrier((received, result))
            results.append(result)
        else:
            received = swap(send, axis, bit)
        value = keep + received
    for job, inputs in work[len(rounds) :]:
        results.append(job(*inputs))
    return value, results


def local(grades, cotangent, weight, bias):
    field = grades[0]
    chans, planes, rows, depth = field.shape
    lanes = rows * depth
    taps_in = weight.shape[1]
    packed = jnp.concatenate([weight, bias[:, None]], axis=1)
    whole = gather_rows(packed, "real")
    whole_weight, whole_bias = whole[:, :taps_in], whole[:, taps_in]
    out_chan = whole_weight.shape[0]
    w5 = whole_weight.reshape(out_chan, 3, 3, 3, chans)
    forward_w = w5.transpose(2, 3, 0, 1, 4).reshape(9 * out_chan, 3 * chans)
    backward_w = w5[:, ::-1].transpose(2, 3, 4, 1, 0).reshape(9 * chans, 3 * out_chan)
    mask = jnp.asarray(plane_masks(rows, depth))

    def flat(value):
        return value.transpose(1, 0, 2, 3).reshape(value.shape[1], value.shape[0], lanes)

    def unflat(value):
        return value.reshape(planes, value.shape[1], rows, depth).transpose(1, 0, 2, 3)

    below, above = neighbours(field[:, :1], field[:, planes - 1 :], "strike")
    mid = flat(field)
    lo, hi = flat(below), flat(above)
    act, dpre, first, last = forward_call(
        lo, mid, hi, forward_w, whole_bias.astype(jnp.float32)[:, None], flat(cotangent[0]), mask, depth
    )
    dlo, dhi = neighbours(first, last, "strike")
    local_grads = weight_call(first_upper().astype(jnp.int32)[None], lo, mid, hi, dpre, mask, depth)
    work = [
        (functools.partial(input_call, depth=depth, first=p, count=1), (dlo, dpre, dhi, backward_w, mask))
        for p in range(planes)
    ]
    owned, pieces = reduce_beside(local_grads, work)
    grad_input = unflat(jnp.concatenate(pieces, axis=0))
    cells = lax.axis_size("real") * lax.axis_size("strike") * planes * rows * depth
    factor = 1.0 / cells**0.5
    owned = owned * factor
    return (unflat(act)[None], grad_input[None], owned[:, :taps_in], owned[:, taps_in])


def solution(mesh):
    in_specs = (
        P("real", None, "strike", None, None),
        P("real", None, "strike", None, None),
        P("real", None),
        P("real"),
    )
    out_specs = (
        P("real", None, "strike", None, None),
        P("real", None, "strike", None, None),
        P("real", None),
        P("real"),
    )
    return jax.shard_map(local, mesh=mesh, in_specs=in_specs, out_specs=out_specs, check_vma=False)
```

```python
import functools

import jax
import jax.numpy as jnp
import numpy as np
from jax import lax
from jax.experimental import pallas as pl
from jax.experimental.pallas import tpu as pltpu
from jax.sharding import PartitionSpec as P

OFFSETS = [(b, c) for b in (-1, 0, 1) for c in (-1, 0, 1)]


def plane_masks(rows, depth):
    y = np.arange(rows)[:, None]
    z = np.arange(depth)[None, :]
    masks = [((y + b >= 0) & (y + b < rows) & (z + c >= 0) & (z + c < depth)) for b, c in OFFSETS]
    return np.stack(masks).reshape(len(OFFSETS), 1, rows * depth).astype(np.float32)


def _stacked_parts(lo, mid, hi, h, planes):
    def plane(index):
        if index == 0:
            return lo[0]
        if index == planes + 1:
            return hi[0]
        return mid[index - 1]
    return jnp.concatenate([plane(h), plane(h + 1), plane(h + 2)], axis=0)


def _stacked_edges(edges, mid, h, planes):
    return _stacked_parts(edges.at[0:1], mid, edges.at[1:2], h, planes)


def _shifted_sum(y, mask, chans, lanes, depth, sign):
    total = None
    for k, (b, c) in enumerate(OFFSETS):
        off = sign * (b * depth + c)
        block = y[k * chans : (k + 1) * chans]
        if off != 0:
            block = pltpu.roll(block, (-off) % lanes, 1)
            block = jnp.where(mask[k if sign > 0 else len(OFFSETS) - 1 - k] > 0.5, block, 0.0)
        total = block if total is None else total + block
    return total


def _forward_kernel(edges, mid, wall, bias, cot, mask, act_out, dpre_out, first_out, last_out, *, planes, depth):
    chans, lanes = mid.shape[1], mid.shape[2]
    for p in range(planes):
        y = jnp.dot(wall[...], _stacked_edges(edges, mid, p, planes), preferred_element_type=jnp.float32)
        pre = _shifted_sum(y, mask, chans, lanes, depth, 1) + bias[...]
        sig = 1.0 / (1.0 + jnp.exp(-pre))
        act_out[p] = (pre * sig).astype(act_out.dtype)
        dpre = (cot[p].astype(jnp.float32) * sig * (1.0 + pre * (1.0 - sig))).astype(dpre_out.dtype)
        dpre_out[p] = dpre
        if p == 0:
            first_out[0] = dpre
        if p == planes - 1:
            last_out[0] = dpre


def _input_kernel(lo, mid, hi, wall, mask, out, *, planes, first, depth):
    chans, lanes = mid.shape[1], mid.shape[2]
    for n in range(out.shape[0]):
        y = jnp.dot(wall[...], _stacked_parts(lo, mid, hi, first + n, planes), preferred_element_type=jnp.float32)
        out[n] = _shifted_sum(y, mask, chans, lanes, depth, -1).astype(out.dtype)


def _weight_kernel(upper, edges, mid, dpre, mask, keep_out, send_out, full, *, planes, depth):
    chans, lanes = dpre.shape[1], dpre.shape[2]
    gw = jnp.zeros((9 * chans, 3 * chans), jnp.float32)
    gb = jnp.zeros((chans, 1), jnp.float32)
    for p in range(planes):
        d = dpre[p].astype(jnp.float32)
        gb = gb + jnp.sum(d, axis=1, keepdims=True)
        parts = []
        for k, (b, c) in enumerate(OFFSETS):
            off = b * depth + c
            e = d
            if off != 0:
                e = pltpu.roll(jnp.where(mask[k] > 0.5, d, 0.0), off % lanes, 1)
            parts.append(e.astype(jnp.bfloat16))
        gw = gw + lax.dot_general(
            jnp.concatenate(parts, axis=0), _stacked_edges(edges, mid, p, planes),
            (((1,), (1,)), ((), ())), preferred_element_type=jnp.float32,
        )
    chans_in = gw.shape[1] // 3
    for k in range(len(OFFSETS)):
        for a in range(3):
            t = 9 * a + k
            full[:, t * chans_in : (t + 1) * chans_in] = gw[k * chans : (k + 1) * chans, a * chans_in : (a + 1) * chans_in]
    full[:, 27 * chans_in :] = gb
    half = keep_out.shape[0]
    kept = upper[0]
    keep_out[...] = full[pl.ds(pl.multiple_of(kept * half, 8), half), :]
    send_out[...] = full[pl.ds(pl.multiple_of((1 - kept) * half, 8), half), :]


def _vmem(n):
    return [pl.BlockSpec(memory_space=pltpu.VMEM)] * n


def forward_call(edges, mid, wall, bias, cot, mask, depth):
    planes, chans, lanes = cot.shape
    shape = jax.ShapeDtypeStruct(cot.shape, jnp.bfloat16)
    edge = jax.ShapeDtypeStruct((1, chans, lanes), jnp.bfloat16)
    flops = 2 * planes * wall.shape[0] * wall.shape[1] * lanes
    return pl.pallas_call(
        functools.partial(_forward_kernel, planes=planes, depth=depth),
        out_shape=(shape, shape, edge, edge),
        in_specs=_vmem(6),
        out_specs=tuple(_vmem(4)),
        cost_estimate=pl.CostEstimate(flops=flops, transcendentals=planes * chans * lanes, bytes_accessed=5 * cot.size * 2),
    )(edges, mid, wall, bias, cot, mask)


def input_call(lo, mid, hi, wall, mask, depth, first, count):
    planes, chans, lanes = mid.shape
    flops = 2 * count * wall.shape[0] * wall.shape[1] * lanes
    return pl.pallas_call(
        functools.partial(_input_kernel, planes=planes, first=first, depth=depth),
        out_shape=jax.ShapeDtypeStruct((count, chans, lanes), jnp.bfloat16),
        in_specs=_vmem(5),
        out_specs=_vmem(1)[0],
        cost_estimate=pl.CostEstimate(flops=flops, transcendentals=0, bytes_accessed=3 * mid.size * 2),
    )(lo, mid, hi, wall, mask)


def weight_call(upper, edges, mid, dpre, mask, depth):
    planes, chans, lanes = dpre.shape
    flops = 2 * planes * 9 * chans * 3 * chans * lanes
    half = jax.ShapeDtypeStruct((chans // 2, 27 * chans + 1), jnp.float32)
    return pl.pallas_call(
        functools.partial(_weight_kernel, planes=planes, depth=depth),
        out_shape=(half, half),
        in_specs=[pl.BlockSpec(memory_space=pltpu.SMEM)] + _vmem(4),
        out_specs=tuple(_vmem(2)),
        scratch_shapes=[pltpu.VMEM((chans, 27 * chans + 1), jnp.float32)],
        cost_estimate=pl.CostEstimate(flops=flops, transcendentals=0, bytes_accessed=3 * dpre.size * 2),
    )(upper, edges, mid, dpre, mask)


def neighbours(first, last, axis):
    peers = lax.axis_size(axis)
    up = [(i, i + 1) for i in range(peers - 1)]
    down = [(j, i) for i, j in up]
    return lax.ppermute(last, axis, up), lax.ppermute(first, axis, down)


def swap(value, axis, bit):
    peers = lax.axis_size(axis)
    return lax.ppermute(value, axis, [(i, i ^ bit) for i in range(peers)])


def gather_rows(value, axis):
    peers = lax.axis_size(axis)
    me = lax.axis_index(axis)
    blocks = jnp.zeros((peers,) + value.shape, value.dtype)
    blocks = lax.dynamic_update_index_in_dim(blocks, value, me, 0)
    for k in range(1, peers):
        blocks = lax.dynamic_update_index_in_dim(blocks, swap(value, axis, k), me ^ k, 0)
    return blocks.reshape((peers * value.shape[0],) + value.shape[1:])


def first_upper():
    return (lax.axis_index("real") // (lax.axis_size("real") // 2)) % 2


def reduce_beside(local_grads, work):
    rounds = []
    bit = lax.axis_size("real") // 2
    while bit >= 1:
        rounds.append(("real", bit))
        bit //= 2
    bit = 1
    while bit < lax.axis_size("strike"):
        rounds.append(("strike", bit))
        bit *= 2
    results = []
    value = None
    for k, (axis, bit) in enumerate(rounds):
        if k == 0:
            keep, send = local_grads
        elif axis == "real":
            half = value.shape[0] // 2
            upper = (lax.axis_index(axis) // bit) % 2
            keep = lax.dynamic_slice_in_dim(value, upper * half, half, 0)
            send = lax.dynamic_slice_in_dim(value, (1 - upper) * half, half, 0)
        else:
            keep, send = value, value
        if k < len(work):
            send, inputs = lax.optimization_barrier((send, work[k][1]))
            received = swap(send, axis, bit)
            result = work[k][0](*inputs)
            received, result = lax.optimization_barrier((received, result))
            results.append(result)
        else:
            received = swap(send, axis, bit)
        value = keep + received
    for job, inputs in work[len(rounds) :]:
        results.append(job(*inputs))
    return value, results


def local(grades, cotangent, weight, bias):
    field = grades[0]
    chans, planes, rows, depth = field.shape
    lanes = rows * depth
    taps_in = weight.shape[1]
    packed = jnp.concatenate([weight, bias[:, None]], axis=1)
    whole = gather_rows(packed, "real")
    whole_weight, whole_bias = whole[:, :taps_in], whole[:, taps_in]
    out_chan = whole_weight.shape[0]
    w5 = whole_weight.reshape(out_chan, 3, 3, 3, chans)
    forward_w = w5.transpose(2, 3, 0, 1, 4).reshape(9 * out_chan, 3 * chans)
    backward_w = w5[:, ::-1].transpose(2, 3, 4, 1, 0).reshape(9 * chans, 3 * out_chan)
    mask = jnp.asarray(plane_masks(rows, depth))

    def flat(value):
        return value.transpose(1, 0, 2, 3).reshape(value.shape[1], value.shape[0], lanes)

    def unflat(value):
        return value.reshape(planes, value.shape[1], rows, depth).transpose(1, 0, 2, 3)

    below, above = neighbours(field[:, :1], field[:, planes - 1 :], "strike")
    mid = flat(field)
    edges = flat(jnp.concatenate([below, above], axis=1))
    act, dpre, first, last = forward_call(
        edges, mid, forward_w, whole_bias.astype(jnp.float32)[:, None], flat(cotangent[0]), mask, depth
    )
    dlo, dhi = neighbours(first, last, "strike")
    local_grads = weight_call(first_upper().astype(jnp.int32)[None], edges, mid, dpre, mask, depth)
    work = [
        (functools.partial(input_call, depth=depth, first=p, count=1), (dlo, dpre, dhi, backward_w, mask))
        for p in range(planes)
    ]
    owned, pieces = reduce_beside(local_grads, work)
    grad_input = unflat(jnp.concatenate(pieces, axis=0))
    cells = lax.axis_size("real") * lax.axis_size("strike") * planes * rows * depth
    factor = 1.0 / cells**0.5
    owned = owned * factor
    return (unflat(act)[None], grad_input[None], owned[:, :taps_in], owned[:, taps_in])


def solution(mesh):
    in_specs = (
        P("real", None, "strike", None, None),
        P("real", None, "strike", None, None),
        P("real", None),
        P("real"),
    )
    out_specs = (
        P("real", None, "strike", None, None),
        P("real", None, "strike", None, None),
        P("real", None),
        P("real"),
    )
    return jax.shard_map(local, mesh=mesh, in_specs=in_specs, out_specs=out_specs, check_vma=False)
```

```python
import functools

import jax
import jax.numpy as jnp
import numpy as np
from jax import lax
from jax.experimental import pallas as pl
from jax.experimental.pallas import tpu as pltpu
from jax.sharding import PartitionSpec as P

OFFSETS = [(b, c) for b in (-1, 0, 1) for c in (-1, 0, 1)]


def plane_masks(rows, depth):
    y = np.arange(rows)[:, None]
    z = np.arange(depth)[None, :]
    masks = [((y + b >= 0) & (y + b < rows) & (z + c >= 0) & (z + c < depth)) for b, c in OFFSETS]
    return np.stack(masks).reshape(len(OFFSETS), 1, rows * depth).astype(np.float32)


def _stacked_parts(lo, mid, hi, h, planes):
    def plane(index):
        if index == 0:
            return lo[0]
        if index == planes + 1:
            return hi[0]
        return mid[index - 1]
    return jnp.concatenate([plane(h), plane(h + 1), plane(h + 2)], axis=0)


def _shifted_sum(y, mask, chans, lanes, depth, sign):
    total = None
    for k, (b, c) in enumerate(OFFSETS):
        off = sign * (b * depth + c)
        block = y[k * chans : (k + 1) * chans]
        if off != 0:
            block = pltpu.roll(block, (-off) % lanes, 1)
            block = jnp.where(mask[k if sign > 0 else len(OFFSETS) - 1 - k] > 0.5, block, 0.0)
        total = block if total is None else total + block
    return total


def _forward_kernel(lo, mid, hi, wall, packed, cot, mask, act_out, dpre_out, first_out, last_out, *, planes, depth):
    chans, lanes = mid.shape[1], mid.shape[2]
    bias = packed[:, packed.shape[1] - 1 :].astype(jnp.float32)
    for p in range(planes):
        y = jnp.dot(wall[...], _stacked_parts(lo, mid, hi, p, planes), preferred_element_type=jnp.float32)
        pre = _shifted_sum(y, mask, chans, lanes, depth, 1) + bias
        sig = 1.0 / (1.0 + jnp.exp(-pre))
        act_out[p] = (pre * sig).astype(act_out.dtype)
        dpre = (cot[p].astype(jnp.float32) * sig * (1.0 + pre * (1.0 - sig))).astype(dpre_out.dtype)
        dpre_out[p] = dpre
        if p == 0:
            first_out[0] = dpre
        if p == planes - 1:
            last_out[0] = dpre


def _input_kernel(lo, mid, hi, wall, mask, out, *, planes, first, depth):
    chans, lanes = mid.shape[1], mid.shape[2]
    for n in range(out.shape[0]):
        y = jnp.dot(wall[...], _stacked_parts(lo, mid, hi, first + n, planes), preferred_element_type=jnp.float32)
        out[n] = _shifted_sum(y, mask, chans, lanes, depth, -1).astype(out.dtype)


def _weight_kernel(upper, lo, mid, hi, dpre, mask, keep_out, send_out, full, *, planes, depth):
    chans, lanes = dpre.shape[1], dpre.shape[2]
    gw = jnp.zeros((9 * chans, 3 * chans), jnp.float32)
    gb = jnp.zeros((chans, 1), jnp.float32)
    for p in range(planes):
        d = dpre[p].astype(jnp.float32)
        gb = gb + jnp.sum(d, axis=1, keepdims=True)
        parts = []
        for k, (b, c) in enumerate(OFFSETS):
            off = b * depth + c
            e = d
            if off != 0:
                e = pltpu.roll(jnp.where(mask[k] > 0.5, d, 0.0), off % lanes, 1)
            parts.append(e.astype(jnp.bfloat16))
        gw = gw + lax.dot_general(
            jnp.concatenate(parts, axis=0), _stacked_parts(lo, mid, hi, p, planes),
            (((1,), (1,)), ((), ())), preferred_element_type=jnp.float32,
        )
    chans_in = gw.shape[1] // 3
    for k in range(len(OFFSETS)):
        for a in range(3):
            t = 9 * a + k
            full[:, t * chans_in : (t + 1) * chans_in] = gw[k * chans : (k + 1) * chans, a * chans_in : (a + 1) * chans_in]
    full[:, 27 * chans_in :] = gb
    half = keep_out.shape[0]
    kept = upper[0]
    keep_out[...] = full[pl.ds(pl.multiple_of(kept * half, 8), half), :]
    send_out[...] = full[pl.ds(pl.multiple_of((1 - kept) * half, 8), half), :]


def _vmem(n):
    return [pl.BlockSpec(memory_space=pltpu.VMEM)] * n


def forward_call(lo, mid, hi, wall, packed, cot, mask, depth):
    planes, chans, lanes = cot.shape
    shape = jax.ShapeDtypeStruct(cot.shape, jnp.bfloat16)
    edge = jax.ShapeDtypeStruct((1, chans, lanes), jnp.bfloat16)
    flops = 2 * planes * wall.shape[0] * wall.shape[1] * lanes
    return pl.pallas_call(
        functools.partial(_forward_kernel, planes=planes, depth=depth),
        out_shape=(shape, shape, edge, edge),
        in_specs=_vmem(7),
        out_specs=tuple(_vmem(4)),
        cost_estimate=pl.CostEstimate(flops=flops, transcendentals=planes * chans * lanes, bytes_accessed=5 * cot.size * 2),
    )(lo, mid, hi, wall, packed, cot, mask)


def input_call(lo, mid, hi, wall, mask, depth, first, count):
    planes, chans, lanes = mid.shape
    flops = 2 * count * wall.shape[0] * wall.shape[1] * lanes
    return pl.pallas_call(
        functools.partial(_input_kernel, planes=planes, first=first, depth=depth),
        out_shape=jax.ShapeDtypeStruct((count, chans, lanes), jnp.bfloat16),
        in_specs=_vmem(5),
        out_specs=_vmem(1)[0],
        cost_estimate=pl.CostEstimate(flops=flops, transcendentals=0, bytes_accessed=3 * mid.size * 2),
    )(lo, mid, hi, wall, mask)


def weight_call(upper, lo, mid, hi, dpre, mask, depth):
    planes, chans, lanes = dpre.shape
    flops = 2 * planes * 9 * chans * 3 * chans * lanes
    half = jax.ShapeDtypeStruct((chans // 2, 27 * chans + 1), jnp.float32)
    return pl.pallas_call(
        functools.partial(_weight_kernel, planes=planes, depth=depth),
        out_shape=(half, half),
        in_specs=[pl.BlockSpec(memory_space=pltpu.SMEM)] + _vmem(5),
        out_specs=tuple(_vmem(2)),
        scratch_shapes=[pltpu.VMEM((chans, 27 * chans + 1), jnp.float32)],
        cost_estimate=pl.CostEstimate(flops=flops, transcendentals=0, bytes_accessed=3 * dpre.size * 2),
    )(upper, lo, mid, hi, dpre, mask)


def neighbours(first, last, axis):
    peers = lax.axis_size(axis)
    up = [(i, i + 1) for i in range(peers - 1)]
    down = [(j, i) for i, j in up]
    return lax.ppermute(last, axis, up), lax.ppermute(first, axis, down)


def swap(value, axis, bit):
    peers = lax.axis_size(axis)
    return lax.ppermute(value, axis, [(i, i ^ bit) for i in range(peers)])


def gather_rows(value, axis):
    peers = lax.axis_size(axis)
    me = lax.axis_index(axis)
    blocks = jnp.zeros((peers,) + value.shape, value.dtype)
    blocks = lax.dynamic_update_index_in_dim(blocks, value, me, 0)
    for k in range(1, peers):
        blocks = lax.dynamic_update_index_in_dim(blocks, swap(value, axis, k), me ^ k, 0)
    return blocks.reshape((peers * value.shape[0],) + value.shape[1:])


def first_upper():
    return (lax.axis_index("real") // (lax.axis_size("real") // 2)) % 2


def reduce_beside(local_grads, work):
    rounds = []
    bit = lax.axis_size("real") // 2
    while bit >= 1:
        rounds.append(("real", bit))
        bit //= 2
    bit = 1
    while bit < lax.axis_size("strike"):
        rounds.append(("strike", bit))
        bit *= 2
    results = []
    value = None
    for k, (axis, bit) in enumerate(rounds):
        if k == 0:
            keep, send = local_grads
        elif axis == "real":
            half = value.shape[0] // 2
            upper = (lax.axis_index(axis) // bit) % 2
            keep = lax.dynamic_slice_in_dim(value, upper * half, half, 0)
            send = lax.dynamic_slice_in_dim(value, (1 - upper) * half, half, 0)
        else:
            keep, send = value, value
        if k < len(work):
            send, inputs = lax.optimization_barrier((send, work[k][1]))
            received = swap(send, axis, bit)
            result = work[k][0](*inputs)
            received, result = lax.optimization_barrier((received, result))
            results.append(result)
        else:
            received = swap(send, axis, bit)
        value = keep + received
    for job, inputs in work[len(rounds) :]:
        results.append(job(*inputs))
    return value, results


def local(grades, cotangent, weight, bias):
    field = grades[0]
    chans, planes, rows, depth = field.shape
    lanes = rows * depth
    taps_in = weight.shape[1]
    packed = jnp.concatenate([weight, bias[:, None]], axis=1)
    whole = gather_rows(packed, "real")
    whole_weight = whole[:, :taps_in]
    out_chan = whole_weight.shape[0]
    w5 = whole_weight.reshape(out_chan, 3, 3, 3, chans)
    forward_w = w5.transpose(2, 3, 0, 1, 4).reshape(9 * out_chan, 3 * chans)
    backward_w = w5[:, ::-1].transpose(2, 3, 4, 1, 0).reshape(9 * chans, 3 * out_chan)
    mask = jnp.asarray(plane_masks(rows, depth))

    def flat(value):
        return value.transpose(1, 0, 2, 3).reshape(value.shape[1], value.shape[0], lanes)

    def unflat(value):
        return value.reshape(planes, value.shape[1], rows, depth).transpose(1, 0, 2, 3)

    below, above = neighbours(field[:, :1], field[:, planes - 1 :], "strike")
    mid = flat(field)
    lo, hi = flat(below), flat(above)
    act, dpre, first, last = forward_call(
        lo, mid, hi, forward_w, whole, flat(cotangent[0]), mask, depth
    )
    dlo, dhi = neighbours(first, last, "strike")
    local_grads = weight_call(first_upper().astype(jnp.int32)[None], lo, mid, hi, dpre, mask, depth)
    work = [
        (functools.partial(input_call, depth=depth, first=p, count=1), (dlo, dpre, dhi, backward_w, mask))
        for p in range(planes)
    ]
    owned, pieces = reduce_beside(local_grads, work)
    grad_input = unflat(jnp.concatenate(pieces, axis=0))
    cells = lax.axis_size("real") * lax.axis_size("strike") * planes * rows * depth
    factor = 1.0 / cells**0.5
    owned = owned * factor
    return (unflat(act)[None], grad_input[None], owned[:, :taps_in], owned[:, taps_in])


def solution(mesh):
    in_specs = (
        P("real", None, "strike", None, None),
        P("real", None, "strike", None, None),
        P("real", None),
        P("real"),
    )
    out_specs = (
        P("real", None, "strike", None, None),
        P("real", None, "strike", None, None),
        P("real", None),
        P("real"),
    )
    return jax.shard_map(local, mesh=mesh, in_specs=in_specs, out_specs=out_specs, check_vma=False)
```

```python
import functools

import jax
import jax.numpy as jnp
import numpy as np
from jax import lax
from jax.experimental import pallas as pl
from jax.experimental.pallas import tpu as pltpu
from jax.sharding import PartitionSpec as P

OFFSETS = [(b, c) for b in (-1, 0, 1) for c in (-1, 0, 1)]


def plane_masks(rows, depth):
    y = np.arange(rows)[:, None]
    z = np.arange(depth)[None, :]
    masks = [((y + b >= 0) & (y + b < rows) & (z + c >= 0) & (z + c < depth)) for b, c in OFFSETS]
    return np.stack(masks).reshape(len(OFFSETS), 1, rows * depth).astype(np.float32)


def _stacked_parts(lo, mid, hi, h, planes):
    def plane(index):
        if index == 0:
            return lo[0]
        if index == planes + 1:
            return hi[0]
        return mid[index - 1]
    return jnp.concatenate([plane(h), plane(h + 1), plane(h + 2)], axis=0)


def _shifted_sum(y, mask, chans, lanes, depth, sign):
    total = None
    for k, (b, c) in enumerate(OFFSETS):
        off = sign * (b * depth + c)
        block = y[k * chans : (k + 1) * chans]
        if off != 0:
            block = pltpu.roll(block, (-off) % lanes, 1)
            block = jnp.where(mask[k if sign > 0 else len(OFFSETS) - 1 - k] > 0.5, block, 0.0)
        total = block if total is None else total + block
    return total


def _forward_kernel(lo, mid, hi, wall, bias, cot, mask, act_out, dpre_out, first_out, last_out, *, planes, depth):
    chans, lanes = mid.shape[1], mid.shape[2]
    for p in range(planes):
        y = jnp.dot(wall[...], _stacked_parts(lo, mid, hi, p, planes), preferred_element_type=jnp.float32)
        pre = _shifted_sum(y, mask, chans, lanes, depth, 1) + bias[...]
        sig = 1.0 / (1.0 + jnp.exp(-pre))
        act_out[p] = (pre * sig).astype(act_out.dtype)
        dpre = (cot[p].astype(jnp.float32) * sig * (1.0 + pre * (1.0 - sig))).astype(dpre_out.dtype)
        dpre_out[p] = dpre
        if p == 0:
            first_out[0] = dpre
        if p == planes - 1:
            last_out[0] = dpre


def _input_kernel(lo, mid, hi, wall, mask, out, *, planes, first, depth):
    chans, lanes = mid.shape[1], mid.shape[2]
    for n in range(out.shape[0]):
        y = jnp.dot(wall[...], _stacked_parts(lo, mid, hi, first + n, planes), preferred_element_type=jnp.float32)
        out[n] = _shifted_sum(y, mask, chans, lanes, depth, -1).astype(out.dtype)


def _weight_kernel(upper, lo, mid, hi, dpre, mask, keep_out, send_out, full, *, planes, depth):
    chans, lanes = dpre.shape[1], dpre.shape[2]
    gw = jnp.zeros((9 * chans, 3 * chans), jnp.float32)
    gb = jnp.zeros((chans, 1), jnp.float32)
    for p in range(planes):
        d = dpre[p].astype(jnp.float32)
        gb = gb + jnp.sum(d, axis=1, keepdims=True)
        parts = []
        for k, (b, c) in enumerate(OFFSETS):
            off = b * depth + c
            e = d
            if off != 0:
                e = pltpu.roll(jnp.where(mask[k] > 0.5, d, 0.0), off % lanes, 1)
            parts.append(e.astype(jnp.bfloat16))
        gw = gw + lax.dot_general(
            jnp.concatenate(parts, axis=0), _stacked_parts(lo, mid, hi, p, planes),
            (((1,), (1,)), ((), ())), preferred_element_type=jnp.float32,
        )
    chans_in = gw.shape[1] // 3
    for k in range(len(OFFSETS)):
        for a in range(3):
            t = 9 * a + k
            full[:, t * chans_in : (t + 1) * chans_in] = gw[k * chans : (k + 1) * chans, a * chans_in : (a + 1) * chans_in]
    full[:, 27 * chans_in :] = gb
    half = keep_out.shape[0]
    kept = upper[0]
    keep_out[...] = full[pl.ds(pl.multiple_of(kept * half, 8), half), :]
    send_out[...] = full[pl.ds(pl.multiple_of((1 - kept) * half, 8), half), :]


def _vmem(n):
    return [pl.BlockSpec(memory_space=pltpu.VMEM)] * n


def forward_call(lo, mid, hi, wall, bias, cot, mask, depth):
    planes, chans, lanes = cot.shape
    shape = jax.ShapeDtypeStruct(cot.shape, jnp.bfloat16)
    edge = jax.ShapeDtypeStruct((1, chans, lanes), jnp.bfloat16)
    flops = 2 * planes * wall.shape[0] * wall.shape[1] * lanes
    return pl.pallas_call(
        functools.partial(_forward_kernel, planes=planes, depth=depth),
        out_shape=(shape, shape, edge, edge),
        in_specs=_vmem(7),
        out_specs=tuple(_vmem(4)),
        cost_estimate=pl.CostEstimate(flops=flops, transcendentals=planes * chans * lanes, bytes_accessed=5 * cot.size * 2),
    )(lo, mid, hi, wall, bias, cot, mask)


def input_call(lo, mid, hi, wall, mask, depth, first, count):
    planes, chans, lanes = mid.shape
    flops = 2 * count * wall.shape[0] * wall.shape[1] * lanes
    return pl.pallas_call(
        functools.partial(_input_kernel, planes=planes, first=first, depth=depth),
        out_shape=jax.ShapeDtypeStruct((count, chans, lanes), jnp.bfloat16),
        in_specs=_vmem(5),
        out_specs=_vmem(1)[0],
        cost_estimate=pl.CostEstimate(flops=flops, transcendentals=0, bytes_accessed=3 * mid.size * 2),
    )(lo, mid, hi, wall, mask)


def weight_call(upper, lo, mid, hi, dpre, mask, depth):
    planes, chans, lanes = dpre.shape
    flops = 2 * planes * 9 * chans * 3 * chans * lanes
    half = jax.ShapeDtypeStruct((chans // 2, 27 * chans + 1), jnp.float32)
    return pl.pallas_call(
        functools.partial(_weight_kernel, planes=planes, depth=depth),
        out_shape=(half, half),
        in_specs=[pl.BlockSpec(memory_space=pltpu.SMEM)] + _vmem(5),
        out_specs=tuple(_vmem(2)),
        scratch_shapes=[pltpu.VMEM((chans, 27 * chans + 1), jnp.float32)],
        cost_estimate=pl.CostEstimate(flops=flops, transcendentals=0, bytes_accessed=3 * dpre.size * 2),
    )(upper, lo, mid, hi, dpre, mask)


def neighbours(first, last, axis):
    peers = lax.axis_size(axis)
    up = [(i, i + 1) for i in range(peers - 1)]
    down = [(j, i) for i, j in up]
    return lax.ppermute(last, axis, up), lax.ppermute(first, axis, down)


def swap(value, axis, bit):
    peers = lax.axis_size(axis)
    return lax.ppermute(value, axis, [(i, i ^ bit) for i in range(peers)])


def gather_rows(value, axis):
    peers = lax.axis_size(axis)
    me = lax.axis_index(axis)
    blocks = jnp.zeros((peers,) + value.shape, value.dtype)
    blocks = lax.dynamic_update_index_in_dim(blocks, value, me, 0)
    for k in range(1, peers):
        blocks = lax.dynamic_update_index_in_dim(blocks, swap(value, axis, k), me ^ k, 0)
    return blocks.reshape((peers * value.shape[0],) + value.shape[1:])


def first_upper():
    return (lax.axis_index("real") // (lax.axis_size("real") // 2)) % 2


def reduce_beside(local_grads, work):
    rounds = []
    bit = lax.axis_size("real") // 2
    while bit >= 1:
        rounds.append(("real", bit))
        bit //= 2
    bit = lax.axis_size("strike") // 2
    while bit >= 1:
        rounds.append(("strike", bit))
        bit //= 2
    results = []
    value = None
    for k, (axis, bit) in enumerate(rounds):
        if k == 0:
            keep, send = local_grads
        elif axis == "real":
            half = value.shape[0] // 2
            upper = (lax.axis_index(axis) // bit) % 2
            keep = lax.dynamic_slice_in_dim(value, upper * half, half, 0)
            send = lax.dynamic_slice_in_dim(value, (1 - upper) * half, half, 0)
        else:
            keep, send = value, value
        if k < len(work):
            send, inputs = lax.optimization_barrier((send, work[k][1]))
            received = swap(send, axis, bit)
            result = work[k][0](*inputs)
            received, result = lax.optimization_barrier((received, result))
            results.append(result)
        else:
            received = swap(send, axis, bit)
        value = keep + received
    for job, inputs in work[len(rounds) :]:
        results.append(job(*inputs))
    return value, results


def local(grades, cotangent, weight, bias):
    field = grades[0]
    chans, planes, rows, depth = field.shape
    lanes = rows * depth
    taps_in = weight.shape[1]
    packed = jnp.concatenate([weight, bias[:, None]], axis=1)
    whole = gather_rows(packed, "real")
    whole_weight, whole_bias = whole[:, :taps_in], whole[:, taps_in]
    out_chan = whole_weight.shape[0]
    w5 = whole_weight.reshape(out_chan, 3, 3, 3, chans)
    forward_w = w5.transpose(2, 3, 0, 1, 4).reshape(9 * out_chan, 3 * chans)
    backward_w = w5[:, ::-1].transpose(2, 3, 4, 1, 0).reshape(9 * chans, 3 * out_chan)
    mask = jnp.asarray(plane_masks(rows, depth))

    def flat(value):
        return value.transpose(1, 0, 2, 3).reshape(value.shape[1], value.shape[0], lanes)

    def unflat(value):
        return value.reshape(planes, value.shape[1], rows, depth).transpose(1, 0, 2, 3)

    below, above = neighbours(field[:, :1], field[:, planes - 1 :], "strike")
    mid = flat(field)
    lo, hi = flat(below), flat(above)
    act, dpre, first, last = forward_call(
        lo, mid, hi, forward_w, whole_bias.astype(jnp.float32)[:, None], flat(cotangent[0]), mask, depth
    )
    dlo, dhi = neighbours(first, last, "strike")
    local_grads = weight_call(first_upper().astype(jnp.int32)[None], lo, mid, hi, dpre, mask, depth)
    work = [
        (functools.partial(input_call, depth=depth, first=p, count=1), (dlo, dpre, dhi, backward_w, mask))
        for p in range(planes)
    ]
    owned, pieces = reduce_beside(local_grads, work)
    grad_input = unflat(jnp.concatenate(pieces, axis=0))
    cells = lax.axis_size("real") * lax.axis_size("strike") * planes * rows * depth
    factor = 1.0 / cells**0.5
    owned = owned * factor
    return (unflat(act)[None], grad_input[None], owned[:, :taps_in], owned[:, taps_in])


def solution(mesh):
    in_specs = (
        P("real", None, "strike", None, None),
        P("real", None, "strike", None, None),
        P("real", None),
        P("real"),
    )
    out_specs = (
        P("real", None, "strike", None, None),
        P("real", None, "strike", None, None),
        P("real", None),
        P("real"),
    )
    return jax.shard_map(local, mesh=mesh, in_specs=in_specs, out_specs=out_specs, check_vma=False)
```

```python
import functools

import jax
import jax.numpy as jnp
import numpy as np
from jax import lax
from jax.experimental import pallas as pl
from jax.experimental.pallas import tpu as pltpu
from jax.sharding import PartitionSpec as P

OFFSETS = [(b, c) for b in (-1, 0, 1) for c in (-1, 0, 1)]


def plane_masks(rows, depth):
    y = np.arange(rows)[:, None]
    z = np.arange(depth)[None, :]
    masks = [((y + b >= 0) & (y + b < rows) & (z + c >= 0) & (z + c < depth)) for b, c in OFFSETS]
    return np.stack(masks).reshape(len(OFFSETS), 1, rows * depth).astype(np.float32)


def _stacked_parts(lo, mid, hi, h, planes):
    def plane(index):
        if index == 0:
            return lo[0]
        if index == planes + 1:
            return hi[0]
        return mid[index - 1]
    return jnp.concatenate([plane(h), plane(h + 1), plane(h + 2)], axis=0)


def _shifted_sum(y, mask, chans, lanes, depth, sign):
    total = None
    for k, (b, c) in enumerate(OFFSETS):
        off = sign * (b * depth + c)
        block = y[k * chans : (k + 1) * chans]
        if off != 0:
            block = pltpu.roll(block, (-off) % lanes, 1)
            block = jnp.where(mask[k if sign > 0 else len(OFFSETS) - 1 - k] > 0.5, block, 0.0)
        total = block if total is None else total + block
    return total


def _forward_kernel(lo, mid, hi, wall, bias, cot, mask, act_out, dpre_out, first_out, last_out, *, planes, depth):
    chans, lanes = mid.shape[1], mid.shape[2]
    for p in range(planes):
        y = jnp.dot(wall[...], _stacked_parts(lo, mid, hi, p, planes), preferred_element_type=jnp.float32)
        pre = _shifted_sum(y, mask, chans, lanes, depth, 1) + bias[...]
        sig = 1.0 / (1.0 + jnp.exp(-pre))
        act_out[p] = (pre * sig).astype(act_out.dtype)
        dpre = (cot[p].astype(jnp.float32) * sig * (1.0 + pre * (1.0 - sig))).astype(dpre_out.dtype)
        dpre_out[p] = dpre
        if p == 0:
            first_out[0] = dpre
        if p == planes - 1:
            last_out[0] = dpre


def _input_kernel(lo, mid, hi, wall, mask, out, *, planes, first, depth):
    chans, lanes = mid.shape[1], mid.shape[2]
    for n in range(out.shape[0]):
        y = jnp.dot(wall[...], _stacked_parts(lo, mid, hi, first + n, planes), preferred_element_type=jnp.float32)
        out[n] = _shifted_sum(y, mask, chans, lanes, depth, -1).astype(out.dtype)


def _weight_kernel(upper, lo, mid, hi, dpre, mask, keep_out, send_out, full, *, planes, depth):
    chans, lanes = dpre.shape[1], dpre.shape[2]
    gw = jnp.zeros((9 * chans, 3 * chans), jnp.float32)
    gb = jnp.zeros((chans, 1), jnp.float32)
    for p in range(planes):
        d = dpre[p].astype(jnp.float32)
        gb = gb + jnp.sum(d, axis=1, keepdims=True)
        parts = []
        for k, (b, c) in enumerate(OFFSETS):
            off = b * depth + c
            e = d
            if off != 0:
                e = pltpu.roll(jnp.where(mask[k] > 0.5, d, 0.0), off % lanes, 1)
            parts.append(e.astype(jnp.bfloat16))
        gw = gw + lax.dot_general(
            jnp.concatenate(parts, axis=0), _stacked_parts(lo, mid, hi, p, planes),
            (((1,), (1,)), ((), ())), preferred_element_type=jnp.float32,
        )
    chans_in = gw.shape[1] // 3
    for k in range(len(OFFSETS)):
        for a in range(3):
            t = 9 * a + k
            full[:, t * chans_in : (t + 1) * chans_in] = gw[k * chans : (k + 1) * chans, a * chans_in : (a + 1) * chans_in]
    full[:, 27 * chans_in :] = gb
    half = keep_out.shape[0]
    kept = upper[0]
    keep_out[...] = full[pl.ds(pl.multiple_of(kept * half, 8), half), :]
    send_out[...] = full[pl.ds(pl.multiple_of((1 - kept) * half, 8), half), :]


def _vmem(n):
    return [pl.BlockSpec(memory_space=pltpu.VMEM)] * n


def forward_call(lo, mid, hi, wall, bias, cot, mask, depth):
    planes, chans, lanes = cot.shape
    shape = jax.ShapeDtypeStruct(cot.shape, jnp.bfloat16)
    edge = jax.ShapeDtypeStruct((1, chans, lanes), jnp.bfloat16)
    flops = 2 * planes * wall.shape[0] * wall.shape[1] * lanes
    return pl.pallas_call(
        functools.partial(_forward_kernel, planes=planes, depth=depth),
        out_shape=(shape, shape, edge, edge),
        in_specs=_vmem(7),
        out_specs=tuple(_vmem(4)),
        cost_estimate=pl.CostEstimate(flops=flops, transcendentals=planes * chans * lanes, bytes_accessed=5 * cot.size * 2),
    )(lo, mid, hi, wall, bias, cot, mask)


def input_call(lo, mid, hi, wall, mask, depth, first, count):
    planes, chans, lanes = mid.shape
    flops = 2 * count * wall.shape[0] * wall.shape[1] * lanes
    return pl.pallas_call(
        functools.partial(_input_kernel, planes=planes, first=first, depth=depth),
        out_shape=jax.ShapeDtypeStruct((count, chans, lanes), jnp.bfloat16),
        in_specs=_vmem(5),
        out_specs=_vmem(1)[0],
        cost_estimate=pl.CostEstimate(flops=flops, transcendentals=0, bytes_accessed=3 * mid.size * 2),
    )(lo, mid, hi, wall, mask)


def weight_call(upper, lo, mid, hi, dpre, mask, depth):
    planes, chans, lanes = dpre.shape
    flops = 2 * planes * 9 * chans * 3 * chans * lanes
    half = jax.ShapeDtypeStruct((chans // 2, 27 * chans + 1), jnp.float32)
    return pl.pallas_call(
        functools.partial(_weight_kernel, planes=planes, depth=depth),
        out_shape=(half, half),
        in_specs=[pl.BlockSpec(memory_space=pltpu.SMEM)] + _vmem(5),
        out_specs=tuple(_vmem(2)),
        scratch_shapes=[pltpu.VMEM((chans, 27 * chans + 1), jnp.float32)],
        cost_estimate=pl.CostEstimate(flops=flops, transcendentals=0, bytes_accessed=3 * dpre.size * 2),
    )(upper, lo, mid, hi, dpre, mask)


def neighbours(first, last, axis):
    peers = lax.axis_size(axis)
    up = [(i, i + 1) for i in range(peers - 1)]
    down = [(j, i) for i, j in up]
    return lax.ppermute(last, axis, up), lax.ppermute(first, axis, down)


def swap(value, axis, bit):
    peers = lax.axis_size(axis)
    return lax.ppermute(value, axis, [(i, i ^ bit) for i in range(peers)])


def gather_rows(value, axis):
    peers = lax.axis_size(axis)
    me = lax.axis_index(axis)
    blocks = jnp.zeros((peers,) + value.shape, value.dtype)
    blocks = lax.dynamic_update_index_in_dim(blocks, value, me, 0)
    for k in range(1, peers):
        blocks = lax.dynamic_update_index_in_dim(blocks, swap(value, axis, k), me ^ k, 0)
    return blocks.reshape((peers * value.shape[0],) + value.shape[1:])


def first_upper():
    return (lax.axis_index("real") // (lax.axis_size("real") // 2)) % 2


def reduce_beside(local_grads, work):
    rounds = []
    bit = lax.axis_size("real") // 2
    while bit >= 1:
        rounds.append(("real", bit))
        bit //= 2
    bit = 1
    while bit < lax.axis_size("strike"):
        rounds.append(("strike", bit))
        bit *= 2
    results = []
    value = None
    for k, (axis, bit) in enumerate(rounds):
        if k == 0:
            keep, send = local_grads
        elif axis == "real":
            half = value.shape[0] // 2
            upper = (lax.axis_index(axis) // bit) % 2
            keep = lax.dynamic_slice_in_dim(value, upper * half, half, 0)
            send = lax.dynamic_slice_in_dim(value, (1 - upper) * half, half, 0)
        else:
            keep, send = value, value
        if k < len(work) and work[k] is not None:
            job_inputs = work[k][1](results) if callable(work[k][1]) else work[k][1]
            send, inputs = lax.optimization_barrier((send, job_inputs))
            received = swap(send, axis, bit)
            result = work[k][0](*inputs)
            received, result = lax.optimization_barrier((received, result))
            results.append(result)
        else:
            received = swap(send, axis, bit)
        value = keep + received
    for job, inputs in work[len(rounds) :]:
        results.append(job(*(inputs(results) if callable(inputs) else inputs)))
    return value, results


def local(grades, cotangent, weight, bias):
    field = grades[0]
    chans, planes, rows, depth = field.shape
    lanes = rows * depth
    taps_in = weight.shape[1]
    packed = jnp.concatenate([weight, bias[:, None]], axis=1)
    whole = gather_rows(packed, "real")
    whole_weight, whole_bias = whole[:, :taps_in], whole[:, taps_in]
    out_chan = whole_weight.shape[0]
    w5 = whole_weight.reshape(out_chan, 3, 3, 3, chans)
    forward_w = w5.transpose(2, 3, 0, 1, 4).reshape(9 * out_chan, 3 * chans)
    backward_w = w5[:, ::-1].transpose(2, 3, 4, 1, 0).reshape(9 * chans, 3 * out_chan)
    mask = jnp.asarray(plane_masks(rows, depth))

    def flat(value):
        return value.transpose(1, 0, 2, 3).reshape(value.shape[1], value.shape[0], lanes)

    def unflat(value):
        return value.reshape(planes, value.shape[1], rows, depth).transpose(1, 0, 2, 3)

    below, above = neighbours(field[:, :1], field[:, planes - 1 :], "strike")
    mid = flat(field)
    lo, hi = flat(below), flat(above)
    act, dpre, first, last = forward_call(
        lo, mid, hi, forward_w, whole_bias.astype(jnp.float32)[:, None], flat(cotangent[0]), mask, depth
    )
    dlo, dhi = neighbours(first, last, "strike")
    local_grads = weight_call(first_upper().astype(jnp.int32)[None], lo, mid, hi, dpre, mask, depth)
    work = [
        (functools.partial(input_call, depth=depth, first=p, count=1), (dlo, dpre, dhi, backward_w, mask))
        for p in range(planes)
    ]
    work += [None] * (3 - len(work)) + [(lambda *parts: unflat(jnp.concatenate(parts, axis=0)), lambda done: tuple(done))]
    owned, pieces = reduce_beside(local_grads, work)
    grad_input = pieces[-1]
    cells = lax.axis_size("real") * lax.axis_size("strike") * planes * rows * depth
    factor = 1.0 / cells**0.5
    owned = owned * factor
    return (unflat(act)[None], grad_input[None], owned[:, :taps_in], owned[:, taps_in])


def solution(mesh):
    in_specs = (
        P("real", None, "strike", None, None),
        P("real", None, "strike", None, None),
        P("real", None),
        P("real"),
    )
    out_specs = (
        P("real", None, "strike", None, None),
        P("real", None, "strike", None, None),
        P("real", None),
        P("real"),
    )
    return jax.shard_map(local, mesh=mesh, in_specs=in_specs, out_specs=out_specs, check_vma=False)
```

```python
import functools

import jax
import jax.numpy as jnp
import numpy as np
from jax import lax
from jax.experimental import pallas as pl
from jax.experimental.pallas import tpu as pltpu
from jax.sharding import PartitionSpec as P

OFFSETS = [(b, c) for b in (-1, 0, 1) for c in (-1, 0, 1)]


def plane_masks(rows, depth):
    y = np.arange(rows)[:, None]
    z = np.arange(depth)[None, :]
    masks = [((y + b >= 0) & (y + b < rows) & (z + c >= 0) & (z + c < depth)) for b, c in OFFSETS]
    return np.stack(masks).reshape(len(OFFSETS), 1, rows * depth).astype(np.float32)


def _stacked_parts(lo, mid, hi, h, planes):
    def plane(index):
        if index == 0:
            return lo[0]
        if index == planes + 1:
            return hi[0]
        return mid[index - 1]
    return jnp.concatenate([plane(h), plane(h + 1), plane(h + 2)], axis=0)


def _shifted_sum(y, mask, chans, lanes, depth, sign):
    total = None
    for k, (b, c) in enumerate(OFFSETS):
        off = sign * (b * depth + c)
        block = y[k * chans : (k + 1) * chans]
        if off != 0:
            block = pltpu.roll(block, (-off) % lanes, 1)
            block = jnp.where(mask[k if sign > 0 else len(OFFSETS) - 1 - k] > 0.5, block, 0.0)
        total = block if total is None else total + block
    return total


def _forward_kernel(lo, mid, hi, wall, bias, cot, mask, act_out, dpre_out, first_out, last_out, *, planes, depth):
    chans, lanes = mid.shape[1], mid.shape[2]
    for p in range(planes):
        y = jnp.dot(wall[...], _stacked_parts(lo, mid, hi, p, planes), preferred_element_type=jnp.float32)
        pre = _shifted_sum(y, mask, chans, lanes, depth, 1) + bias[...]
        sig = 0.5 + 0.5 * jnp.tanh(0.5 * pre)
        act_out[p] = (pre * sig).astype(act_out.dtype)
        dpre = (cot[p].astype(jnp.float32) * sig * (1.0 + pre * (1.0 - sig))).astype(dpre_out.dtype)
        dpre_out[p] = dpre
        if p == 0:
            first_out[0] = dpre
        if p == planes - 1:
            last_out[0] = dpre


def _input_kernel(lo, mid, hi, wall, mask, out, *, planes, first, depth):
    chans, lanes = mid.shape[1], mid.shape[2]
    for n in range(out.shape[0]):
        y = jnp.dot(wall[...], _stacked_parts(lo, mid, hi, first + n, planes), preferred_element_type=jnp.float32)
        out[n] = _shifted_sum(y, mask, chans, lanes, depth, -1).astype(out.dtype)


def _weight_kernel(upper, lo, mid, hi, dpre, mask, keep_out, send_out, full, *, planes, depth):
    chans, lanes = dpre.shape[1], dpre.shape[2]
    gw = jnp.zeros((9 * chans, 3 * chans), jnp.float32)
    gb = jnp.zeros((chans, 1), jnp.float32)
    for p in range(planes):
        d = dpre[p].astype(jnp.float32)
        gb = gb + jnp.sum(d, axis=1, keepdims=True)
        parts = []
        for k, (b, c) in enumerate(OFFSETS):
            off = b * depth + c
            e = d
            if off != 0:
                e = pltpu.roll(jnp.where(mask[k] > 0.5, d, 0.0), off % lanes, 1)
            parts.append(e.astype(jnp.bfloat16))
        gw = gw + lax.dot_general(
            jnp.concatenate(parts, axis=0), _stacked_parts(lo, mid, hi, p, planes),
            (((1,), (1,)), ((), ())), preferred_element_type=jnp.float32,
        )
    chans_in = gw.shape[1] // 3
    for k in range(len(OFFSETS)):
        for a in range(3):
            t = 9 * a + k
            full[:, t * chans_in : (t + 1) * chans_in] = gw[k * chans : (k + 1) * chans, a * chans_in : (a + 1) * chans_in]
    full[:, 27 * chans_in :] = gb
    half = keep_out.shape[0]
    kept = upper[0]
    keep_out[...] = full[pl.ds(pl.multiple_of(kept * half, 8), half), :]
    send_out[...] = full[pl.ds(pl.multiple_of((1 - kept) * half, 8), half), :]


def _vmem(n):
    return [pl.BlockSpec(memory_space=pltpu.VMEM)] * n


def forward_call(lo, mid, hi, wall, bias, cot, mask, depth):
    planes, chans, lanes = cot.shape
    shape = jax.ShapeDtypeStruct(cot.shape, jnp.bfloat16)
    edge = jax.ShapeDtypeStruct((1, chans, lanes), jnp.bfloat16)
    flops = 2 * planes * wall.shape[0] * wall.shape[1] * lanes
    return pl.pallas_call(
        functools.partial(_forward_kernel, planes=planes, depth=depth),
        out_shape=(shape, shape, edge, edge),
        in_specs=_vmem(7),
        out_specs=tuple(_vmem(4)),
        cost_estimate=pl.CostEstimate(flops=flops, transcendentals=planes * chans * lanes, bytes_accessed=5 * cot.size * 2),
    )(lo, mid, hi, wall, bias, cot, mask)


def input_call(lo, mid, hi, wall, mask, depth, first, count):
    planes, chans, lanes = mid.shape
    flops = 2 * count * wall.shape[0] * wall.shape[1] * lanes
    return pl.pallas_call(
        functools.partial(_input_kernel, planes=planes, first=first, depth=depth),
        out_shape=jax.ShapeDtypeStruct((count, chans, lanes), jnp.bfloat16),
        in_specs=_vmem(5),
        out_specs=_vmem(1)[0],
        cost_estimate=pl.CostEstimate(flops=flops, transcendentals=0, bytes_accessed=3 * mid.size * 2),
    )(lo, mid, hi, wall, mask)


def weight_call(upper, lo, mid, hi, dpre, mask, depth):
    planes, chans, lanes = dpre.shape
    flops = 2 * planes * 9 * chans * 3 * chans * lanes
    half = jax.ShapeDtypeStruct((chans // 2, 27 * chans + 1), jnp.float32)
    return pl.pallas_call(
        functools.partial(_weight_kernel, planes=planes, depth=depth),
        out_shape=(half, half),
        in_specs=[pl.BlockSpec(memory_space=pltpu.SMEM)] + _vmem(5),
        out_specs=tuple(_vmem(2)),
        scratch_shapes=[pltpu.VMEM((chans, 27 * chans + 1), jnp.float32)],
        cost_estimate=pl.CostEstimate(flops=flops, transcendentals=0, bytes_accessed=3 * dpre.size * 2),
    )(upper, lo, mid, hi, dpre, mask)


def neighbours(first, last, axis):
    peers = lax.axis_size(axis)
    up = [(i, i + 1) for i in range(peers - 1)]
    down = [(j, i) for i, j in up]
    return lax.ppermute(last, axis, up), lax.ppermute(first, axis, down)


def swap(value, axis, bit):
    peers = lax.axis_size(axis)
    return lax.ppermute(value, axis, [(i, i ^ bit) for i in range(peers)])


def gather_rows(value, axis):
    peers = lax.axis_size(axis)
    me = lax.axis_index(axis)
    blocks = jnp.zeros((peers,) + value.shape, value.dtype)
    blocks = lax.dynamic_update_index_in_dim(blocks, value, me, 0)
    for k in range(1, peers):
        blocks = lax.dynamic_update_index_in_dim(blocks, swap(value, axis, k), me ^ k, 0)
    return blocks.reshape((peers * value.shape[0],) + value.shape[1:])


def first_upper():
    return (lax.axis_index("real") // (lax.axis_size("real") // 2)) % 2


def reduce_beside(local_grads, work):
    rounds = []
    bit = lax.axis_size("real") // 2
    while bit >= 1:
        rounds.append(("real", bit))
        bit //= 2
    bit = 1
    while bit < lax.axis_size("strike"):
        rounds.append(("strike", bit))
        bit *= 2
    results = []
    value = None
    for k, (axis, bit) in enumerate(rounds):
        if k == 0:
            keep, send = local_grads
        elif axis == "real":
            half = value.shape[0] // 2
            upper = (lax.axis_index(axis) // bit) % 2
            keep = lax.dynamic_slice_in_dim(value, upper * half, half, 0)
            send = lax.dynamic_slice_in_dim(value, (1 - upper) * half, half, 0)
        else:
            keep, send = value, value
        if k < len(work):
            send, inputs = lax.optimization_barrier((send, work[k][1]))
            received = swap(send, axis, bit)
            result = work[k][0](*inputs)
            received, result = lax.optimization_barrier((received, result))
            results.append(result)
        else:
            received = swap(send, axis, bit)
        value = keep + received
    for job, inputs in work[len(rounds) :]:
        results.append(job(*inputs))
    return value, results


def local(grades, cotangent, weight, bias):
    field = grades[0]
    chans, planes, rows, depth = field.shape
    lanes = rows * depth
    taps_in = weight.shape[1]
    packed = jnp.concatenate([weight, bias[:, None]], axis=1)
    whole = gather_rows(packed, "real")
    whole_weight, whole_bias = whole[:, :taps_in], whole[:, taps_in]
    out_chan = whole_weight.shape[0]
    w5 = whole_weight.reshape(out_chan, 3, 3, 3, chans)
    forward_w = w5.transpose(2, 3, 0, 1, 4).reshape(9 * out_chan, 3 * chans)
    backward_w = w5[:, ::-1].transpose(2, 3, 4, 1, 0).reshape(9 * chans, 3 * out_chan)
    mask = jnp.asarray(plane_masks(rows, depth))

    def flat(value):
        return value.transpose(1, 0, 2, 3).reshape(value.shape[1], value.shape[0], lanes)

    def unflat(value):
        return value.reshape(planes, value.shape[1], rows, depth).transpose(1, 0, 2, 3)

    below, above = neighbours(field[:, :1], field[:, planes - 1 :], "strike")
    mid = flat(field)
    lo, hi = flat(below), flat(above)
    act, dpre, first, last = forward_call(
        lo, mid, hi, forward_w, whole_bias.astype(jnp.float32)[:, None], flat(cotangent[0]), mask, depth
    )
    dlo, dhi = neighbours(first, last, "strike")
    local_grads = weight_call(first_upper().astype(jnp.int32)[None], lo, mid, hi, dpre, mask, depth)
    work = [
        (functools.partial(input_call, depth=depth, first=p, count=1), (dlo, dpre, dhi, backward_w, mask))
        for p in range(planes)
    ]
    owned, pieces = reduce_beside(local_grads, work)
    grad_input = unflat(jnp.concatenate(pieces, axis=0))
    cells = lax.axis_size("real") * lax.axis_size("strike") * planes * rows * depth
    factor = 1.0 / cells**0.5
    owned = owned * factor
    return (unflat(act)[None], grad_input[None], owned[:, :taps_in], owned[:, taps_in])


def solution(mesh):
    in_specs = (
        P("real", None, "strike", None, None),
        P("real", None, "strike", None, None),
        P("real", None),
        P("real"),
    )
    out_specs = (
        P("real", None, "strike", None, None),
        P("real", None, "strike", None, None),
        P("real", None),
        P("real"),
    )
    return jax.shard_map(local, mesh=mesh, in_specs=in_specs, out_specs=out_specs, check_vma=False)
```

```python
import functools

import jax
import jax.numpy as jnp
import numpy as np
from jax import lax
from jax.experimental import pallas as pl
from jax.experimental.pallas import tpu as pltpu
from jax.sharding import PartitionSpec as P

OFFSETS = [(b, c) for b in (-1, 0, 1) for c in (-1, 0, 1)]


def plane_masks(rows, depth):
    y = np.arange(rows)[:, None]
    z = np.arange(depth)[None, :]
    masks = [((y + b >= 0) & (y + b < rows) & (z + c >= 0) & (z + c < depth)) for b, c in OFFSETS]
    return np.stack(masks).reshape(len(OFFSETS), 1, rows * depth).astype(np.float32)


def _stacked_parts(lo, mid, hi, h, planes):
    def plane(index):
        if index == 0:
            return lo[0]
        if index == planes + 1:
            return hi[0]
        return mid[index - 1]
    return jnp.concatenate([plane(h), plane(h + 1), plane(h + 2)], axis=0)


def _shifted_sum(y, mask, chans, lanes, depth, sign):
    total = None
    for k, (b, c) in enumerate(OFFSETS):
        off = sign * (b * depth + c)
        block = y[k * chans : (k + 1) * chans]
        if off != 0:
            block = pltpu.roll(block, (-off) % lanes, 1)
            block = jnp.where(mask[k if sign > 0 else len(OFFSETS) - 1 - k] > 0.5, block, 0.0)
        total = block if total is None else total + block
    return total


def _forward_kernel(lo, mid, hi, wall, bias, cot, mask, act_out, dpre_out, first_out, last_out, *, planes, depth):
    chans, lanes = mid.shape[1], mid.shape[2]
    for p in range(planes):
        y = jnp.dot(wall[...], _stacked_parts(lo, mid, hi, p, planes), preferred_element_type=jnp.float32)
        pre = _shifted_sum(y, mask, chans, lanes, depth, 1) + bias[...]
        sig = 1.0 / (1.0 + jnp.exp(-pre))
        act_out[p] = (pre * sig).astype(act_out.dtype)
        dpre = (cot[p].astype(jnp.float32) * sig * (1.0 + pre * (1.0 - sig))).astype(dpre_out.dtype)
        dpre_out[p] = dpre
        if p == 0:
            first_out[0] = dpre
        if p == planes - 1:
            last_out[0] = dpre


def _input_kernel(lo, mid, hi, wall, mask, out, *, planes, first, depth):
    chans, lanes = mid.shape[1], mid.shape[2]
    for n in range(out.shape[0]):
        y = jnp.dot(wall[...], _stacked_parts(lo, mid, hi, first + n, planes), preferred_element_type=jnp.float32)
        out[n] = _shifted_sum(y, mask, chans, lanes, depth, -1).astype(out.dtype)


def _weight_kernel(upper, lo, mid, hi, dpre, mask, keep_out, send_out, full, *, planes, depth):
    chans, lanes = dpre.shape[1], dpre.shape[2]
    gw = jnp.zeros((9 * chans, 3 * chans), jnp.float32)
    gb = jnp.zeros((chans, 1), jnp.float32)
    for p in range(planes):
        d = dpre[p].astype(jnp.float32)
        gb = gb + jnp.sum(d, axis=1, keepdims=True)
        parts = []
        for k, (b, c) in enumerate(OFFSETS):
            off = b * depth + c
            e = d
            if off != 0:
                e = pltpu.roll(jnp.where(mask[k] > 0.5, d, 0.0), off % lanes, 1)
            parts.append(e.astype(jnp.bfloat16))
        gw = gw + lax.dot_general(
            jnp.concatenate(parts, axis=0), _stacked_parts(lo, mid, hi, p, planes),
            (((1,), (1,)), ((), ())), preferred_element_type=jnp.float32,
        )
    chans_in = gw.shape[1] // 3
    for k in range(len(OFFSETS)):
        for a in range(3):
            t = 9 * a + k
            full[:, t * chans_in : (t + 1) * chans_in] = gw[k * chans : (k + 1) * chans, a * chans_in : (a + 1) * chans_in]
    full[:, 27 * chans_in :] = gb
    half = keep_out.shape[0]
    kept = upper[0]
    keep_out[...] = full[pl.ds(pl.multiple_of(kept * half, 8), half), :]
    send_out[...] = full[pl.ds(pl.multiple_of((1 - kept) * half, 8), half), :]


def _vmem(n):
    return [pl.BlockSpec(memory_space=pltpu.VMEM)] * n


def forward_call(lo, mid, hi, wall, bias, cot, mask, depth):
    planes, chans, lanes = cot.shape
    shape = jax.ShapeDtypeStruct(cot.shape, jnp.bfloat16)
    edge = jax.ShapeDtypeStruct((1, chans, lanes), jnp.bfloat16)
    flops = 2 * planes * wall.shape[0] * wall.shape[1] * lanes
    return pl.pallas_call(
        functools.partial(_forward_kernel, planes=planes, depth=depth),
        out_shape=(shape, shape, edge, edge),
        in_specs=_vmem(7),
        out_specs=tuple(_vmem(4)),
        cost_estimate=pl.CostEstimate(flops=flops, transcendentals=planes * chans * lanes, bytes_accessed=5 * cot.size * 2),
    )(lo, mid, hi, wall, bias, cot, mask)


def input_call(lo, mid, hi, wall, mask, depth, first, count):
    planes, chans, lanes = mid.shape
    flops = 2 * count * wall.shape[0] * wall.shape[1] * lanes
    return pl.pallas_call(
        functools.partial(_input_kernel, planes=planes, first=first, depth=depth),
        out_shape=jax.ShapeDtypeStruct((count, chans, lanes), jnp.bfloat16),
        in_specs=_vmem(5),
        out_specs=_vmem(1)[0],
        cost_estimate=pl.CostEstimate(flops=flops, transcendentals=0, bytes_accessed=3 * mid.size * 2),
    )(lo, mid, hi, wall, mask)


def weight_call(upper, lo, mid, hi, dpre, mask, depth):
    planes, chans, lanes = dpre.shape
    flops = 2 * planes * 9 * chans * 3 * chans * lanes
    half = jax.ShapeDtypeStruct((chans // 2, 27 * chans + 1), jnp.float32)
    return pl.pallas_call(
        functools.partial(_weight_kernel, planes=planes, depth=depth),
        out_shape=(half, half),
        in_specs=[pl.BlockSpec(memory_space=pltpu.SMEM)] + _vmem(5),
        out_specs=tuple(_vmem(2)),
        scratch_shapes=[pltpu.VMEM((chans, 27 * chans + 1), jnp.float32)],
        cost_estimate=pl.CostEstimate(flops=flops, transcendentals=0, bytes_accessed=3 * dpre.size * 2),
    )(upper, lo, mid, hi, dpre, mask)


def neighbours(first, last, axis):
    peers = lax.axis_size(axis)
    up = [(i, i + 1) for i in range(peers - 1)]
    down = [(j, i) for i, j in up]
    return lax.ppermute(last, axis, up), lax.ppermute(first, axis, down)


def swap(value, axis, bit):
    peers = lax.axis_size(axis)
    return lax.ppermute(value, axis, [(i, i ^ bit) for i in range(peers)])


def gather_rows(value, axis):
    peers = lax.axis_size(axis)
    me = lax.axis_index(axis)
    blocks = jnp.zeros((peers,) + value.shape, value.dtype)
    blocks = lax.dynamic_update_index_in_dim(blocks, value, me, 0)
    for k in range(1, peers):
        blocks = lax.dynamic_update_index_in_dim(blocks, swap(value, axis, k), me ^ k, 0)
    return blocks.reshape((peers * value.shape[0],) + value.shape[1:])


def first_upper():
    return (lax.axis_index("real") // (lax.axis_size("real") // 2)) % 2


def reduce_beside(local_grads, work):
    rounds = []
    bit = lax.axis_size("real") // 2
    while bit >= 1:
        rounds.append(("real", bit))
        bit //= 2
    bit = 1
    while bit < lax.axis_size("strike"):
        rounds.append(("strike", bit))
        bit *= 2
    results = []
    value = None
    for k, (axis, bit) in enumerate(rounds):
        if k == 0:
            keep, send = local_grads
        elif axis == "real":
            half = value.shape[0] // 2
            upper = (lax.axis_index(axis) // bit) % 2
            keep = lax.dynamic_slice_in_dim(value, upper * half, half, 0)
            send = lax.dynamic_slice_in_dim(value, (1 - upper) * half, half, 0)
        else:
            keep, send = value, value
        if k < len(work):
            send, inputs = lax.optimization_barrier((send, work[k][1]))
            received = swap(send, axis, bit)
            result = work[k][0](*inputs)
            received, result = lax.optimization_barrier((received, result))
            results.append(result)
        else:
            received = swap(send, axis, bit)
        value = keep + received
    for job, inputs in work[len(rounds) :]:
        results.append(job(*inputs))
    return value, results


def local(grades, cotangent, weight, bias):
    field = grades[0]
    chans, planes, rows, depth = field.shape
    lanes = rows * depth
    taps_in = weight.shape[1]
    packed = jnp.concatenate([weight, bias[:, None]], axis=1)
    below, above = neighbours(field[:, :1], field[:, planes - 1 :], "strike")
    packed, below = lax.optimization_barrier((packed, below))
    whole = gather_rows(packed, "real")
    whole_weight, whole_bias = whole[:, :taps_in], whole[:, taps_in]
    out_chan = whole_weight.shape[0]
    w5 = whole_weight.reshape(out_chan, 3, 3, 3, chans)
    forward_w = w5.transpose(2, 3, 0, 1, 4).reshape(9 * out_chan, 3 * chans)
    backward_w = w5[:, ::-1].transpose(2, 3, 4, 1, 0).reshape(9 * chans, 3 * out_chan)
    mask = jnp.asarray(plane_masks(rows, depth))

    def flat(value):
        return value.transpose(1, 0, 2, 3).reshape(value.shape[1], value.shape[0], lanes)

    def unflat(value):
        return value.reshape(planes, value.shape[1], rows, depth).transpose(1, 0, 2, 3)

    mid = flat(field)
    lo, hi = flat(below), flat(above)
    act, dpre, first, last = forward_call(
        lo, mid, hi, forward_w, whole_bias.astype(jnp.float32)[:, None], flat(cotangent[0]), mask, depth
    )
    dlo, dhi = neighbours(first, last, "strike")
    local_grads = weight_call(first_upper().astype(jnp.int32)[None], lo, mid, hi, dpre, mask, depth)
    work = [
        (functools.partial(input_call, depth=depth, first=p, count=1), (dlo, dpre, dhi, backward_w, mask))
        for p in range(planes)
    ]
    owned, pieces = reduce_beside(local_grads, work)
    grad_input = unflat(jnp.concatenate(pieces, axis=0))
    cells = lax.axis_size("real") * lax.axis_size("strike") * planes * rows * depth
    factor = 1.0 / cells**0.5
    owned = owned * factor
    return (unflat(act)[None], grad_input[None], owned[:, :taps_in], owned[:, taps_in])


def solution(mesh):
    in_specs = (
        P("real", None, "strike", None, None),
        P("real", None, "strike", None, None),
        P("real", None),
        P("real"),
    )
    out_specs = (
        P("real", None, "strike", None, None),
        P("real", None, "strike", None, None),
        P("real", None),
        P("real"),
    )
    return jax.shard_map(local, mesh=mesh, in_specs=in_specs, out_specs=out_specs, check_vma=False)
```

```python
import functools

import jax
import jax.numpy as jnp
import numpy as np
from jax import lax
from jax.experimental import pallas as pl
from jax.experimental.pallas import tpu as pltpu
from jax.sharding import PartitionSpec as P

OFFSETS = [(b, c) for b in (-1, 0, 1) for c in (-1, 0, 1)]


def plane_masks(rows, depth):
    y = np.arange(rows)[:, None]
    z = np.arange(depth)[None, :]
    masks = [((y + b >= 0) & (y + b < rows) & (z + c >= 0) & (z + c < depth)) for b, c in OFFSETS]
    return np.stack(masks).reshape(len(OFFSETS), 1, rows * depth).astype(np.float32)


def _stacked_parts(lo, mid, hi, h, planes):
    def plane(index):
        if index == 0:
            return lo[0]
        if index == planes + 1:
            return hi[0]
        return mid[index - 1]
    return jnp.concatenate([plane(h), plane(h + 1), plane(h + 2)], axis=0)


def _shifted_sum(y, mask, chans, lanes, depth, sign):
    total = None
    for k, (b, c) in enumerate(OFFSETS):
        off = sign * (b * depth + c)
        block = y[k * chans : (k + 1) * chans]
        if off != 0:
            block = pltpu.roll(block, (-off) % lanes, 1)
            block = jnp.where(mask[k if sign > 0 else len(OFFSETS) - 1 - k] > 0.5, block, 0.0)
        total = block if total is None else total + block
    return total


def _forward_kernel(lo, mid, hi, wall, bias, cot, mask, act_out, dpre_out, first_out, last_out, *, planes, depth):
    chans, lanes = mid.shape[1], mid.shape[2]
    for p in range(planes):
        y = jnp.dot(wall[...], _stacked_parts(lo, mid, hi, p, planes), preferred_element_type=jnp.float32)
        pre = _shifted_sum(y, mask, chans, lanes, depth, 1) + bias[...]
        sig = 1.0 / (1.0 + jnp.exp(-pre))
        act_out[p] = (pre * sig).astype(act_out.dtype)
        dpre = (cot[p].astype(jnp.float32) * sig * (1.0 + pre * (1.0 - sig))).astype(dpre_out.dtype)
        dpre_out[p] = dpre
        if p == 0:
            first_out[0] = dpre
        if p == planes - 1:
            last_out[0] = dpre


def _input_kernel(lo, mid, hi, wall, mask, out, *, planes, first, depth):
    chans, lanes = mid.shape[1], mid.shape[2]
    for n in range(out.shape[0]):
        y = jnp.dot(wall[...], _stacked_parts(lo, mid, hi, first + n, planes), preferred_element_type=jnp.float32)
        out[n] = _shifted_sum(y, mask, chans, lanes, depth, -1).astype(out.dtype)


def _weight_kernel(upper, lo, mid, hi, dpre, mask, keep_out, send_out, full, *, planes, depth):
    chans, lanes = dpre.shape[1], dpre.shape[2]
    gw = jnp.zeros((9 * chans, 3 * chans), jnp.float32)
    gb = jnp.zeros((chans, 1), jnp.float32)
    for p in range(planes):
        d = dpre[p].astype(jnp.float32)
        gb = gb + jnp.sum(d, axis=1, keepdims=True)
        parts = []
        for k, (b, c) in enumerate(OFFSETS):
            off = b * depth + c
            e = d
            if off != 0:
                e = pltpu.roll(jnp.where(mask[k] > 0.5, d, 0.0), off % lanes, 1)
            parts.append(e.astype(jnp.bfloat16))
        gw = gw + lax.dot_general(
            jnp.concatenate(parts, axis=0), _stacked_parts(lo, mid, hi, p, planes),
            (((1,), (1,)), ((), ())), preferred_element_type=jnp.float32,
        )
    chans_in = gw.shape[1] // 3
    for k in range(len(OFFSETS)):
        for a in range(3):
            t = 9 * a + k
            full[:, t * chans_in : (t + 1) * chans_in] = gw[k * chans : (k + 1) * chans, a * chans_in : (a + 1) * chans_in]
    full[:, 27 * chans_in :] = gb
    half = keep_out.shape[0]
    kept = upper[0]
    keep_out[...] = full[pl.ds(pl.multiple_of(kept * half, 8), half), :]
    send_out[...] = full[pl.ds(pl.multiple_of((1 - kept) * half, 8), half), :]


def _vmem(n):
    return [pl.BlockSpec(memory_space=pltpu.VMEM)] * n


def forward_call(lo, mid, hi, wall, bias, cot, mask, depth):
    planes, chans, lanes = cot.shape
    shape = jax.ShapeDtypeStruct(cot.shape, jnp.bfloat16)
    edge = jax.ShapeDtypeStruct((1, chans, lanes), jnp.bfloat16)
    flops = 2 * planes * wall.shape[0] * wall.shape[1] * lanes
    return pl.pallas_call(
        functools.partial(_forward_kernel, planes=planes, depth=depth),
        out_shape=(shape, shape, edge, edge),
        in_specs=_vmem(7),
        out_specs=tuple(_vmem(4)),
        cost_estimate=pl.CostEstimate(flops=flops, transcendentals=planes * chans * lanes, bytes_accessed=5 * cot.size * 2),
    )(lo, mid, hi, wall, bias, cot, mask)


def input_call(lo, mid, hi, wall, mask, depth, first, count):
    planes, chans, lanes = mid.shape
    flops = 2 * count * wall.shape[0] * wall.shape[1] * lanes
    return pl.pallas_call(
        functools.partial(_input_kernel, planes=planes, first=first, depth=depth),
        out_shape=jax.ShapeDtypeStruct((count, chans, lanes), jnp.bfloat16),
        in_specs=_vmem(5),
        out_specs=_vmem(1)[0],
        cost_estimate=pl.CostEstimate(flops=flops, transcendentals=0, bytes_accessed=3 * mid.size * 2),
    )(lo, mid, hi, wall, mask)


def weight_call(upper, lo, mid, hi, dpre, mask, depth):
    planes, chans, lanes = dpre.shape
    flops = 2 * planes * 9 * chans * 3 * chans * lanes
    half = jax.ShapeDtypeStruct((chans // 2, 27 * chans + 1), jnp.float32)
    return pl.pallas_call(
        functools.partial(_weight_kernel, planes=planes, depth=depth),
        out_shape=(half, half),
        in_specs=[pl.BlockSpec(memory_space=pltpu.SMEM)] + _vmem(5),
        out_specs=tuple(_vmem(2)),
        scratch_shapes=[pltpu.VMEM((chans, 27 * chans + 1), jnp.float32)],
        cost_estimate=pl.CostEstimate(flops=flops, transcendentals=0, bytes_accessed=3 * dpre.size * 2),
    )(upper, lo, mid, hi, dpre, mask)


def neighbours(first, last, axis):
    peers = lax.axis_size(axis)
    up = [(i, i + 1) for i in range(peers - 1)]
    down = [(j, i) for i, j in up]
    return lax.ppermute(last, axis, up), lax.ppermute(first, axis, down)


def swap(value, axis, bit):
    peers = lax.axis_size(axis)
    return lax.ppermute(value, axis, [(i, i ^ bit) for i in range(peers)])


def gather_rows(value, axis):
    peers = lax.axis_size(axis)
    me = lax.axis_index(axis)
    blocks = jnp.zeros((peers,) + value.shape, value.dtype)
    blocks = lax.dynamic_update_index_in_dim(blocks, value, me, 0)
    for k in range(1, peers):
        blocks = lax.dynamic_update_index_in_dim(blocks, swap(value, axis, k), me ^ k, 0)
    return blocks.reshape((peers * value.shape[0],) + value.shape[1:])


def first_upper():
    return (lax.axis_index("real") // (lax.axis_size("real") // 2)) % 2


def reduce_beside(local_grads, work):
    rounds = []
    bit = lax.axis_size("real") // 2
    while bit >= 1:
        rounds.append(("real", bit))
        bit //= 2
    bit = 1
    while bit < lax.axis_size("strike"):
        rounds.append(("strike", bit))
        bit *= 2
    results = []
    value = None
    for k, (axis, bit) in enumerate(rounds):
        if k == 0:
            keep, send = local_grads
        elif axis == "real":
            half = value.shape[0] // 2
            upper = (lax.axis_index(axis) // bit) % 2
            keep = lax.dynamic_slice_in_dim(value, upper * half, half, 0)
            send = lax.dynamic_slice_in_dim(value, (1 - upper) * half, half, 0)
        else:
            keep, send = value, value
        if k < len(work):
            send, inputs = lax.optimization_barrier((send, work[k][1]))
            received = swap(send, axis, bit)
            result = work[k][0](*inputs)
            received, result = lax.optimization_barrier((received, result))
            results.append(result)
        else:
            received = swap(send, axis, bit)
        value = keep + received
    for job, inputs in work[len(rounds) :]:
        results.append(job(*inputs))
    return value, results


def local(grades, cotangent, weight, bias):
    field = grades[0]
    chans, planes, rows, depth = field.shape
    lanes = rows * depth
    taps_in = weight.shape[1]
    packed = jnp.concatenate([weight, bias[:, None]], axis=1)
    whole = gather_rows(packed, "real")
    whole_weight, whole_bias = whole[:, :taps_in], whole[:, taps_in]
    out_chan = whole_weight.shape[0]
    w5 = whole_weight.reshape(out_chan, 3, 3, 3, chans)
    forward_w = w5.transpose(2, 3, 0, 1, 4).reshape(9 * out_chan, 3 * chans)
    backward_w = w5[:, ::-1].transpose(2, 3, 4, 1, 0).reshape(9 * chans, 3 * out_chan)
    mask = jnp.asarray(plane_masks(rows, depth))

    def flat(value):
        return value.transpose(1, 0, 2, 3).reshape(value.shape[1], value.shape[0], lanes)

    def unflat(value):
        return value.reshape(planes, value.shape[1], rows, depth).transpose(1, 0, 2, 3)

    lo, hi = neighbours(flat(field[:, :1]), flat(field[:, planes - 1 :]), "strike")
    mid = flat(field)
    act, dpre, first, last = forward_call(
        lo, mid, hi, forward_w, whole_bias.astype(jnp.float32)[:, None], flat(cotangent[0]), mask, depth
    )
    dlo, dhi = neighbours(first, last, "strike")
    local_grads = weight_call(first_upper().astype(jnp.int32)[None], lo, mid, hi, dpre, mask, depth)
    work = [
        (functools.partial(input_call, depth=depth, first=p, count=1), (dlo, dpre, dhi, backward_w, mask))
        for p in range(planes)
    ]
    owned, pieces = reduce_beside(local_grads, work)
    grad_input = unflat(jnp.concatenate(pieces, axis=0))
    cells = lax.axis_size("real") * lax.axis_size("strike") * planes * rows * depth
    factor = 1.0 / cells**0.5
    owned = owned * factor
    return (unflat(act)[None], grad_input[None], owned[:, :taps_in], owned[:, taps_in])


def solution(mesh):
    in_specs = (
        P("real", None, "strike", None, None),
        P("real", None, "strike", None, None),
        P("real", None),
        P("real"),
    )
    out_specs = (
        P("real", None, "strike", None, None),
        P("real", None, "strike", None, None),
        P("real", None),
        P("real"),
    )
    return jax.shard_map(local, mesh=mesh, in_specs=in_specs, out_specs=out_specs, check_vma=False)
```

```python
import functools

import jax
import jax.numpy as jnp
import numpy as np
from jax import lax
from jax.experimental import pallas as pl
from jax.experimental.pallas import tpu as pltpu
from jax.sharding import PartitionSpec as P

OFFSETS = [(b, c) for b in (-1, 0, 1) for c in (-1, 0, 1)]


def plane_masks(rows, depth):
    y = np.arange(rows)[:, None]
    z = np.arange(depth)[None, :]
    masks = [((y + b >= 0) & (y + b < rows) & (z + c >= 0) & (z + c < depth)) for b, c in OFFSETS]
    return np.stack(masks).reshape(len(OFFSETS), 1, rows * depth).astype(np.float32)


def _stacked_parts(lo, mid, hi, h, planes):
    def plane(index):
        if index == 0:
            return lo[0]
        if index == planes + 1:
            return hi[0]
        return mid[index - 1]
    return jnp.concatenate([plane(h), plane(h + 1), plane(h + 2)], axis=0)


def _shifted_sum(y, mask, chans, lanes, depth, sign):
    total = None
    for k, (b, c) in enumerate(OFFSETS):
        off = sign * (b * depth + c)
        block = y[k * chans : (k + 1) * chans]
        if off != 0:
            block = pltpu.roll(block, (-off) % lanes, 1)
            block = jnp.where(mask[k if sign > 0 else len(OFFSETS) - 1 - k] > 0.5, block, 0.0)
        total = block if total is None else total + block
    return total


def _forward_kernel(lo, mid, hi, wall, bias, cot, mask, act_out, dpre_out, first_out, last_out, *, planes, depth):
    chans, lanes = mid.shape[1], mid.shape[2]
    for p in range(planes):
        y = jnp.dot(wall[...], _stacked_parts(lo, mid, hi, p, planes), preferred_element_type=jnp.float32)
        pre = _shifted_sum(y, mask, chans, lanes, depth, 1) + bias[...]
        sig = 1.0 / (1.0 + jnp.exp(-pre))
        act_out[p] = (pre * sig).astype(act_out.dtype)
        dpre = (cot[p].astype(jnp.float32) * sig * (1.0 + pre * (1.0 - sig))).astype(dpre_out.dtype)
        dpre_out[p] = dpre
        if p == 0:
            first_out[0] = dpre
        if p == planes - 1:
            last_out[0] = dpre


def _input_kernel(lo, mid, hi, wall, mask, out, *, planes, first, depth):
    chans, lanes = mid.shape[1], mid.shape[2]
    for n in range(out.shape[0]):
        y = jnp.dot(wall[...], _stacked_parts(lo, mid, hi, first + n, planes), preferred_element_type=jnp.float32)
        out[n] = _shifted_sum(y, mask, chans, lanes, depth, -1).astype(out.dtype)


def _weight_kernel(upper, lo, mid, hi, dpre, mask, keep_out, send_out, full, *, planes, depth):
    chans, lanes = dpre.shape[1], dpre.shape[2]
    gw = jnp.zeros((9 * chans, 3 * chans), jnp.float32)
    gb = jnp.zeros((chans, 1), jnp.float32)
    for p in range(planes):
        d = dpre[p].astype(jnp.float32)
        gb = gb + jnp.sum(d, axis=1, keepdims=True)
        parts = []
        for k, (b, c) in enumerate(OFFSETS):
            off = b * depth + c
            e = d
            if off != 0:
                e = pltpu.roll(jnp.where(mask[k] > 0.5, d, 0.0), off % lanes, 1)
            parts.append(e.astype(jnp.bfloat16))
        gw = gw + lax.dot_general(
            jnp.concatenate(parts, axis=0), _stacked_parts(lo, mid, hi, p, planes),
            (((1,), (1,)), ((), ())), preferred_element_type=jnp.float32,
        )
    chans_in = gw.shape[1] // 3
    for k in range(len(OFFSETS)):
        for a in range(3):
            t = 9 * a + k
            full[:, t * chans_in : (t + 1) * chans_in] = gw[k * chans : (k + 1) * chans, a * chans_in : (a + 1) * chans_in]
    full[:, 27 * chans_in :] = gb
    half = keep_out.shape[0]
    kept = upper[0]
    keep_out[...] = full[pl.ds(pl.multiple_of(kept * half, 8), half), :]
    send_out[...] = full[pl.ds(pl.multiple_of((1 - kept) * half, 8), half), :]


def _vmem(n):
    return [pl.BlockSpec(memory_space=pltpu.VMEM)] * n


def forward_call(lo, mid, hi, wall, bias, cot, mask, depth):
    planes, chans, lanes = cot.shape
    shape = jax.ShapeDtypeStruct(cot.shape, jnp.bfloat16)
    edge = jax.ShapeDtypeStruct((1, chans, lanes), jnp.bfloat16)
    flops = 2 * planes * wall.shape[0] * wall.shape[1] * lanes
    return pl.pallas_call(
        functools.partial(_forward_kernel, planes=planes, depth=depth),
        out_shape=(shape, shape, edge, edge),
        in_specs=_vmem(7),
        out_specs=tuple(_vmem(4)),
        cost_estimate=pl.CostEstimate(flops=flops, transcendentals=planes * chans * lanes, bytes_accessed=5 * cot.size * 2),
    )(lo, mid, hi, wall, bias, cot, mask)


def input_call(lo, mid, hi, wall, mask, depth, first, count):
    planes, chans, lanes = mid.shape
    flops = 2 * count * wall.shape[0] * wall.shape[1] * lanes
    return pl.pallas_call(
        functools.partial(_input_kernel, planes=planes, first=first, depth=depth),
        out_shape=jax.ShapeDtypeStruct((count, chans, lanes), jnp.bfloat16),
        in_specs=_vmem(5),
        out_specs=_vmem(1)[0],
        cost_estimate=pl.CostEstimate(flops=flops, transcendentals=0, bytes_accessed=3 * mid.size * 2),
    )(lo, mid, hi, wall, mask)


def weight_call(upper, lo, mid, hi, dpre, mask, depth):
    planes, chans, lanes = dpre.shape
    flops = 2 * planes * 9 * chans * 3 * chans * lanes
    half = jax.ShapeDtypeStruct((chans // 2, 27 * chans + 1), jnp.float32)
    return pl.pallas_call(
        functools.partial(_weight_kernel, planes=planes, depth=depth),
        out_shape=(half, half),
        in_specs=[pl.BlockSpec(memory_space=pltpu.SMEM)] + _vmem(5),
        out_specs=tuple(_vmem(2)),
        scratch_shapes=[pltpu.VMEM((chans, 27 * chans + 1), jnp.float32)],
        cost_estimate=pl.CostEstimate(flops=flops, transcendentals=0, bytes_accessed=3 * dpre.size * 2),
    )(upper, lo, mid, hi, dpre, mask)


def neighbours(first, last, axis):
    peers = lax.axis_size(axis)
    up = [(i, i + 1) for i in range(peers - 1)]
    down = [(j, i) for i, j in up]
    return lax.ppermute(last, axis, up), lax.ppermute(first, axis, down)


def swap(value, axis, bit):
    peers = lax.axis_size(axis)
    return lax.ppermute(value, axis, [(i, i ^ bit) for i in range(peers)])


def gather_rows(value, axis):
    peers = lax.axis_size(axis)
    me = lax.axis_index(axis)
    blocks = jnp.zeros((peers,) + value.shape, value.dtype)
    blocks = lax.dynamic_update_index_in_dim(blocks, value, me, 0)
    for k in range(1, peers):
        blocks = lax.dynamic_update_index_in_dim(blocks, swap(value, axis, k), me ^ k, 0)
    return blocks.reshape((peers * value.shape[0],) + value.shape[1:])


def first_upper():
    return (lax.axis_index("real") // (lax.axis_size("real") // 2)) % 2


def reduce_beside(local_grads, work):
    rounds = []
    bit = lax.axis_size("real") // 2
    while bit >= 1:
        rounds.append(("real", bit))
        bit //= 2
    bit = 1
    while bit < lax.axis_size("strike"):
        rounds.append(("strike", bit))
        bit *= 2
    results = []
    value = None
    for k, (axis, bit) in enumerate(rounds):
        if k == 0:
            keep, send = local_grads
        elif axis == "real":
            half = value.shape[0] // 2
            upper = (lax.axis_index(axis) // bit) % 2
            keep = lax.dynamic_slice_in_dim(value, upper * half, half, 0)
            send = lax.dynamic_slice_in_dim(value, (1 - upper) * half, half, 0)
        else:
            keep, send = value, value
        if k < len(work):
            send, inputs = lax.optimization_barrier((send, work[k][1]))
            received = swap(send, axis, bit)
            result = work[k][0](*inputs)
            received, result = lax.optimization_barrier((received, result))
            results.append(result)
        else:
            received = swap(send, axis, bit)
        value = keep + received
    for job, inputs in work[len(rounds) :]:
        results.append(job(*inputs))
    return value, results


def local(grades, cotangent, weight, bias):
    field = grades[0]
    chans, planes, rows, depth = field.shape
    lanes = rows * depth
    taps_in = weight.shape[1]
    packed = jnp.concatenate([weight, bias[:, None]], axis=1)
    whole = gather_rows(packed, "real")
    whole_weight, whole_bias = whole[:, :taps_in], whole[:, taps_in]
    out_chan = whole_weight.shape[0]
    w5 = whole_weight.reshape(out_chan, 3, 3, 3, chans)
    forward_w = w5.transpose(2, 3, 0, 1, 4).reshape(9 * out_chan, 3 * chans)
    backward_w = w5[:, ::-1].transpose(2, 3, 4, 1, 0).reshape(9 * chans, 3 * out_chan)
    mask = jnp.asarray(plane_masks(rows, depth))

    def flat(value):
        return value.transpose(1, 0, 2, 3).reshape(value.shape[1], value.shape[0], lanes)

    def unflat(value):
        return value.reshape(planes, value.shape[1], rows, depth).transpose(1, 0, 2, 3)

    below, above = neighbours(field[:, :1], field[:, planes - 1 :], "strike")
    mid = flat(field)
    lo, hi = flat(below), flat(above)
    act, dpre, first, last = forward_call(
        lo, mid, hi, forward_w, whole_bias.astype(jnp.float32)[:, None], flat(cotangent[0]), mask, depth
    )
    dlo, dhi = neighbours(first, last, "strike")
    local_grads = weight_call(first_upper().astype(jnp.int32)[None], lo, mid, hi, dpre, mask, depth)
    work = [
        (functools.partial(input_call, depth=depth, first=0, count=planes), (dlo, dpre, dhi, backward_w, mask))
    ]
    owned, pieces = reduce_beside(local_grads, work)
    grad_input = unflat(jnp.concatenate(pieces, axis=0))
    cells = lax.axis_size("real") * lax.axis_size("strike") * planes * rows * depth
    factor = 1.0 / cells**0.5
    owned = owned * factor
    return (unflat(act)[None], grad_input[None], owned[:, :taps_in], owned[:, taps_in])


def solution(mesh):
    in_specs = (
        P("real", None, "strike", None, None),
        P("real", None, "strike", None, None),
        P("real", None),
        P("real"),
    )
    out_specs = (
        P("real", None, "strike", None, None),
        P("real", None, "strike", None, None),
        P("real", None),
        P("real"),
    )
    return jax.shard_map(local, mesh=mesh, in_specs=in_specs, out_specs=out_specs, check_vma=False)
```
